32 devices in a mesh: ens: 2 (over x), gx: 16 (over z, y, core).
Axes of the slice: x: 2, y: 2, z: 4, core: 2. Of those that a mesh axis runs over, the one named last changes fastest.
Arguments:
- misfit: float32 [4, 16, 128, 512], P('ens', None, 'gx'), parts along dimension 0, may hold values from -8 to 8
- adjoint_guess: float32 [4, 16, 128, 512], P('ens', None, 'gx'), parts along dimension 0, may hold values from -4 to 4
- viscosity: float32 [32, 128, 512], P('ens', 'gx'), parts along dimension 0, may hold values from 0.3 to 3
- friction: float32 [128, 1024], P('gx', 'ens'), parts along dimension 1, may hold values from 0.1 to 10
- ice_mask: int32 [128, 1024], P('gx', 'ens'), parts along dimension 1, may hold values from 0 to 2
- forward_bed: float32 [4, 128, 512], P('ens', 'gx'), parts along dimension 0, may hold values from -6 to 6
Outputs:
- adjoint: float32 [4, 16, 128, 512], P('ens', None, 'gx'), parts along dimension 0
- friction_gradient: float32 [128, 1024], P('gx', 'ens'), parts along dimension 1
The draws below stay inside these ranges and needn't reach their ends.
There are 2 independent parts, one for each index of `ens`. The reference program is written for one: setup_inputs(seed, part) draws one part's arguments, and reference() takes and returns one part's arrays. A program takes and returns all parts, laid end to end along the dimension named above; each array names one. Nothing has to cross between parts.
All inputs are finite; a program needn't handle non-finite values.
Results may differ from the reference program's by a relative error of at most 0.0003.
Values sent between devices are 32-bit elements; how exact they have to be, the bound alone decides.
No kernel may reach another device: no remote copies, remote signals or barrier semaphores. Data moves between devices by JAX's collectives and lax.ppermute only.
A program may use at most 64 MiB of HBM per device.

```python
import math
import jax
import jax.numpy as jnp

CX = 8
NY = 512
NZ = 16
NU = 2
COARSE_SWEEPS = 6
NX = 128


def draw_misfit(key, part):
    noise_key = jax.random.fold_in(key, 11)
    phase_key = jax.random.fold_in(key, 12)
    positions = jnp.arange(NX, dtype=jnp.float32).reshape(1, 1, NX, 1)
    period = 16.0 * CX
    phase = jax.random.uniform(phase_key, (2, 1, 1, 1), jnp.float32, -math.pi, math.pi)
    wave = jnp.sin(2.0 * math.pi * positions / period + phase)
    noise = jnp.clip(jax.random.normal(noise_key, (2, NZ, NX, NY), jnp.float32), -3.0, 3.0)
    smooth = 1.5 + 3.5 * wave
    return jnp.clip(smooth + noise, -8.0, 8.0).astype(jnp.float32)


def draw_ice_mask(key, part):
    codes = jax.random.randint(jax.random.fold_in(key, 21), (NX, NY), 0, 20)
    return jnp.where(codes == 0, 0, jnp.where(codes < 7, 2, 1)).astype(jnp.int32)


def shard_levels(key, extent, split, low, largest):
    factor_of = 1.0
    for axis_at, blocks in split:
        heights = jax.random.uniform(jax.random.fold_in(jax.random.fold_in(key, 6), axis_at), (blocks,), jnp.float32, low / len(split), largest / len(split))
        factor_of = factor_of * jnp.repeat(jnp.exp(heights), extent[axis_at] // blocks).reshape((-1,) + (1,) * (len(extent) - 1 - axis_at))
    return factor_of


def centred(key, extent, deviation, reach, pieces=(), kind=jnp.bfloat16):
    entries = deviation * jax.random.normal(key, extent, jnp.float32)
    if pieces:
        entries = entries * shard_levels(key, extent, pieces, -0.22, 0.18)
    return jnp.clip(entries, -reach, reach).astype(kind)


def setup_inputs(seed: int = 0, part: int = 0) -> dict:
    seeds = jax.random.split(jax.random.key(seed), 7)
    part_keys = jax.random.split(jax.random.fold_in(seeds[6], part), 7)
    return {
        "misfit": draw_misfit(jax.random.fold_in(jax.random.fold_in(seeds[6], part), 71), part),
        "adjoint_guess": centred(part_keys[1], (2, NZ, NX, NY), 0.5, 4.0, ((2, 16),), jnp.float32),
        "viscosity": jnp.clip(jnp.exp(math.log(3.0) - 2.3025851 * jax.random.uniform(part_keys[2], (NZ, NX, NY), jnp.float32) ** shard_levels(part_keys[2], (NZ, NX, NY), ((1, 16),), -0.2, 0.2)), 0.3, 3.0),
        "friction": jnp.clip(jnp.exp(math.log(10.0) - 4.6051702 * jax.random.uniform(part_keys[3], (NX, NY), jnp.float32) ** shard_levels(part_keys[3], (NX, NY), ((0, 16),), -0.2, 0.2)), 0.1, 10.0),
        "ice_mask": draw_ice_mask(jax.random.fold_in(jax.random.fold_in(seeds[6], part), 71), part),
        "forward_bed": centred(part_keys[5], (2, NX, NY), 1.0, 6.0, ((1, 16),), jnp.float32),
    }


horizontal_scale = 1.0
vertical_scale = 4.0
relax_weight = 0.8


def block_mean(field, factor):
    lead = field.shape[:-2]
    rows, cols = field.shape[-2], field.shape[-1]
    shaped = field.reshape(lead + (rows // factor, factor, cols // factor, factor))
    return shaped.mean(axis=(-3, -1))


def reaction_field(friction, ice_mask, layers):
    open_water = (ice_mask == 0).astype(jnp.float32)
    grounded = (ice_mask == 2).astype(jnp.float32)
    bottom = (jnp.arange(layers) == 0).astype(jnp.float32).reshape(layers, 1, 1)
    return 0.02 + 2.0 * open_water[None] + bottom * (grounded * friction)[None]


def level_fields(eta_wide, react_fine, level_index):
    factor = 2 ** level_index
    width = eta_wide.shape[1]
    segment = eta_wide[:, 4 - factor:width - 4 + factor, :]
    return block_mean(segment, factor), block_mean(react_fine, factor)


def build_operator(eta_level, react_level, level_index):
    scale = horizontal_scale / 4.0 ** level_index
    weight_x = jnp.array([4.0, 1.0], jnp.float32).reshape(2, 1, 1, 1) * scale
    weight_y = jnp.array([1.0, 4.0], jnp.float32).reshape(2, 1, 1, 1) * scale
    inner = eta_level[:, 1:-1, :]
    face_x = weight_x * (0.5 * (eta_level[:, 1:, :] + eta_level[:, :-1, :]))[None]
    padded = jnp.pad(inner, ((0, 0), (0, 0), (1, 1)))
    face_y = weight_y * (0.5 * (padded[:, :, 1:] + padded[:, :, :-1]))[None]
    face_z = vertical_scale * 0.5 * (inner[1:] + inner[:-1])
    vertical = jnp.pad(face_z, ((1, 1), (0, 0), (0, 0)))
    diagonal = face_x[:, :, 1:] + face_x[:, :, :-1] + face_y[..., 1:] + face_y[..., :-1]
    diagonal = diagonal + (vertical[1:] + vertical[:-1] + react_level)[None]
    layers = diagonal.shape[1]
    inverses = []
    ratios = []
    for layer in range(layers):
        pivot = diagonal[:, layer]
        if layer > 0:
            pivot = pivot - face_z[layer - 1] * ratios[-1]
        inverse = 1.0 / pivot
        inverses.append(inverse)
        if layer < layers - 1:
            ratios.append(face_z[layer] * inverse)
    return (face_x, face_y, face_z, react_level, jnp.stack(inverses, 1), jnp.stack(ratios, 1))


def apply_operator(field_rim, operator):
    face_x, face_y, face_z, react_level, inverses, ratios = operator
    field = field_rim[:, :, 1:-1, :]
    flux_x = face_x * (field_rim[:, :, 1:, :] - field_rim[:, :, :-1, :])
    result = -(flux_x[:, :, 1:] - flux_x[:, :, :-1])
    padded = jnp.pad(field, ((0, 0), (0, 0), (0, 0), (1, 1)))
    flux_y = face_y * (padded[..., 1:] - padded[..., :-1])
    result = result - (flux_y[..., 1:] - flux_y[..., :-1])
    flux_z = face_z[None] * (field[:, 1:] - field[:, :-1])
    flux_z = jnp.pad(flux_z, ((0, 0), (1, 1), (0, 0), (0, 0)))
    result = result - (flux_z[:, 1:] - flux_z[:, :-1])
    return result + react_level[None] * field


def line_solve(residual, operator):
    face_z, inverses, ratios = operator[2], operator[4], operator[5]
    layers = residual.shape[1]
    forward = [residual[:, 0] * inverses[:, 0]]
    for layer in range(1, layers):
        forward.append((residual[:, layer] + face_z[layer - 1] * forward[-1]) * inverses[:, layer])
    backward = [forward[-1]]
    for layer in range(layers - 2, -1, -1):
        backward.append(forward[layer] + ratios[:, layer] * backward[-1])
    return jnp.stack(backward[::-1], 1)


def sweep(field_rim, target, operator):
    field = field_rim[:, :, 1:-1, :]
    return field + relax_weight * line_solve(target - apply_operator(field_rim, operator), operator)


def restrict(field):
    return block_mean(field, 2)


def prolong(field):
    return jnp.repeat(jnp.repeat(field, 2, axis=2), 2, axis=3)


def pad_rim(field):
    return jnp.pad(field, ((0, 0), (0, 0), (1, 1), (0, 0)))


def reference(misfit, adjoint_guess, viscosity, friction, ice_mask, forward_bed):
    layers = viscosity.shape[0]
    react_fine = reaction_field(friction, ice_mask, layers)
    eta_wide = jnp.pad(viscosity, ((0, 0), (4, 4), (0, 0)))
    operators = [build_operator(*level_fields(eta_wide, react_fine, level_index), level_index) for level_index in range(3)]
    fine = adjoint_guess
    for turn in range(NU):
        fine = sweep(pad_rim(fine), misfit, operators[0])
    middle_rhs = restrict(misfit - apply_operator(pad_rim(fine), operators[0]))
    middle = jnp.zeros_like(middle_rhs)
    for turn in range(NU):
        middle = sweep(pad_rim(middle), middle_rhs, operators[1])
    coarse_rhs = restrict(middle_rhs - apply_operator(pad_rim(middle), operators[1]))
    coarse = jnp.zeros_like(coarse_rhs)
    for turn in range(COARSE_SWEEPS):
        coarse = sweep(pad_rim(coarse), coarse_rhs, operators[2])
    middle = middle + prolong(coarse)
    for turn in range(NU):
        middle = sweep(pad_rim(middle), middle_rhs, operators[1])
    fine = fine + prolong(middle)
    for turn in range(NU):
        fine = sweep(pad_rim(fine), misfit, operators[0])
    grounded = (ice_mask == 2).astype(jnp.float32)
    gradient = -grounded * (forward_bed[0] * fine[0, 0] + forward_bed[1] * fine[1, 0])
    return fine, gradient
```

```python
import jax
import jax.numpy as jnp
from jax import lax
from jax.sharding import PartitionSpec as P

NU = 2
COARSE_SWEEPS = 6


horizontal_scale = 1.0
vertical_scale = 4.0
relax_weight = 0.8


def with_halo(cells, sides, width):
    for axis, dim in sides:
        count = lax.axis_size(axis)
        ends = count - 1
        head = lax.slice_in_dim(cells, 0, width, axis=dim)
        tail = lax.slice_in_dim(cells, cells.shape[dim] - width, cells.shape[dim], axis=dim)
        cells = jnp.concatenate(
            [
                lax.ppermute(tail, axis, [(i, (i + 1) % count) for i in range(ends)]),
                cells,
                lax.ppermute(head, axis, [((i + 1) % count, i) for i in range(ends)]),
            ],
            axis=dim,
        )
    return cells


def trade(parts, width):
    count = lax.axis_size("gx")
    ends = count - 1
    heads = [lax.slice_in_dim(a, 0, width, axis=dim) for a, dim in parts]
    tails = [lax.slice_in_dim(a, a.shape[dim] - width, a.shape[dim], axis=dim) for a, dim in parts]
    pack = lambda pieces: jnp.concatenate([p.reshape(-1) for p in pieces])
    from_left = lax.ppermute(pack(tails), "gx", [(i, i + 1) for i in range(ends)])
    from_right = lax.ppermute(pack(heads), "gx", [(i + 1, i) for i in range(ends)])
    out = []
    offset = 0
    for (a, dim), h in zip(parts, heads):
        size = h.size
        left = from_left[offset : offset + size].reshape(h.shape)
        right = from_right[offset : offset + size].reshape(h.shape)
        offset += size
        out.append(jnp.concatenate([left, a, right], axis=dim))
    return out


def block_mean(field, factor):
    lead = field.shape[:-2]
    rows, cols = (field.shape[-2], field.shape[-1])
    shaped = field.reshape(lead + (rows // factor, factor, cols // factor, factor))
    return shaped.mean(axis=(-3, -1))


def reaction_field(friction, ice_mask, layers):
    open_water = (ice_mask == 0).astype(jnp.float32)
    grounded = (ice_mask == 2).astype(jnp.float32)
    bottom = (jnp.arange(layers) == 0).astype(jnp.float32).reshape(layers, 1, 1)
    return 0.02 + 2.0 * open_water[None] + bottom * (grounded * friction)[None]


def build_operator(eta_level, react_level, level_index):
    scale = horizontal_scale / 4.0**level_index
    weight_x = jnp.array([4.0, 1.0], jnp.float32).reshape(2, 1, 1, 1) * scale
    weight_y = jnp.array([1.0, 4.0], jnp.float32).reshape(2, 1, 1, 1) * scale
    inner = eta_level[:, 1:-1, :]
    face_x = weight_x * (0.5 * (eta_level[:, 1:, :] + eta_level[:, :-1, :]))[None]
    padded = jnp.pad(inner, ((0, 0), (0, 0), (1, 1)))
    face_y = weight_y * (0.5 * (padded[:, :, 1:] + padded[:, :, :-1]))[None]
    face_z = vertical_scale * 0.5 * (inner[1:] + inner[:-1])
    vertical = jnp.pad(face_z, ((1, 1), (0, 0), (0, 0)))
    diagonal = face_x[:, :, 1:] + face_x[:, :, :-1] + face_y[..., 1:] + face_y[..., :-1]
    diagonal = diagonal + (vertical[1:] + vertical[:-1] + react_level)[None]
    layers = diagonal.shape[1]
    inverses = []
    ratios = []
    for layer in range(layers):
        pivot = diagonal[:, layer]
        if layer > 0:
            pivot = pivot - face_z[layer - 1] * ratios[-1]
        inverse = 1.0 / pivot
        inverses.append(inverse)
        if layer < layers - 1:
            ratios.append(face_z[layer] * inverse)
    return (face_x, face_y, face_z, react_level, jnp.stack(inverses, 1), jnp.stack(ratios, 1))


def shrink(operator, cut):
    if cut == 0:
        return operator
    face_x, face_y, face_z, react_level, inverses, ratios = operator
    rows = face_y.shape[2]
    return (
        face_x[:, :, cut : rows + 1 - cut],
        face_y[:, :, cut : rows - cut],
        face_z[:, cut : rows - cut],
        react_level[:, cut : rows - cut],
        inverses[:, :, cut : rows - cut],
        ratios[:, :, cut : rows - cut],
    )


def apply_operator(field_rim, operator):
    face_x, face_y, face_z, react_level, inverses, ratios = operator
    field = field_rim[:, :, 1:-1, :]
    flux_x = face_x * (field_rim[:, :, 1:, :] - field_rim[:, :, :-1, :])
    result = -(flux_x[:, :, 1:] - flux_x[:, :, :-1])
    padded = jnp.pad(field, ((0, 0), (0, 0), (0, 0), (1, 1)))
    flux_y = face_y * (padded[..., 1:] - padded[..., :-1])
    result = result - (flux_y[..., 1:] - flux_y[..., :-1])
    flux_z = face_z[None] * (field[:, 1:] - field[:, :-1])
    flux_z = jnp.pad(flux_z, ((0, 0), (1, 1), (0, 0), (0, 0)))
    result = result - (flux_z[:, 1:] - flux_z[:, :-1])
    return result + react_level[None] * field


def line_solve(residual, operator):
    face_z, inverses, ratios = (operator[2], operator[4], operator[5])
    layers = residual.shape[1]
    forward = [residual[:, 0] * inverses[:, 0]]
    for layer in range(1, layers):
        forward.append((residual[:, layer] + face_z[layer - 1] * forward[-1]) * inverses[:, layer])
    backward = [forward[-1]]
    for layer in range(layers - 2, -1, -1):
        backward.append(forward[layer] + ratios[:, layer] * backward[-1])
    return jnp.stack(backward[::-1], 1)


def sweep(field_rim, target, operator):
    field = field_rim[:, :, 1:-1, :]
    return field + relax_weight * line_solve(target - apply_operator(field_rim, operator), operator)


def restrict(field):
    return block_mean(field, 2)


def prolong(field):
    return jnp.repeat(jnp.repeat(field, 2, axis=2), 2, axis=3)


def pad_rim(field):
    return jnp.pad(field, ((0, 0), (0, 0), (1, 1), (0, 0)))


def inside(cells, halo, extent):
    count = lax.axis_size("gx")
    first = lax.axis_index("gx") * cells - halo
    index = first + jnp.arange(extent)
    return ((index >= 0) & (index < count * cells)).reshape(1, 1, extent, 1)


def keep_inside(field, cells, halo):
    return jnp.where(inside(cells, halo, field.shape[2]), field, 0.0)


def window(full, dim, start, size, pad):
    widths = [(0, 0)] * full.ndim
    widths[dim] = (pad, pad)
    return lax.dynamic_slice_in_dim(jnp.pad(full, widths), start, size, axis=dim)


def shards(misfit, adjoint_guess, viscosity, friction, ice_mask, forward_bed):
    layers, cells, cols = viscosity.shape
    where = lax.axis_index("gx")
    react_fine = reaction_field(friction, ice_mask, layers)
    react_pair = react_fine[:2]

    eta_1 = block_mean(viscosity, 2)
    eta_2 = block_mean(viscosity, 4)
    react_1 = block_mean(react_pair, 2)
    react_2 = block_mean(react_pair, 4)
    eta_1_all = lax.all_gather(eta_1, "gx", axis=1, tiled=True)
    eta_2_all = lax.all_gather(eta_2, "gx", axis=1, tiled=True)
    react_1_all = lax.all_gather(react_1, "gx", axis=1, tiled=True)
    react_2_all = lax.all_gather(react_2, "gx", axis=1, tiled=True)

    halo = 4
    eta_wide, guess_wide, misfit_wide, react_wide = trade(
        [(viscosity, 1), (adjoint_guess, 2), (misfit, 2), (react_pair, 1)], halo
    )
    react_wide = jnp.concatenate(
        [react_wide[:1], jnp.broadcast_to(react_wide[1:], (layers - 1,) + react_wide.shape[1:])], axis=0
    )
    op_0 = build_operator(eta_wide, react_wide[:, 1:-1], 0)
    fine = keep_inside(sweep(guess_wide, misfit_wide[:, :, 1:-1], op_0), cells, 3)
    fine = keep_inside(sweep(fine, misfit_wide[:, :, 2:-2], shrink(op_0, 1)), cells, 2)
    middle_rhs = restrict(misfit - apply_operator(fine[:, :, 1:-1], shrink(op_0, 3)))

    half = cells // 2
    rhs_wide = with_halo(middle_rhs, (("gx", 2),), half)
    eta_1_wide = window(eta_1_all, 1, where * half, 3 * half + 2, half + 1)
    react_1_wide = window(react_1_all, 1, where * half, 3 * half, half)
    react_1_wide = jnp.concatenate(
        [react_1_wide[:1], jnp.broadcast_to(react_1_wide[1:], (layers - 1,) + react_1_wide.shape[1:])], axis=0
    )
    op_1 = build_operator(eta_1_wide, react_1_wide, 1)
    middle = keep_inside(relax_weight * line_solve(rhs_wide, op_1), half, half)
    middle = keep_inside(sweep(middle, rhs_wide[:, :, 1:-1], shrink(op_1, 1)), half, half - 1)
    coarse_rhs = restrict(middle_rhs - apply_operator(middle[:, :, half - 2 : 2 * half], shrink(op_1, half)))

    quarter = cells // 4
    reach = 3
    span = reach + COARSE_SWEEPS - 1
    coarse_rhs_all = lax.all_gather(coarse_rhs, "gx", axis=2, tiled=True)
    coarse_rhs_near = window(coarse_rhs_all, 2, where * quarter, quarter + 2 * span, span)
    eta_2_near = window(eta_2_all, 1, where * quarter, quarter + 2 * span + 2, span + 1)
    react_2_near = window(react_2_all, 1, where * quarter, quarter + 2 * span, span)
    react_2_near = jnp.concatenate(
        [react_2_near[:1], jnp.broadcast_to(react_2_near[1:], (layers - 1,) + react_2_near.shape[1:])], axis=0
    )
    op_2 = build_operator(eta_2_near, react_2_near, 2)
    coarse = jnp.zeros_like(coarse_rhs_near)
    for turn in range(COARSE_SWEEPS):
        coarse = keep_inside(sweep(pad_rim(coarse), coarse_rhs_near, op_2), quarter, span)
    coarse_near = coarse[:, :, span - reach : span + quarter + reach]

    lift = prolong(coarse_near)
    trim = 2 * reach - (half - 1)
    middle = middle + lift[:, :, trim : lift.shape[2] - trim]
    middle = keep_inside(sweep(middle, rhs_wide[:, :, 2:-2], shrink(op_1, 2)), half, half - 2)
    middle = keep_inside(sweep(middle, rhs_wide[:, :, 3:-3], shrink(op_1, 3)), half, half - 3)
    fine = fine + prolong(middle)
    fine = keep_inside(sweep(fine, misfit_wide[:, :, 3:-3], shrink(op_0, 2)), cells, 1)
    fine = sweep(fine, misfit, shrink(op_0, 3))
    grounded = (ice_mask == 2).astype(jnp.float32)
    gradient = -grounded * (forward_bed[0] * fine[0, 0] + forward_bed[1] * fine[1, 0])
    return (fine, gradient)


def solution(mesh):
    placed = (
        P("ens", None, "gx", None),
        P("ens", None, "gx", None),
        P("ens", "gx", None),
        P("gx", "ens"),
        P("gx", "ens"),
        P("ens", "gx", None),
    )
    return jax.shard_map(
        shards,
        mesh=mesh,
        in_specs=placed,
        out_specs=(P("ens", None, "gx", None), P("gx", "ens")),
        check_vma=False,
    )
```

```python
import jax
import jax.numpy as jnp
from jax import lax
from jax.sharding import PartitionSpec as P

NU = 2
COARSE_SWEEPS = 6


horizontal_scale = 1.0
vertical_scale = 4.0
relax_weight = 0.8


def with_halo(cells, sides, width):
    for axis, dim in sides:
        count = lax.axis_size(axis)
        ends = count - 1
        head = lax.slice_in_dim(cells, 0, width, axis=dim)
        tail = lax.slice_in_dim(cells, cells.shape[dim] - width, cells.shape[dim], axis=dim)
        cells = jnp.concatenate(
            [
                lax.ppermute(tail, axis, [(i, (i + 1) % count) for i in range(ends)]),
                cells,
                lax.ppermute(head, axis, [((i + 1) % count, i) for i in range(ends)]),
            ],
            axis=dim,
        )
    return cells


def trade(parts, width):
    count = lax.axis_size("gx")
    ends = count - 1
    heads = [lax.slice_in_dim(a, 0, width, axis=dim) for a, dim in parts]
    tails = [lax.slice_in_dim(a, a.shape[dim] - width, a.shape[dim], axis=dim) for a, dim in parts]
    pack = lambda pieces: jnp.concatenate([p.reshape(-1) for p in pieces])
    from_left = lax.ppermute(pack(tails), "gx", [(i, i + 1) for i in range(ends)])
    from_right = lax.ppermute(pack(heads), "gx", [(i + 1, i) for i in range(ends)])
    out = []
    offset = 0
    for (a, dim), h in zip(parts, heads):
        size = h.size
        left = from_left[offset : offset + size].reshape(h.shape)
        right = from_right[offset : offset + size].reshape(h.shape)
        offset += size
        out.append(jnp.concatenate([left, a, right], axis=dim))
    return out


def block_mean(field, factor):
    lead = field.shape[:-2]
    rows, cols = (field.shape[-2], field.shape[-1])
    shaped = field.reshape(lead + (rows // factor, factor, cols // factor, factor))
    return shaped.mean(axis=(-3, -1))


def reaction_field(friction, ice_mask, layers):
    open_water = (ice_mask == 0).astype(jnp.float32)
    grounded = (ice_mask == 2).astype(jnp.float32)
    bottom = (jnp.arange(layers) == 0).astype(jnp.float32).reshape(layers, 1, 1)
    return 0.02 + 2.0 * open_water[None] + bottom * (grounded * friction)[None]


def build_operator(eta_level, react_level, level_index):
    scale = horizontal_scale / 4.0**level_index
    weight_x = jnp.array([4.0, 1.0], jnp.float32).reshape(2, 1, 1, 1) * scale
    weight_y = jnp.array([1.0, 4.0], jnp.float32).reshape(2, 1, 1, 1) * scale
    inner = eta_level[:, 1:-1, :]
    face_x = weight_x * (0.5 * (eta_level[:, 1:, :] + eta_level[:, :-1, :]))[None]
    padded = jnp.pad(inner, ((0, 0), (0, 0), (1, 1)))
    face_y = weight_y * (0.5 * (padded[:, :, 1:] + padded[:, :, :-1]))[None]
    face_z = vertical_scale * 0.5 * (inner[1:] + inner[:-1])
    vertical = jnp.pad(face_z, ((1, 1), (0, 0), (0, 0)))
    diagonal = face_x[:, :, 1:] + face_x[:, :, :-1] + face_y[..., 1:] + face_y[..., :-1]
    diagonal = diagonal + (vertical[1:] + vertical[:-1] + react_level)[None]
    layers = diagonal.shape[1]
    inverses = []
    ratios = []
    for layer in range(layers):
        pivot = diagonal[:, layer]
        if layer > 0:
            pivot = pivot - face_z[layer - 1] * ratios[-1]
        inverse = 1.0 / pivot
        inverses.append(inverse)
        if layer < layers - 1:
            ratios.append(face_z[layer] * inverse)
    return (face_x, face_y, face_z, react_level, jnp.stack(inverses, 1), jnp.stack(ratios, 1))


def shrink(operator, cut):
    if cut == 0:
        return operator
    face_x, face_y, face_z, react_level, inverses, ratios = operator
    rows = face_y.shape[2]
    return (
        face_x[:, :, cut : rows + 1 - cut],
        face_y[:, :, cut : rows - cut],
        face_z[:, cut : rows - cut],
        react_level[:, cut : rows - cut],
        inverses[:, :, cut : rows - cut],
        ratios[:, :, cut : rows - cut],
    )


def apply_operator(field_rim, operator):
    face_x, face_y, face_z, react_level, inverses, ratios = operator
    field = field_rim[:, :, 1:-1, :]
    flux_x = face_x * (field_rim[:, :, 1:, :] - field_rim[:, :, :-1, :])
    result = -(flux_x[:, :, 1:] - flux_x[:, :, :-1])
    padded = jnp.pad(field, ((0, 0), (0, 0), (0, 0), (1, 1)))
    flux_y = face_y * (padded[..., 1:] - padded[..., :-1])
    result = result - (flux_y[..., 1:] - flux_y[..., :-1])
    flux_z = face_z[None] * (field[:, 1:] - field[:, :-1])
    flux_z = jnp.pad(flux_z, ((0, 0), (1, 1), (0, 0), (0, 0)))
    result = result - (flux_z[:, 1:] - flux_z[:, :-1])
    return result + react_level[None] * field


def line_solve(residual, operator):
    face_z, inverses, ratios = (operator[2], operator[4], operator[5])
    layers = residual.shape[1]
    forward = [residual[:, 0] * inverses[:, 0]]
    for layer in range(1, layers):
        forward.append((residual[:, layer] + face_z[layer - 1] * forward[-1]) * inverses[:, layer])
    backward = [forward[-1]]
    for layer in range(layers - 2, -1, -1):
        backward.append(forward[layer] + ratios[:, layer] * backward[-1])
    return jnp.stack(backward[::-1], 1)


def sweep(field_rim, target, operator):
    field = field_rim[:, :, 1:-1, :]
    return field + relax_weight * line_solve(target - apply_operator(field_rim, operator), operator)


def restrict(field):
    return block_mean(field, 2)


def prolong(field):
    return jnp.repeat(jnp.repeat(field, 2, axis=2), 2, axis=3)


def pad_rim(field):
    return jnp.pad(field, ((0, 0), (0, 0), (1, 1), (0, 0)))


def inside(cells, halo, extent):
    count = lax.axis_size("gx")
    first = lax.axis_index("gx") * cells - halo
    index = first + jnp.arange(extent)
    return ((index >= 0) & (index < count * cells)).reshape(1, 1, extent, 1)


def keep_inside(field, cells, halo):
    return jnp.where(inside(cells, halo, field.shape[2]), field, 0.0)


def window(full, dim, start, size, pad):
    widths = [(0, 0)] * full.ndim
    widths[dim] = (pad, pad)
    return lax.dynamic_slice_in_dim(jnp.pad(full, widths), start, size, axis=dim)


def nearby(cells, dim, hops):
    count = lax.axis_size("gx")
    lows = []
    highs = []
    for step in range(1, hops + 1):
        lows.insert(0, lax.ppermute(cells, "gx", [(i, i + step) for i in range(count - step)]))
        highs.append(lax.ppermute(cells, "gx", [(i + step, i) for i in range(count - step)]))
    return jnp.concatenate(lows + [cells] + highs, axis=dim)


def shards(misfit, adjoint_guess, viscosity, friction, ice_mask, forward_bed):
    layers, cells, cols = viscosity.shape
    where = lax.axis_index("gx")
    react_fine = reaction_field(friction, ice_mask, layers)
    react_pair = react_fine[:2]

    eta_1 = block_mean(viscosity, 2)
    eta_2 = block_mean(viscosity, 4)
    react_1 = block_mean(react_pair, 2)
    react_2 = block_mean(react_pair, 4)
    pieces = [eta_1, react_1, eta_2, react_2]
    packed = jnp.concatenate([p.reshape(-1) for p in pieces])
    gathered = lax.all_gather(packed[None], "gx", axis=0, tiled=True)
    count = gathered.shape[0]
    unpacked = []
    offset = 0
    for p in pieces:
        block = gathered[:, offset : offset + p.size].reshape((count,) + p.shape)
        offset += p.size
        unpacked.append(jnp.moveaxis(block, 0, 1).reshape((p.shape[0], count * p.shape[1], p.shape[2])))
    eta_1_all, react_1_all, eta_2_all, react_2_all = unpacked

    halo = 4
    eta_wide, guess_wide, misfit_wide, react_wide = trade(
        [(viscosity, 1), (adjoint_guess, 2), (misfit, 2), (react_pair, 1)], halo
    )
    react_wide = jnp.concatenate(
        [react_wide[:1], jnp.broadcast_to(react_wide[1:], (layers - 1,) + react_wide.shape[1:])], axis=0
    )
    op_0 = build_operator(eta_wide, react_wide[:, 1:-1], 0)
    fine = keep_inside(sweep(guess_wide, misfit_wide[:, :, 1:-1], op_0), cells, 3)
    fine = keep_inside(sweep(fine, misfit_wide[:, :, 2:-2], shrink(op_0, 1)), cells, 2)
    middle_rhs = restrict(misfit - apply_operator(fine[:, :, 1:-1], shrink(op_0, 3)))

    half = cells // 2
    rhs_wide = with_halo(middle_rhs, (("gx", 2),), half)
    eta_1_wide = window(eta_1_all, 1, where * half, 3 * half + 2, half + 1)
    react_1_wide = window(react_1_all, 1, where * half, 3 * half, half)
    react_1_wide = jnp.concatenate(
        [react_1_wide[:1], jnp.broadcast_to(react_1_wide[1:], (layers - 1,) + react_1_wide.shape[1:])], axis=0
    )
    op_1 = build_operator(eta_1_wide, react_1_wide, 1)
    middle = keep_inside(relax_weight * line_solve(rhs_wide, op_1), half, half)
    middle = keep_inside(sweep(middle, rhs_wide[:, :, 1:-1], shrink(op_1, 1)), half, half - 1)
    coarse_rhs = restrict(middle_rhs - apply_operator(middle[:, :, half - 2 : 2 * half], shrink(op_1, half)))

    quarter = cells // 4
    reach = 3
    span = reach + COARSE_SWEEPS - 1
    coarse_rhs_near = nearby(coarse_rhs, 2, span // quarter)
    eta_2_near = window(eta_2_all, 1, where * quarter, quarter + 2 * span + 2, span + 1)
    react_2_near = window(react_2_all, 1, where * quarter, quarter + 2 * span, span)
    react_2_near = jnp.concatenate(
        [react_2_near[:1], jnp.broadcast_to(react_2_near[1:], (layers - 1,) + react_2_near.shape[1:])], axis=0
    )
    op_2 = build_operator(eta_2_near, react_2_near, 2)
    coarse = jnp.zeros_like(coarse_rhs_near)
    for turn in range(COARSE_SWEEPS):
        coarse = keep_inside(sweep(pad_rim(coarse), coarse_rhs_near, op_2), quarter, span)
    coarse_near = coarse[:, :, span - reach : span + quarter + reach]

    lift = prolong(coarse_near)
    trim = 2 * reach - (half - 1)
    middle = middle + lift[:, :, trim : lift.shape[2] - trim]
    middle = keep_inside(sweep(middle, rhs_wide[:, :, 2:-2], shrink(op_1, 2)), half, half - 2)
    middle = keep_inside(sweep(middle, rhs_wide[:, :, 3:-3], shrink(op_1, 3)), half, half - 3)
    fine = fine + prolong(middle)
    fine = keep_inside(sweep(fine, misfit_wide[:, :, 3:-3], shrink(op_0, 2)), cells, 1)
    fine = sweep(fine, misfit, shrink(op_0, 3))
    grounded = (ice_mask == 2).astype(jnp.float32)
    gradient = -grounded * (forward_bed[0] * fine[0, 0] + forward_bed[1] * fine[1, 0])
    return (fine, gradient)


def solution(mesh):
    placed = (
        P("ens", None, "gx", None),
        P("ens", None, "gx", None),
        P("ens", "gx", None),
        P("gx", "ens"),
        P("gx", "ens"),
        P("ens", "gx", None),
    )
    return jax.shard_map(
        shards,
        mesh=mesh,
        in_specs=placed,
        out_specs=(P("ens", None, "gx", None), P("gx", "ens")),
        check_vma=False,
    )
```

```python
import functools

import jax
import jax.numpy as jnp
from jax import lax
from jax.experimental import pallas as pl
from jax.experimental.pallas import tpu as pltpu
from jax.sharding import PartitionSpec as P

NU = 2
COARSE_SWEEPS = 6


horizontal_scale = 1.0
vertical_scale = 4.0
relax_weight = 0.8


def with_halo(cells, sides, width):
    for axis, dim in sides:
        count = lax.axis_size(axis)
        ends = count - 1
        head = lax.slice_in_dim(cells, 0, width, axis=dim)
        tail = lax.slice_in_dim(cells, cells.shape[dim] - width, cells.shape[dim], axis=dim)
        cells = jnp.concatenate(
            [
                lax.ppermute(tail, axis, [(i, (i + 1) % count) for i in range(ends)]),
                cells,
                lax.ppermute(head, axis, [((i + 1) % count, i) for i in range(ends)]),
            ],
            axis=dim,
        )
    return cells


def trade(parts, width):
    count = lax.axis_size("gx")
    ends = count - 1
    heads = [lax.slice_in_dim(a, 0, width, axis=dim) for a, dim in parts]
    tails = [lax.slice_in_dim(a, a.shape[dim] - width, a.shape[dim], axis=dim) for a, dim in parts]
    pack = lambda pieces: jnp.concatenate([p.reshape(-1) for p in pieces])
    from_left = lax.ppermute(pack(tails), "gx", [(i, i + 1) for i in range(ends)])
    from_right = lax.ppermute(pack(heads), "gx", [(i + 1, i) for i in range(ends)])
    out = []
    offset = 0
    for (a, dim), h in zip(parts, heads):
        size = h.size
        left = from_left[offset : offset + size].reshape(h.shape)
        right = from_right[offset : offset + size].reshape(h.shape)
        offset += size
        out.append(jnp.concatenate([left, a, right], axis=dim))
    return out


def block_mean(field, factor):
    lead = field.shape[:-2]
    rows, cols = (field.shape[-2], field.shape[-1])
    shaped = field.reshape(lead + (rows // factor, factor, cols // factor, factor))
    return shaped.mean(axis=(-3, -1))


def reaction_field(friction, ice_mask, layers):
    open_water = (ice_mask == 0).astype(jnp.float32)
    grounded = (ice_mask == 2).astype(jnp.float32)
    bottom = (jnp.arange(layers) == 0).astype(jnp.float32).reshape(layers, 1, 1)
    return 0.02 + 2.0 * open_water[None] + bottom * (grounded * friction)[None]


def build_operator(eta_level, react_level, level_index):
    scale = horizontal_scale / 4.0**level_index
    weight_x = jnp.array([4.0, 1.0], jnp.float32).reshape(2, 1, 1, 1) * scale
    weight_y = jnp.array([1.0, 4.0], jnp.float32).reshape(2, 1, 1, 1) * scale
    inner = eta_level[:, 1:-1, :]
    face_x = weight_x * (0.5 * (eta_level[:, 1:, :] + eta_level[:, :-1, :]))[None]
    padded = jnp.pad(inner, ((0, 0), (0, 0), (1, 1)))
    face_y = weight_y * (0.5 * (padded[:, :, 1:] + padded[:, :, :-1]))[None]
    face_z = vertical_scale * 0.5 * (inner[1:] + inner[:-1])
    vertical = jnp.pad(face_z, ((1, 1), (0, 0), (0, 0)))
    diagonal = face_x[:, :, 1:] + face_x[:, :, :-1] + face_y[..., 1:] + face_y[..., :-1]
    diagonal = diagonal + (vertical[1:] + vertical[:-1] + react_level)[None]
    layers = diagonal.shape[1]
    inverses = []
    ratios = []
    for layer in range(layers):
        pivot = diagonal[:, layer]
        if layer > 0:
            pivot = pivot - face_z[layer - 1] * ratios[-1]
        inverse = 1.0 / pivot
        inverses.append(inverse)
        if layer < layers - 1:
            ratios.append(face_z[layer] * inverse)
    return (face_x, face_y, face_z, react_level, jnp.stack(inverses, 1), jnp.stack(ratios, 1))


def lane_ops(operator):
    face_x, face_y, face_z, react_level, inverses, ratios = operator
    return (face_x[:, :, :-1], face_x[:, :, 1:], face_y[..., :-1], face_y[..., 1:], face_z, react_level, inverses, ratios)


def sweep_kernel(w_ref, b_ref, fxl_ref, fxr_ref, fyl_ref, fyr_ref, fz_ref, re_ref, inv_ref, rat_ref, mask_ref, out_ref,
                 *, rows, cut_w, cut_b, cut_op, mode):
    layers = out_ref.shape[1]
    cols = out_ref.shape[3]
    lane = lax.broadcasted_iota(jnp.int32, (rows, cols), 1)
    probe = pltpu.roll(lane, 1, 1)
    forward_roll = probe == jnp.where(lane == 0, cols - 1, lane - 1)
    first_col = lane == 0
    last_col = lane == cols - 1

    def cell(ref, k, cut):
        return ref[0, k, pl.ds(cut, rows), :]

    def field(k):
        return w_ref[0, k, pl.ds(cut_w + 1, rows), :]

    def applied(k):
        w = field(k)
        west = w_ref[0, k, pl.ds(cut_w, rows), :]
        east = w_ref[0, k, pl.ds(cut_w + 2, rows), :]
        result = -(cell(fxr_ref, k, cut_op) * (east - w) - cell(fxl_ref, k, cut_op) * (w - west))
        ahead = pltpu.roll(w, 1, 1)
        behind = pltpu.roll(w, cols - 1, 1)
        south = jnp.where(forward_roll, ahead, behind)
        north = jnp.where(forward_roll, behind, ahead)
        south = jnp.where(first_col, 0.0, south)
        north = jnp.where(last_col, 0.0, north)
        result = result - (cell(fyr_ref, k, cut_op) * (north - w) - cell(fyl_ref, k, cut_op) * (w - south))
        up = fz_ref[k, pl.ds(cut_op, rows), :] * (field(k + 1) - w) if k < layers - 1 else 0.0
        down = fz_ref[k - 1, pl.ds(cut_op, rows), :] * (w - field(k - 1)) if k > 0 else 0.0
        result = result - (up - down)
        return result + re_ref[k, pl.ds(cut_op, rows), :] * w

    if mode == "residual":
        for k in range(layers):
            out_ref[0, k] = cell(b_ref, k, cut_b) - applied(k)
        return
    keep = mask_ref[...] > 0.5
    previous = None
    for k in range(layers):
        residual = cell(b_ref, k, cut_b)
        if mode == "sweep":
            residual = residual - applied(k)
        if k == 0:
            forward = residual * cell(inv_ref, 0, cut_op)
        else:
            forward = (residual + fz_ref[k - 1, pl.ds(cut_op, rows), :] * previous) * cell(inv_ref, k, cut_op)
        out_ref[0, k] = forward
        previous = forward
    back = previous
    for k in range(layers - 1, -1, -1):
        if k < layers - 1:
            back = out_ref[0, k] + rat_ref[0, k, pl.ds(cut_op, rows), :] * back
        if mode == "sweep":
            value = field(k) + relax_weight * back
        else:
            value = relax_weight * back
        out_ref[0, k] = jnp.where(keep, value, 0.0)


def kernel_sweep(field_rim, target, lanes, cut_b, cut_op, mask, mode="sweep", cut_w=0, rows=None):
    parts, layers, rows_rim, cols = field_rim.shape
    rows = rows_rim - 2 if rows is None else rows
    fxl, fxr, fyl, fyr, fz, re, inv, rat = lanes
    per_part = lambda a: pl.BlockSpec((1,) + a.shape[1:], lambda c: (c,) + (0,) * (a.ndim - 1))
    whole = lambda a: pl.BlockSpec(a.shape, lambda c: (0,) * a.ndim)
    operands = [field_rim, target, fxl, fxr, fyl, fyr, fz, re, inv, rat, mask]
    specs = [per_part(field_rim), per_part(target), per_part(fxl), per_part(fxr), per_part(fyl), per_part(fyr),
             whole(fz), whole(re), per_part(inv), per_part(rat), whole(mask)]
    body = functools.partial(sweep_kernel, rows=rows, cut_w=cut_w, cut_b=cut_b, cut_op=cut_op, mode=mode)
    return pl.pallas_call(
        body,
        grid=(parts,),
        in_specs=specs,
        out_specs=pl.BlockSpec((1, layers, rows, cols), lambda c: (c, 0, 0, 0)),
        out_shape=jax.ShapeDtypeStruct((parts, layers, rows, cols), jnp.float32),
    )(*operands)


def rows_inside(cells, halo, extent, cols):
    return jnp.broadcast_to(inside(cells, halo, extent)[0, 0], (extent, cols)).astype(jnp.float32)


def shrink(operator, cut):
    if cut == 0:
        return operator
    face_x, face_y, face_z, react_level, inverses, ratios = operator
    rows = face_y.shape[2]
    return (
        face_x[:, :, cut : rows + 1 - cut],
        face_y[:, :, cut : rows - cut],
        face_z[:, cut : rows - cut],
        react_level[:, cut : rows - cut],
        inverses[:, :, cut : rows - cut],
        ratios[:, :, cut : rows - cut],
    )


def apply_operator(field_rim, operator):
    face_x, face_y, face_z, react_level, inverses, ratios = operator
    field = field_rim[:, :, 1:-1, :]
    flux_x = face_x * (field_rim[:, :, 1:, :] - field_rim[:, :, :-1, :])
    result = -(flux_x[:, :, 1:] - flux_x[:, :, :-1])
    padded = jnp.pad(field, ((0, 0), (0, 0), (0, 0), (1, 1)))
    flux_y = face_y * (padded[..., 1:] - padded[..., :-1])
    result = result - (flux_y[..., 1:] - flux_y[..., :-1])
    flux_z = face_z[None] * (field[:, 1:] - field[:, :-1])
    flux_z = jnp.pad(flux_z, ((0, 0), (1, 1), (0, 0), (0, 0)))
    result = result - (flux_z[:, 1:] - flux_z[:, :-1])
    return result + react_level[None] * field


def line_solve(residual, operator):
    face_z, inverses, ratios = (operator[2], operator[4], operator[5])
    layers = residual.shape[1]
    forward = [residual[:, 0] * inverses[:, 0]]
    for layer in range(1, layers):
        forward.append((residual[:, layer] + face_z[layer - 1] * forward[-1]) * inverses[:, layer])
    backward = [forward[-1]]
    for layer in range(layers - 2, -1, -1):
        backward.append(forward[layer] + ratios[:, layer] * backward[-1])
    return jnp.stack(backward[::-1], 1)


def sweep(field_rim, target, operator):
    field = field_rim[:, :, 1:-1, :]
    return field + relax_weight * line_solve(target - apply_operator(field_rim, operator), operator)


def restrict(field):
    return block_mean(field, 2)


def prolong(field):
    return jnp.repeat(jnp.repeat(field, 2, axis=2), 2, axis=3)


def pad_rim(field):
    return jnp.pad(field, ((0, 0), (0, 0), (1, 1), (0, 0)))


def inside(cells, halo, extent):
    count = lax.axis_size("gx")
    first = lax.axis_index("gx") * cells - halo
    index = first + jnp.arange(extent)
    return ((index >= 0) & (index < count * cells)).reshape(1, 1, extent, 1)


def keep_inside(field, cells, halo):
    return jnp.where(inside(cells, halo, field.shape[2]), field, 0.0)


def window(full, dim, start, size, pad):
    widths = [(0, 0)] * full.ndim
    widths[dim] = (pad, pad)
    return lax.dynamic_slice_in_dim(jnp.pad(full, widths), start, size, axis=dim)


def nearby(cells, dim, hops):
    count = lax.axis_size("gx")
    lows = []
    highs = []
    for step in range(1, hops + 1):
        lows.insert(0, lax.ppermute(cells, "gx", [(i, i + step) for i in range(count - step)]))
        highs.append(lax.ppermute(cells, "gx", [(i + step, i) for i in range(count - step)]))
    return jnp.concatenate(lows + [cells] + highs, axis=dim)


def shards(misfit, adjoint_guess, viscosity, friction, ice_mask, forward_bed):
    layers, cells, cols = viscosity.shape
    where = lax.axis_index("gx")
    react_fine = reaction_field(friction, ice_mask, layers)
    react_pair = react_fine[:2]

    eta_1 = block_mean(viscosity, 2)
    eta_2 = block_mean(viscosity, 4)
    react_1 = block_mean(react_pair, 2)
    react_2 = block_mean(react_pair, 4)
    pieces = [eta_1, react_1, eta_2, react_2]
    packed = jnp.concatenate([p.reshape(-1) for p in pieces])
    gathered = lax.all_gather(packed[None], "gx", axis=0, tiled=True)
    count = gathered.shape[0]
    unpacked = []
    offset = 0
    for p in pieces:
        block = gathered[:, offset : offset + p.size].reshape((count,) + p.shape)
        offset += p.size
        unpacked.append(jnp.moveaxis(block, 0, 1).reshape((p.shape[0], count * p.shape[1], p.shape[2])))
    eta_1_all, react_1_all, eta_2_all, react_2_all = unpacked

    halo = 4
    eta_wide, guess_wide, misfit_wide, react_wide = trade(
        [(viscosity, 1), (adjoint_guess, 2), (misfit, 2), (react_pair, 1)], halo
    )
    react_wide = jnp.concatenate(
        [react_wide[:1], jnp.broadcast_to(react_wide[1:], (layers - 1,) + react_wide.shape[1:])], axis=0
    )
    op_0 = lane_ops(build_operator(eta_wide, react_wide[:, 1:-1], 0))
    fine = kernel_sweep(guess_wide, misfit_wide, op_0, 1, 0, rows_inside(cells, 3, cells + 6, cols))
    fine = kernel_sweep(fine, misfit_wide, op_0, 2, 1, rows_inside(cells, 2, cells + 4, cols))
    residual = kernel_sweep(fine, misfit_wide, op_0, 4, 3, rows_inside(cells, 0, cells, cols), "residual", 1, cells)
    middle_rhs = restrict(residual)

    half = cells // 2
    wide = cols // 2
    rhs_wide = with_halo(middle_rhs, (("gx", 2),), half)
    eta_1_wide = window(eta_1_all, 1, where * half, 3 * half + 2, half + 1)
    react_1_wide = window(react_1_all, 1, where * half, 3 * half, half)
    react_1_wide = jnp.concatenate(
        [react_1_wide[:1], jnp.broadcast_to(react_1_wide[1:], (layers - 1,) + react_1_wide.shape[1:])], axis=0
    )
    op_1 = lane_ops(build_operator(eta_1_wide, react_1_wide, 1))
    middle = kernel_sweep(rhs_wide, rhs_wide, op_1, 0, 0, rows_inside(half, half, 3 * half, wide), "zero", 0, 3 * half)
    middle = kernel_sweep(middle, rhs_wide, op_1, 1, 1, rows_inside(half, half - 1, 3 * half - 2, wide))
    residual = kernel_sweep(middle, rhs_wide, op_1, half, half, rows_inside(half, 0, half, wide), "residual", half - 2, half)
    coarse_rhs = restrict(residual)

    quarter = cells // 4
    narrow = cols // 4
    reach = 3
    span = reach + COARSE_SWEEPS - 1
    coarse_rhs_near = nearby(coarse_rhs, 2, span // quarter)
    eta_2_near = window(eta_2_all, 1, where * quarter, quarter + 2 * span + 2, span + 1)
    react_2_near = window(react_2_all, 1, where * quarter, quarter + 2 * span, span)
    react_2_near = jnp.concatenate(
        [react_2_near[:1], jnp.broadcast_to(react_2_near[1:], (layers - 1,) + react_2_near.shape[1:])], axis=0
    )
    op_2 = lane_ops(build_operator(eta_2_near, react_2_near, 2))
    extent = quarter + 2 * span
    coarse_mask = rows_inside(quarter, span, extent, narrow)
    coarse = kernel_sweep(coarse_rhs_near, coarse_rhs_near, op_2, 0, 0, coarse_mask, "zero", 0, extent)
    for turn in range(COARSE_SWEEPS - 1):
        coarse = kernel_sweep(pad_rim(coarse), coarse_rhs_near, op_2, 0, 0, coarse_mask)
    coarse_near = coarse[:, :, span - reach : span + quarter + reach]

    lift = prolong(coarse_near)
    trim = 2 * reach - (half - 1)
    middle = middle + lift[:, :, trim : lift.shape[2] - trim]
    middle = kernel_sweep(middle, rhs_wide, op_1, 2, 2, rows_inside(half, half - 2, 3 * half - 4, wide))
    middle = kernel_sweep(middle, rhs_wide, op_1, 3, 3, rows_inside(half, half - 3, 3 * half - 6, wide))
    fine = fine + prolong(middle)
    fine = kernel_sweep(fine, misfit_wide, op_0, 3, 2, rows_inside(cells, 1, cells + 2, cols))
    fine = kernel_sweep(fine, misfit_wide, op_0, 4, 3, rows_inside(cells, 0, cells, cols))
    grounded = (ice_mask == 2).astype(jnp.float32)
    gradient = -grounded * (forward_bed[0] * fine[0, 0] + forward_bed[1] * fine[1, 0])
    return (fine, gradient)


def solution(mesh):
    placed = (
        P("ens", None, "gx", None),
        P("ens", None, "gx", None),
        P("ens", "gx", None),
        P("gx", "ens"),
        P("gx", "ens"),
        P("ens", "gx", None),
    )
    return jax.shard_map(
        shards,
        mesh=mesh,
        in_specs=placed,
        out_specs=(P("ens", None, "gx", None), P("gx", "ens")),
        check_vma=False,
    )
```

```python
import functools

import jax
import jax.numpy as jnp
from jax import lax
from jax.experimental import pallas as pl
from jax.experimental.pallas import tpu as pltpu
from jax.sharding import PartitionSpec as P

NU = 2
COARSE_SWEEPS = 6


horizontal_scale = 1.0
vertical_scale = 4.0
relax_weight = 0.8


def with_halo(cells, sides, width):
    for axis, dim in sides:
        count = lax.axis_size(axis)
        ends = count - 1
        head = lax.slice_in_dim(cells, 0, width, axis=dim)
        tail = lax.slice_in_dim(cells, cells.shape[dim] - width, cells.shape[dim], axis=dim)
        cells = jnp.concatenate(
            [
                lax.ppermute(tail, axis, [(i, (i + 1) % count) for i in range(ends)]),
                cells,
                lax.ppermute(head, axis, [((i + 1) % count, i) for i in range(ends)]),
            ],
            axis=dim,
        )
    return cells


def trade(parts, width):
    count = lax.axis_size("gx")
    ends = count - 1
    heads = [lax.slice_in_dim(a, 0, width, axis=dim) for a, dim in parts]
    tails = [lax.slice_in_dim(a, a.shape[dim] - width, a.shape[dim], axis=dim) for a, dim in parts]
    pack = lambda pieces: jnp.concatenate([p.reshape(-1) for p in pieces])
    from_left = lax.ppermute(pack(tails), "gx", [(i, i + 1) for i in range(ends)])
    from_right = lax.ppermute(pack(heads), "gx", [(i + 1, i) for i in range(ends)])
    out = []
    offset = 0
    for (a, dim), h in zip(parts, heads):
        size = h.size
        left = from_left[offset : offset + size].reshape(h.shape)
        right = from_right[offset : offset + size].reshape(h.shape)
        offset += size
        out.append(jnp.concatenate([left, a, right], axis=dim))
    return out


def block_mean(field, factor):
    lead = field.shape[:-2]
    rows, cols = (field.shape[-2], field.shape[-1])
    shaped = field.reshape(lead + (rows // factor, factor, cols // factor, factor))
    return shaped.mean(axis=(-3, -1))


def reaction_field(friction, ice_mask, layers):
    open_water = (ice_mask == 0).astype(jnp.float32)
    grounded = (ice_mask == 2).astype(jnp.float32)
    bottom = (jnp.arange(layers) == 0).astype(jnp.float32).reshape(layers, 1, 1)
    return 0.02 + 2.0 * open_water[None] + bottom * (grounded * friction)[None]


def build_operator(eta_level, react_level, level_index):
    scale = horizontal_scale / 4.0**level_index
    weight_x = jnp.array([4.0, 1.0], jnp.float32).reshape(2, 1, 1, 1) * scale
    weight_y = jnp.array([1.0, 4.0], jnp.float32).reshape(2, 1, 1, 1) * scale
    inner = eta_level[:, 1:-1, :]
    face_x = weight_x * (0.5 * (eta_level[:, 1:, :] + eta_level[:, :-1, :]))[None]
    padded = jnp.pad(inner, ((0, 0), (0, 0), (1, 1)))
    face_y = weight_y * (0.5 * (padded[:, :, 1:] + padded[:, :, :-1]))[None]
    face_z = vertical_scale * 0.5 * (inner[1:] + inner[:-1])
    vertical = jnp.pad(face_z, ((1, 1), (0, 0), (0, 0)))
    diagonal = face_x[:, :, 1:] + face_x[:, :, :-1] + face_y[..., 1:] + face_y[..., :-1]
    diagonal = diagonal + (vertical[1:] + vertical[:-1] + react_level)[None]
    layers = diagonal.shape[1]
    inverses = []
    ratios = []
    for layer in range(layers):
        pivot = diagonal[:, layer]
        if layer > 0:
            pivot = pivot - face_z[layer - 1] * ratios[-1]
        inverse = 1.0 / pivot
        inverses.append(inverse)
        if layer < layers - 1:
            ratios.append(face_z[layer] * inverse)
    return (face_x, face_y, face_z, react_level, jnp.stack(inverses, 1), jnp.stack(ratios, 1))


def lane_ops(operator):
    face_x, face_y, face_z, react_level, inverses, ratios = operator
    return (face_x[:, :, :-1], face_x[:, :, 1:], face_y[..., :-1], face_y[..., 1:], face_z, react_level, inverses, ratios)


def sweep_kernel(w_ref, b_ref, fxl_ref, fxr_ref, fyl_ref, fyr_ref, fz_ref, re_ref, inv_ref, rat_ref, mask_ref, out_ref,
                 *, rows, cut_w, cut_b, cut_op, mode):
    layers = out_ref.shape[1]
    cols = out_ref.shape[3]
    lane = lax.broadcasted_iota(jnp.int32, (rows, cols), 1)
    probe = pltpu.roll(lane, 1, 1)
    forward_roll = probe == jnp.where(lane == 0, cols - 1, lane - 1)
    first_col = lane == 0
    last_col = lane == cols - 1

    def cell(ref, k, cut):
        return ref[0, k, pl.ds(cut, rows), :]

    def field(k):
        return w_ref[0, k, pl.ds(cut_w + 1, rows), :]

    def applied(k):
        w = field(k)
        west = w_ref[0, k, pl.ds(cut_w, rows), :]
        east = w_ref[0, k, pl.ds(cut_w + 2, rows), :]
        result = -(cell(fxr_ref, k, cut_op) * (east - w) - cell(fxl_ref, k, cut_op) * (w - west))
        ahead = pltpu.roll(w, 1, 1)
        behind = pltpu.roll(w, cols - 1, 1)
        south = jnp.where(forward_roll, ahead, behind)
        north = jnp.where(forward_roll, behind, ahead)
        south = jnp.where(first_col, 0.0, south)
        north = jnp.where(last_col, 0.0, north)
        result = result - (cell(fyr_ref, k, cut_op) * (north - w) - cell(fyl_ref, k, cut_op) * (w - south))
        up = fz_ref[k, pl.ds(cut_op, rows), :] * (field(k + 1) - w) if k < layers - 1 else 0.0
        down = fz_ref[k - 1, pl.ds(cut_op, rows), :] * (w - field(k - 1)) if k > 0 else 0.0
        result = result - (up - down)
        return result + re_ref[k, pl.ds(cut_op, rows), :] * w

    if mode == "residual":
        for k in range(layers):
            out_ref[0, k] = cell(b_ref, k, cut_b) - applied(k)
        return
    keep = mask_ref[...] > 0.5
    previous = None
    for k in range(layers):
        residual = cell(b_ref, k, cut_b)
        if mode == "sweep":
            residual = residual - applied(k)
        if k == 0:
            forward = residual * cell(inv_ref, 0, cut_op)
        else:
            forward = (residual + fz_ref[k - 1, pl.ds(cut_op, rows), :] * previous) * cell(inv_ref, k, cut_op)
        out_ref[0, k] = forward
        previous = forward
    back = previous
    for k in range(layers - 1, -1, -1):
        if k < layers - 1:
            back = out_ref[0, k] + rat_ref[0, k, pl.ds(cut_op, rows), :] * back
        if mode == "sweep":
            value = field(k) + relax_weight * back
        else:
            value = relax_weight * back
        out_ref[0, k] = jnp.where(keep, value, 0.0)


def kernel_sweep(field_rim, target, lanes, cut_b, cut_op, mask, mode="sweep", cut_w=0, rows=None):
    parts, layers, rows_rim, cols = field_rim.shape
    rows = rows_rim - 2 if rows is None else rows
    fxl, fxr, fyl, fyr, fz, re, inv, rat = lanes
    per_part = lambda a: pl.BlockSpec((1,) + a.shape[1:], lambda c: (c,) + (0,) * (a.ndim - 1))
    whole = lambda a: pl.BlockSpec(a.shape, lambda c: (0,) * a.ndim)
    operands = [field_rim, target, fxl, fxr, fyl, fyr, fz, re, inv, rat, mask]
    specs = [per_part(field_rim), per_part(target), per_part(fxl), per_part(fxr), per_part(fyl), per_part(fyr),
             whole(fz), whole(re), per_part(inv), per_part(rat), whole(mask)]
    body = functools.partial(sweep_kernel, rows=rows, cut_w=cut_w, cut_b=cut_b, cut_op=cut_op, mode=mode)
    return pl.pallas_call(
        body,
        grid=(parts,),
        in_specs=specs,
        out_specs=pl.BlockSpec((1, layers, rows, cols), lambda c: (c, 0, 0, 0)),
        out_shape=jax.ShapeDtypeStruct((parts, layers, rows, cols), jnp.float32),
    )(*operands)


def build_kernel(eta_ref, re_ref, fxl_ref, fxr_ref, fyl_ref, fyr_ref, fz_ref, reo_ref, inv_ref, rat_ref,
                 *, rows, cut_re, scale):
    component = pl.program_id(0)
    layers = eta_ref.shape[0]
    cols = eta_ref.shape[2]
    lane = lax.broadcasted_iota(jnp.int32, (rows, cols), 1)
    probe = pltpu.roll(lane, 1, 1)
    forward_roll = probe == jnp.where(lane == 0, cols - 1, lane - 1)
    first_col = lane == 0
    last_col = lane == cols - 1
    weight_x = jnp.where(component == 0, 4.0, 1.0) * scale
    weight_y = jnp.where(component == 0, 1.0, 4.0) * scale

    def inner(k):
        return eta_ref[k, pl.ds(1, rows), :]

    faces_z = [vertical_scale * 0.5 * (inner(k + 1) + inner(k)) for k in range(layers - 1)]
    ratio = None
    for k in range(layers):
        middle = inner(k)
        west = eta_ref[k, pl.ds(0, rows), :]
        east = eta_ref[k, pl.ds(2, rows), :]
        ahead = pltpu.roll(middle, 1, 1)
        behind = pltpu.roll(middle, cols - 1, 1)
        south = jnp.where(first_col, 0.0, jnp.where(forward_roll, ahead, behind))
        north = jnp.where(last_col, 0.0, jnp.where(forward_roll, behind, ahead))
        face_w = weight_x * (0.5 * (middle + west))
        face_e = weight_x * (0.5 * (east + middle))
        face_s = weight_y * (0.5 * (middle + south))
        face_n = weight_y * (0.5 * (north + middle))
        react = re_ref[min(k, re_ref.shape[0] - 1), pl.ds(cut_re, rows), :]
        up = faces_z[k] if k < layers - 1 else 0.0
        down = faces_z[k - 1] if k > 0 else 0.0
        diagonal = face_e + face_w + face_n + face_s
        diagonal = diagonal + (up + down + react)
        if k > 0:
            diagonal = diagonal - faces_z[k - 1] * ratio
        inverse = 1.0 / diagonal
        fxl_ref[0, k] = face_w
        fxr_ref[0, k] = face_e
        fyl_ref[0, k] = face_s
        fyr_ref[0, k] = face_n
        reo_ref[k] = react
        inv_ref[0, k] = inverse
        if k < layers - 1:
            ratio = faces_z[k] * inverse
            fz_ref[k] = faces_z[k]
            rat_ref[0, k] = ratio


def kernel_operator(eta_level, react_level, level_index, cut_re=0):
    layers, rows_eta, cols = eta_level.shape
    rows = rows_eta - 2
    whole = lambda a: pl.BlockSpec(a.shape, lambda c: (0,) * a.ndim)
    per_part = lambda shape: pl.BlockSpec((1,) + shape, lambda c: (c,) + (0,) * len(shape))
    cell = (layers, rows, cols)
    faces = (layers - 1, rows, cols)
    body = functools.partial(build_kernel, rows=rows, cut_re=cut_re, scale=horizontal_scale / 4.0**level_index)
    shapes = [(2,) + cell] * 4 + [faces, cell, (2,) + cell, (2,) + faces]
    specs = [per_part(cell)] * 4 + [
        pl.BlockSpec(faces, lambda c: (0, 0, 0)),
        pl.BlockSpec(cell, lambda c: (0, 0, 0)),
        per_part(cell),
        per_part(faces),
    ]
    return tuple(
        pl.pallas_call(
            body,
            grid=(2,),
            in_specs=[whole(eta_level), whole(react_level)],
            out_specs=specs,
            out_shape=[jax.ShapeDtypeStruct(s, jnp.float32) for s in shapes],
        )(eta_level, react_level)
    )


def rows_inside(cells, halo, extent, cols):
    return jnp.broadcast_to(inside(cells, halo, extent)[0, 0], (extent, cols)).astype(jnp.float32)


def shrink(operator, cut):
    if cut == 0:
        return operator
    face_x, face_y, face_z, react_level, inverses, ratios = operator
    rows = face_y.shape[2]
    return (
        face_x[:, :, cut : rows + 1 - cut],
        face_y[:, :, cut : rows - cut],
        face_z[:, cut : rows - cut],
        react_level[:, cut : rows - cut],
        inverses[:, :, cut : rows - cut],
        ratios[:, :, cut : rows - cut],
    )


def apply_operator(field_rim, operator):
    face_x, face_y, face_z, react_level, inverses, ratios = operator
    field = field_rim[:, :, 1:-1, :]
    flux_x = face_x * (field_rim[:, :, 1:, :] - field_rim[:, :, :-1, :])
    result = -(flux_x[:, :, 1:] - flux_x[:, :, :-1])
    padded = jnp.pad(field, ((0, 0), (0, 0), (0, 0), (1, 1)))
    flux_y = face_y * (padded[..., 1:] - padded[..., :-1])
    result = result - (flux_y[..., 1:] - flux_y[..., :-1])
    flux_z = face_z[None] * (field[:, 1:] - field[:, :-1])
    flux_z = jnp.pad(flux_z, ((0, 0), (1, 1), (0, 0), (0, 0)))
    result = result - (flux_z[:, 1:] - flux_z[:, :-1])
    return result + react_level[None] * field


def line_solve(residual, operator):
    face_z, inverses, ratios = (operator[2], operator[4], operator[5])
    layers = residual.shape[1]
    forward = [residual[:, 0] * inverses[:, 0]]
    for layer in range(1, layers):
        forward.append((residual[:, layer] + face_z[layer - 1] * forward[-1]) * inverses[:, layer])
    backward = [forward[-1]]
    for layer in range(layers - 2, -1, -1):
        backward.append(forward[layer] + ratios[:, layer] * backward[-1])
    return jnp.stack(backward[::-1], 1)


def sweep(field_rim, target, operator):
    field = field_rim[:, :, 1:-1, :]
    return field + relax_weight * line_solve(target - apply_operator(field_rim, operator), operator)


def restrict(field):
    return block_mean(field, 2)


def prolong(field):
    return jnp.repeat(jnp.repeat(field, 2, axis=2), 2, axis=3)


def pad_rim(field):
    return jnp.pad(field, ((0, 0), (0, 0), (1, 1), (0, 0)))


def inside(cells, halo, extent):
    count = lax.axis_size("gx")
    first = lax.axis_index("gx") * cells - halo
    index = first + jnp.arange(extent)
    return ((index >= 0) & (index < count * cells)).reshape(1, 1, extent, 1)


def keep_inside(field, cells, halo):
    return jnp.where(inside(cells, halo, field.shape[2]), field, 0.0)


def window(full, dim, start, size, pad):
    widths = [(0, 0)] * full.ndim
    widths[dim] = (pad, pad)
    return lax.dynamic_slice_in_dim(jnp.pad(full, widths), start, size, axis=dim)


def nearby(cells, dim, hops):
    count = lax.axis_size("gx")
    lows = []
    highs = []
    for step in range(1, hops + 1):
        lows.insert(0, lax.ppermute(cells, "gx", [(i, i + step) for i in range(count - step)]))
        highs.append(lax.ppermute(cells, "gx", [(i + step, i) for i in range(count - step)]))
    return jnp.concatenate(lows + [cells] + highs, axis=dim)


def shards(misfit, adjoint_guess, viscosity, friction, ice_mask, forward_bed):
    layers, cells, cols = viscosity.shape
    where = lax.axis_index("gx")
    react_fine = reaction_field(friction, ice_mask, layers)
    react_pair = react_fine[:2]

    eta_1 = block_mean(viscosity, 2)
    eta_2 = block_mean(viscosity, 4)
    react_1 = block_mean(react_pair, 2)
    react_2 = block_mean(react_pair, 4)
    pieces = [eta_1, react_1, eta_2, react_2]
    packed = jnp.concatenate([p.reshape(-1) for p in pieces])
    gathered = lax.all_gather(packed[None], "gx", axis=0, tiled=True)
    count = gathered.shape[0]
    unpacked = []
    offset = 0
    for p in pieces:
        block = gathered[:, offset : offset + p.size].reshape((count,) + p.shape)
        offset += p.size
        unpacked.append(jnp.moveaxis(block, 0, 1).reshape((p.shape[0], count * p.shape[1], p.shape[2])))
    eta_1_all, react_1_all, eta_2_all, react_2_all = unpacked

    halo = 4
    eta_wide, guess_wide, misfit_wide, react_wide = trade(
        [(viscosity, 1), (adjoint_guess, 2), (misfit, 2), (react_pair, 1)], halo
    )
    op_0 = kernel_operator(eta_wide, react_wide, 0, 1)
    fine = kernel_sweep(guess_wide, misfit_wide, op_0, 1, 0, rows_inside(cells, 3, cells + 6, cols))
    fine = kernel_sweep(fine, misfit_wide, op_0, 2, 1, rows_inside(cells, 2, cells + 4, cols))
    residual = kernel_sweep(fine, misfit_wide, op_0, 4, 3, rows_inside(cells, 0, cells, cols), "residual", 1, cells)
    middle_rhs = restrict(residual)

    half = cells // 2
    wide = cols // 2
    rhs_wide = with_halo(middle_rhs, (("gx", 2),), half)
    eta_1_wide = window(eta_1_all, 1, where * half, 3 * half + 2, half + 1)
    react_1_wide = window(react_1_all, 1, where * half, 3 * half, half)
    op_1 = kernel_operator(eta_1_wide, react_1_wide, 1)
    middle = kernel_sweep(rhs_wide, rhs_wide, op_1, 0, 0, rows_inside(half, half, 3 * half, wide), "zero", 0, 3 * half)
    middle = kernel_sweep(middle, rhs_wide, op_1, 1, 1, rows_inside(half, half - 1, 3 * half - 2, wide))
    residual = kernel_sweep(middle, rhs_wide, op_1, half, half, rows_inside(half, 0, half, wide), "residual", half - 2, half)
    coarse_rhs = restrict(residual)

    quarter = cells // 4
    narrow = cols // 4
    reach = 3
    span = reach + COARSE_SWEEPS - 1
    coarse_rhs_near = nearby(coarse_rhs, 2, span // quarter)
    eta_2_near = window(eta_2_all, 1, where * quarter, quarter + 2 * span + 2, span + 1)
    react_2_near = window(react_2_all, 1, where * quarter, quarter + 2 * span, span)
    op_2 = kernel_operator(eta_2_near, react_2_near, 2)
    extent = quarter + 2 * span
    coarse_mask = rows_inside(quarter, span, extent, narrow)
    coarse = kernel_sweep(coarse_rhs_near, coarse_rhs_near, op_2, 0, 0, coarse_mask, "zero", 0, extent)
    for turn in range(COARSE_SWEEPS - 1):
        coarse = kernel_sweep(pad_rim(coarse), coarse_rhs_near, op_2, 0, 0, coarse_mask)
    coarse_near = coarse[:, :, span - reach : span + quarter + reach]

    lift = prolong(coarse_near)
    trim = 2 * reach - (half - 1)
    middle = middle + lift[:, :, trim : lift.shape[2] - trim]
    middle = kernel_sweep(middle, rhs_wide, op_1, 2, 2, rows_inside(half, half - 2, 3 * half - 4, wide))
    middle = kernel_sweep(middle, rhs_wide, op_1, 3, 3, rows_inside(half, half - 3, 3 * half - 6, wide))
    fine = fine + prolong(middle)
    fine = kernel_sweep(fine, misfit_wide, op_0, 3, 2, rows_inside(cells, 1, cells + 2, cols))
    fine = kernel_sweep(fine, misfit_wide, op_0, 4, 3, rows_inside(cells, 0, cells, cols))
    grounded = (ice_mask == 2).astype(jnp.float32)
    gradient = -grounded * (forward_bed[0] * fine[0, 0] + forward_bed[1] * fine[1, 0])
    return (fine, gradient)


def solution(mesh):
    placed = (
        P("ens", None, "gx", None),
        P("ens", None, "gx", None),
        P("ens", "gx", None),
        P("gx", "ens"),
        P("gx", "ens"),
        P("ens", "gx", None),
    )
    return jax.shard_map(
        shards,
        mesh=mesh,
        in_specs=placed,
        out_specs=(P("ens", None, "gx", None), P("gx", "ens")),
        check_vma=False,
    )
```

```python
import functools

import jax
import jax.numpy as jnp
from jax import lax
from jax.experimental import pallas as pl
from jax.experimental.pallas import tpu as pltpu
from jax.sharding import PartitionSpec as P

NU = 2
COARSE_SWEEPS = 6


horizontal_scale = 1.0
vertical_scale = 4.0
relax_weight = 0.8


def with_halo(cells, sides, width):
    for axis, dim in sides:
        count = lax.axis_size(axis)
        ends = count - 1
        head = lax.slice_in_dim(cells, 0, width, axis=dim)
        tail = lax.slice_in_dim(cells, cells.shape[dim] - width, cells.shape[dim], axis=dim)
        cells = jnp.concatenate(
            [
                lax.ppermute(tail, axis, [(i, (i + 1) % count) for i in range(ends)]),
                cells,
                lax.ppermute(head, axis, [((i + 1) % count, i) for i in range(ends)]),
            ],
            axis=dim,
        )
    return cells


def trade(parts, width):
    count = lax.axis_size("gx")
    ends = count - 1
    heads = [lax.slice_in_dim(a, 0, width, axis=dim) for a, dim in parts]
    tails = [lax.slice_in_dim(a, a.shape[dim] - width, a.shape[dim], axis=dim) for a, dim in parts]
    pack = lambda pieces: jnp.concatenate([p.reshape(-1) for p in pieces])
    from_left = lax.ppermute(pack(tails), "gx", [(i, i + 1) for i in range(ends)])
    from_right = lax.ppermute(pack(heads), "gx", [(i + 1, i) for i in range(ends)])
    out = []
    offset = 0
    for (a, dim), h in zip(parts, heads):
        size = h.size
        left = from_left[offset : offset + size].reshape(h.shape)
        right = from_right[offset : offset + size].reshape(h.shape)
        offset += size
        out.append(jnp.concatenate([left, a, right], axis=dim))
    return out


def block_mean(field, factor):
    lead = field.shape[:-2]
    rows, cols = (field.shape[-2], field.shape[-1])
    shaped = field.reshape(lead + (rows // factor, factor, cols // factor, factor))
    return shaped.mean(axis=(-3, -1))


def reaction_field(friction, ice_mask, layers):
    open_water = (ice_mask == 0).astype(jnp.float32)
    grounded = (ice_mask == 2).astype(jnp.float32)
    bottom = (jnp.arange(layers) == 0).astype(jnp.float32).reshape(layers, 1, 1)
    return 0.02 + 2.0 * open_water[None] + bottom * (grounded * friction)[None]


def build_operator(eta_level, react_level, level_index):
    scale = horizontal_scale / 4.0**level_index
    weight_x = jnp.array([4.0, 1.0], jnp.float32).reshape(2, 1, 1, 1) * scale
    weight_y = jnp.array([1.0, 4.0], jnp.float32).reshape(2, 1, 1, 1) * scale
    inner = eta_level[:, 1:-1, :]
    face_x = weight_x * (0.5 * (eta_level[:, 1:, :] + eta_level[:, :-1, :]))[None]
    padded = jnp.pad(inner, ((0, 0), (0, 0), (1, 1)))
    face_y = weight_y * (0.5 * (padded[:, :, 1:] + padded[:, :, :-1]))[None]
    face_z = vertical_scale * 0.5 * (inner[1:] + inner[:-1])
    vertical = jnp.pad(face_z, ((1, 1), (0, 0), (0, 0)))
    diagonal = face_x[:, :, 1:] + face_x[:, :, :-1] + face_y[..., 1:] + face_y[..., :-1]
    diagonal = diagonal + (vertical[1:] + vertical[:-1] + react_level)[None]
    layers = diagonal.shape[1]
    inverses = []
    ratios = []
    for layer in range(layers):
        pivot = diagonal[:, layer]
        if layer > 0:
            pivot = pivot - face_z[layer - 1] * ratios[-1]
        inverse = 1.0 / pivot
        inverses.append(inverse)
        if layer < layers - 1:
            ratios.append(face_z[layer] * inverse)
    return (face_x, face_y, face_z, react_level, jnp.stack(inverses, 1), jnp.stack(ratios, 1))


def lane_ops(operator):
    face_x, face_y, face_z, react_level, inverses, ratios = operator
    return (face_x[:, :, :-1], face_x[:, :, 1:], face_y[..., :-1], face_y[..., 1:], face_z, react_level, inverses, ratios)


def sweep_kernel(w_ref, b_ref, fxl_ref, fxr_ref, fyl_ref, fyr_ref, fz_ref, re_ref, inv_ref, rat_ref, mask_ref, out_ref,
                 *, rows, cut_w, cut_b, cut_op, mode):
    relax(w_ref, b_ref, (fxl_ref, fxr_ref, fyl_ref, fyr_ref, fz_ref, re_ref, inv_ref, rat_ref), mask_ref, out_ref,
          rows=rows, cut_w=cut_w, cut_b=cut_b, cut_op=cut_op, mode=mode)


def coarse_kernel(b_ref, fxl_ref, fxr_ref, fyl_ref, fyr_ref, fz_ref, re_ref, inv_ref, rat_ref, mask_ref, out_ref, w_ref,
                  *, rows, turns):
    lanes = (fxl_ref, fxr_ref, fyl_ref, fyr_ref, fz_ref, re_ref, inv_ref, rat_ref)
    w_ref[...] = jnp.zeros(w_ref.shape, jnp.float32)
    for turn in range(turns):
        relax(w_ref, b_ref, lanes, mask_ref, out_ref, rows=rows, cut_w=7, cut_b=0, cut_op=0, mode="sweep")
        if turn < turns - 1:
            for k in range(out_ref.shape[1]):
                w_ref[0, k, pl.ds(8, rows), :] = out_ref[0, k]


def relax(w_ref, b_ref, lanes, mask_ref, out_ref, *, rows, cut_w, cut_b, cut_op, mode):
    fxl_ref, fxr_ref, fyl_ref, fyr_ref, fz_ref, re_ref, inv_ref, rat_ref = lanes
    layers = out_ref.shape[1]
    cols = out_ref.shape[3]
    lane = lax.broadcasted_iota(jnp.int32, (rows, cols), 1)
    probe = pltpu.roll(lane, 1, 1)
    forward_roll = probe == jnp.where(lane == 0, cols - 1, lane - 1)
    first_col = lane == 0
    last_col = lane == cols - 1

    def cell(ref, k, cut):
        return ref[0, k, pl.ds(cut, rows), :]

    def field(k):
        return w_ref[0, k, pl.ds(cut_w + 1, rows), :]

    def applied(k):
        w = field(k)
        west = w_ref[0, k, pl.ds(cut_w, rows), :]
        east = w_ref[0, k, pl.ds(cut_w + 2, rows), :]
        result = -(cell(fxr_ref, k, cut_op) * (east - w) - cell(fxl_ref, k, cut_op) * (w - west))
        ahead = pltpu.roll(w, 1, 1)
        behind = pltpu.roll(w, cols - 1, 1)
        south = jnp.where(forward_roll, ahead, behind)
        north = jnp.where(forward_roll, behind, ahead)
        south = jnp.where(first_col, 0.0, south)
        north = jnp.where(last_col, 0.0, north)
        result = result - (cell(fyr_ref, k, cut_op) * (north - w) - cell(fyl_ref, k, cut_op) * (w - south))
        up = fz_ref[k, pl.ds(cut_op, rows), :] * (field(k + 1) - w) if k < layers - 1 else 0.0
        down = fz_ref[k - 1, pl.ds(cut_op, rows), :] * (w - field(k - 1)) if k > 0 else 0.0
        result = result - (up - down)
        return result + re_ref[k, pl.ds(cut_op, rows), :] * w

    if mode == "residual":
        for k in range(layers):
            out_ref[0, k] = cell(b_ref, k, cut_b) - applied(k)
        return
    keep = mask_ref[...] > 0.5
    previous = None
    for k in range(layers):
        residual = cell(b_ref, k, cut_b)
        if mode == "sweep":
            residual = residual - applied(k)
        if k == 0:
            forward = residual * cell(inv_ref, 0, cut_op)
        else:
            forward = (residual + fz_ref[k - 1, pl.ds(cut_op, rows), :] * previous) * cell(inv_ref, k, cut_op)
        out_ref[0, k] = forward
        previous = forward
    back = previous
    for k in range(layers - 1, -1, -1):
        if k < layers - 1:
            back = out_ref[0, k] + rat_ref[0, k, pl.ds(cut_op, rows), :] * back
        if mode == "sweep":
            value = field(k) + relax_weight * back
        else:
            value = relax_weight * back
        out_ref[0, k] = jnp.where(keep, value, 0.0)


def kernel_sweep(field_rim, target, lanes, cut_b, cut_op, mask, mode="sweep", cut_w=0, rows=None):
    parts, layers, rows_rim, cols = field_rim.shape
    rows = rows_rim - 2 if rows is None else rows
    fxl, fxr, fyl, fyr, fz, re, inv, rat = lanes
    per_part = lambda a: pl.BlockSpec((1,) + a.shape[1:], lambda c: (c,) + (0,) * (a.ndim - 1))
    whole = lambda a: pl.BlockSpec(a.shape, lambda c: (0,) * a.ndim)
    operands = [field_rim, target, fxl, fxr, fyl, fyr, fz, re, inv, rat, mask]
    specs = [per_part(field_rim), per_part(target), per_part(fxl), per_part(fxr), per_part(fyl), per_part(fyr),
             whole(fz), whole(re), per_part(inv), per_part(rat), whole(mask)]
    body = functools.partial(sweep_kernel, rows=rows, cut_w=cut_w, cut_b=cut_b, cut_op=cut_op, mode=mode)
    return pl.pallas_call(
        body,
        grid=(parts,),
        in_specs=specs,
        out_specs=pl.BlockSpec((1, layers, rows, cols), lambda c: (c, 0, 0, 0)),
        out_shape=jax.ShapeDtypeStruct((parts, layers, rows, cols), jnp.float32),
    )(*operands)


def build_kernel(eta_ref, re_ref, fxl_ref, fxr_ref, fyl_ref, fyr_ref, fz_ref, reo_ref, inv_ref, rat_ref,
                 *, rows, cut_re, scale):
    component = pl.program_id(0)
    layers = eta_ref.shape[0]
    cols = eta_ref.shape[2]
    lane = lax.broadcasted_iota(jnp.int32, (rows, cols), 1)
    probe = pltpu.roll(lane, 1, 1)
    forward_roll = probe == jnp.where(lane == 0, cols - 1, lane - 1)
    first_col = lane == 0
    last_col = lane == cols - 1
    weight_x = jnp.where(component == 0, 4.0, 1.0) * scale
    weight_y = jnp.where(component == 0, 1.0, 4.0) * scale

    def inner(k):
        return eta_ref[k, pl.ds(1, rows), :]

    faces_z = [vertical_scale * 0.5 * (inner(k + 1) + inner(k)) for k in range(layers - 1)]
    ratio = None
    for k in range(layers):
        middle = inner(k)
        west = eta_ref[k, pl.ds(0, rows), :]
        east = eta_ref[k, pl.ds(2, rows), :]
        ahead = pltpu.roll(middle, 1, 1)
        behind = pltpu.roll(middle, cols - 1, 1)
        south = jnp.where(first_col, 0.0, jnp.where(forward_roll, ahead, behind))
        north = jnp.where(last_col, 0.0, jnp.where(forward_roll, behind, ahead))
        face_w = weight_x * (0.5 * (middle + west))
        face_e = weight_x * (0.5 * (east + middle))
        face_s = weight_y * (0.5 * (middle + south))
        face_n = weight_y * (0.5 * (north + middle))
        react = re_ref[min(k, re_ref.shape[0] - 1), pl.ds(cut_re, rows), :]
        up = faces_z[k] if k < layers - 1 else 0.0
        down = faces_z[k - 1] if k > 0 else 0.0
        diagonal = face_e + face_w + face_n + face_s
        diagonal = diagonal + (up + down + react)
        if k > 0:
            diagonal = diagonal - faces_z[k - 1] * ratio
        inverse = 1.0 / diagonal
        fxl_ref[0, k] = face_w
        fxr_ref[0, k] = face_e
        fyl_ref[0, k] = face_s
        fyr_ref[0, k] = face_n
        reo_ref[k] = react
        inv_ref[0, k] = inverse
        if k < layers - 1:
            ratio = faces_z[k] * inverse
            fz_ref[k] = faces_z[k]
            rat_ref[0, k] = ratio


def kernel_operator(eta_level, react_level, level_index, cut_re=0):
    layers, rows_eta, cols = eta_level.shape
    rows = rows_eta - 2
    whole = lambda a: pl.BlockSpec(a.shape, lambda c: (0,) * a.ndim)
    per_part = lambda shape: pl.BlockSpec((1,) + shape, lambda c: (c,) + (0,) * len(shape))
    cell = (layers, rows, cols)
    faces = (layers - 1, rows, cols)
    body = functools.partial(build_kernel, rows=rows, cut_re=cut_re, scale=horizontal_scale / 4.0**level_index)
    shapes = [(2,) + cell] * 4 + [faces, cell, (2,) + cell, (2,) + faces]
    specs = [per_part(cell)] * 4 + [
        pl.BlockSpec(faces, lambda c: (0, 0, 0)),
        pl.BlockSpec(cell, lambda c: (0, 0, 0)),
        per_part(cell),
        per_part(faces),
    ]
    return tuple(
        pl.pallas_call(
            body,
            grid=(2,),
            in_specs=[whole(eta_level), whole(react_level)],
            out_specs=specs,
            out_shape=[jax.ShapeDtypeStruct(s, jnp.float32) for s in shapes],
        )(eta_level, react_level)
    )


def kernel_coarse(target, lanes, mask, turns):
    parts, layers, rows, cols = target.shape
    fxl, fxr, fyl, fyr, fz, re, inv, rat = lanes
    per_part = lambda a: pl.BlockSpec((1,) + a.shape[1:], lambda c: (c,) + (0,) * (a.ndim - 1))
    whole = lambda a: pl.BlockSpec(a.shape, lambda c: (0,) * a.ndim)
    operands = [target, fxl, fxr, fyl, fyr, fz, re, inv, rat, mask]
    specs = [per_part(target), per_part(fxl), per_part(fxr), per_part(fyl), per_part(fyr),
             whole(fz), whole(re), per_part(inv), per_part(rat), whole(mask)]
    body = functools.partial(coarse_kernel, rows=rows, turns=turns)
    return pl.pallas_call(
        body,
        grid=(parts,),
        in_specs=specs,
        out_specs=pl.BlockSpec((1, layers, rows, cols), lambda c: (c, 0, 0, 0)),
        out_shape=jax.ShapeDtypeStruct((parts, layers, rows, cols), jnp.float32),
        scratch_shapes=[pltpu.VMEM((1, layers, rows + 16, cols), jnp.float32)],
    )(*operands)


def rows_inside(cells, halo, extent, cols):
    return jnp.broadcast_to(inside(cells, halo, extent)[0, 0], (extent, cols)).astype(jnp.float32)


def shrink(operator, cut):
    if cut == 0:
        return operator
    face_x, face_y, face_z, react_level, inverses, ratios = operator
    rows = face_y.shape[2]
    return (
        face_x[:, :, cut : rows + 1 - cut],
        face_y[:, :, cut : rows - cut],
        face_z[:, cut : rows - cut],
        react_level[:, cut : rows - cut],
        inverses[:, :, cut : rows - cut],
        ratios[:, :, cut : rows - cut],
    )


def apply_operator(field_rim, operator):
    face_x, face_y, face_z, react_level, inverses, ratios = operator
    field = field_rim[:, :, 1:-1, :]
    flux_x = face_x * (field_rim[:, :, 1:, :] - field_rim[:, :, :-1, :])
    result = -(flux_x[:, :, 1:] - flux_x[:, :, :-1])
    padded = jnp.pad(field, ((0, 0), (0, 0), (0, 0), (1, 1)))
    flux_y = face_y * (padded[..., 1:] - padded[..., :-1])
    result = result - (flux_y[..., 1:] - flux_y[..., :-1])
    flux_z = face_z[None] * (field[:, 1:] - field[:, :-1])
    flux_z = jnp.pad(flux_z, ((0, 0), (1, 1), (0, 0), (0, 0)))
    result = result - (flux_z[:, 1:] - flux_z[:, :-1])
    return result + react_level[None] * field


def line_solve(residual, operator):
    face_z, inverses, ratios = (operator[2], operator[4], operator[5])
    layers = residual.shape[1]
    forward = [residual[:, 0] * inverses[:, 0]]
    for layer in range(1, layers):
        forward.append((residual[:, layer] + face_z[layer - 1] * forward[-1]) * inverses[:, layer])
    backward = [forward[-1]]
    for layer in range(layers - 2, -1, -1):
        backward.append(forward[layer] + ratios[:, layer] * backward[-1])
    return jnp.stack(backward[::-1], 1)


def sweep(field_rim, target, operator):
    field = field_rim[:, :, 1:-1, :]
    return field + relax_weight * line_solve(target - apply_operator(field_rim, operator), operator)


def restrict(field):
    return block_mean(field, 2)


def prolong(field):
    return jnp.repeat(jnp.repeat(field, 2, axis=2), 2, axis=3)


def pad_rim(field):
    return jnp.pad(field, ((0, 0), (0, 0), (1, 1), (0, 0)))


def inside(cells, halo, extent):
    count = lax.axis_size("gx")
    first = lax.axis_index("gx") * cells - halo
    index = first + jnp.arange(extent)
    return ((index >= 0) & (index < count * cells)).reshape(1, 1, extent, 1)


def keep_inside(field, cells, halo):
    return jnp.where(inside(cells, halo, field.shape[2]), field, 0.0)


def window(full, dim, start, size, pad):
    widths = [(0, 0)] * full.ndim
    widths[dim] = (pad, pad)
    return lax.dynamic_slice_in_dim(jnp.pad(full, widths), start, size, axis=dim)


def nearby(cells, dim, hops):
    count = lax.axis_size("gx")
    lows = []
    highs = []
    for step in range(1, hops + 1):
        lows.insert(0, lax.ppermute(cells, "gx", [(i, i + step) for i in range(count - step)]))
        highs.append(lax.ppermute(cells, "gx", [(i + step, i) for i in range(count - step)]))
    return jnp.concatenate(lows + [cells] + highs, axis=dim)


def shards(misfit, adjoint_guess, viscosity, friction, ice_mask, forward_bed):
    layers, cells, cols = viscosity.shape
    where = lax.axis_index("gx")
    react_fine = reaction_field(friction, ice_mask, layers)
    react_pair = react_fine[:2]

    eta_1 = block_mean(viscosity, 2)
    eta_2 = block_mean(viscosity, 4)
    react_1 = block_mean(react_pair, 2)
    react_2 = block_mean(react_pair, 4)
    pieces = [eta_1, react_1, eta_2, react_2]
    packed = jnp.concatenate([p.reshape(-1) for p in pieces])
    gathered = lax.all_gather(packed[None], "gx", axis=0, tiled=True)
    count = gathered.shape[0]
    unpacked = []
    offset = 0
    for p in pieces:
        block = gathered[:, offset : offset + p.size].reshape((count,) + p.shape)
        offset += p.size
        unpacked.append(jnp.moveaxis(block, 0, 1).reshape((p.shape[0], count * p.shape[1], p.shape[2])))
    eta_1_all, react_1_all, eta_2_all, react_2_all = unpacked

    halo = 4
    eta_wide, guess_wide, misfit_wide, react_wide = trade(
        [(viscosity, 1), (adjoint_guess, 2), (misfit, 2), (react_pair, 1)], halo
    )
    op_0 = kernel_operator(eta_wide, react_wide, 0, 1)
    fine = kernel_sweep(guess_wide, misfit_wide, op_0, 1, 0, rows_inside(cells, 3, cells + 6, cols))
    fine = kernel_sweep(fine, misfit_wide, op_0, 2, 1, rows_inside(cells, 2, cells + 4, cols))
    residual = kernel_sweep(fine, misfit_wide, op_0, 4, 3, rows_inside(cells, 0, cells, cols), "residual", 1, cells)
    middle_rhs = restrict(residual)

    half = cells // 2
    wide = cols // 2
    rhs_wide = with_halo(middle_rhs, (("gx", 2),), half)
    eta_1_wide = window(eta_1_all, 1, where * half, 3 * half + 2, half + 1)
    react_1_wide = window(react_1_all, 1, where * half, 3 * half, half)
    op_1 = kernel_operator(eta_1_wide, react_1_wide, 1)
    middle = kernel_sweep(rhs_wide, rhs_wide, op_1, 0, 0, rows_inside(half, half, 3 * half, wide), "zero", 0, 3 * half)
    middle = kernel_sweep(middle, rhs_wide, op_1, 1, 1, rows_inside(half, half - 1, 3 * half - 2, wide))
    residual = kernel_sweep(middle, rhs_wide, op_1, half, half, rows_inside(half, 0, half, wide), "residual", half - 2, half)
    coarse_rhs = restrict(residual)

    quarter = cells // 4
    narrow = cols // 4
    reach = 3
    span = reach + COARSE_SWEEPS - 1
    coarse_rhs_near = nearby(coarse_rhs, 2, span // quarter)
    eta_2_near = window(eta_2_all, 1, where * quarter, quarter + 2 * span + 2, span + 1)
    react_2_near = window(react_2_all, 1, where * quarter, quarter + 2 * span, span)
    op_2 = kernel_operator(eta_2_near, react_2_near, 2)
    extent = quarter + 2 * span
    coarse_mask = rows_inside(quarter, span, extent, narrow)
    coarse = kernel_coarse(coarse_rhs_near, op_2, coarse_mask, COARSE_SWEEPS)
    coarse_near = coarse[:, :, span - reach : span + quarter + reach]

    lift = prolong(coarse_near)
    trim = 2 * reach - (half - 1)
    middle = middle + lift[:, :, trim : lift.shape[2] - trim]
    middle = kernel_sweep(middle, rhs_wide, op_1, 2, 2, rows_inside(half, half - 2, 3 * half - 4, wide))
    middle = kernel_sweep(middle, rhs_wide, op_1, 3, 3, rows_inside(half, half - 3, 3 * half - 6, wide))
    fine = fine + prolong(middle)
    fine = kernel_sweep(fine, misfit_wide, op_0, 3, 2, rows_inside(cells, 1, cells + 2, cols))
    fine = kernel_sweep(fine, misfit_wide, op_0, 4, 3, rows_inside(cells, 0, cells, cols))
    grounded = (ice_mask == 2).astype(jnp.float32)
    gradient = -grounded * (forward_bed[0] * fine[0, 0] + forward_bed[1] * fine[1, 0])
    return (fine, gradient)


def solution(mesh):
    placed = (
        P("ens", None, "gx", None),
        P("ens", None, "gx", None),
        P("ens", "gx", None),
        P("gx", "ens"),
        P("gx", "ens"),
        P("ens", "gx", None),
    )
    return jax.shard_map(
        shards,
        mesh=mesh,
        in_specs=placed,
        out_specs=(P("ens", None, "gx", None), P("gx", "ens")),
        check_vma=False,
    )
```

```python
import functools

import jax
import jax.numpy as jnp
from jax import lax
from jax.experimental import pallas as pl
from jax.experimental.pallas import tpu as pltpu
from jax.sharding import PartitionSpec as P

NU = 2
COARSE_SWEEPS = 6


horizontal_scale = 1.0
vertical_scale = 4.0
relax_weight = 0.8


def with_halo(cells, sides, width):
    for axis, dim in sides:
        count = lax.axis_size(axis)
        ends = count - 1
        head = lax.slice_in_dim(cells, 0, width, axis=dim)
        tail = lax.slice_in_dim(cells, cells.shape[dim] - width, cells.shape[dim], axis=dim)
        cells = jnp.concatenate(
            [
                lax.ppermute(tail, axis, [(i, (i + 1) % count) for i in range(ends)]),
                cells,
                lax.ppermute(head, axis, [((i + 1) % count, i) for i in range(ends)]),
            ],
            axis=dim,
        )
    return cells


def trade(parts, width):
    count = lax.axis_size("gx")
    ends = count - 1
    heads = [lax.slice_in_dim(a, 0, width, axis=dim) for a, dim in parts]
    tails = [lax.slice_in_dim(a, a.shape[dim] - width, a.shape[dim], axis=dim) for a, dim in parts]
    pack = lambda pieces: jnp.concatenate([p.reshape(-1) for p in pieces])
    from_left = lax.ppermute(pack(tails), "gx", [(i, i + 1) for i in range(ends)])
    from_right = lax.ppermute(pack(heads), "gx", [(i + 1, i) for i in range(ends)])
    out = []
    offset = 0
    for (a, dim), h in zip(parts, heads):
        size = h.size
        left = from_left[offset : offset + size].reshape(h.shape)
        right = from_right[offset : offset + size].reshape(h.shape)
        offset += size
        out.append(jnp.concatenate([left, a, right], axis=dim))
    return out


def block_mean(field, factor):
    lead = field.shape[:-2]
    rows, cols = (field.shape[-2], field.shape[-1])
    shaped = field.reshape(lead + (rows // factor, factor, cols // factor, factor))
    return shaped.mean(axis=(-3, -1))


def reaction_field(friction, ice_mask, layers):
    open_water = (ice_mask == 0).astype(jnp.float32)
    grounded = (ice_mask == 2).astype(jnp.float32)
    bottom = (jnp.arange(layers) == 0).astype(jnp.float32).reshape(layers, 1, 1)
    return 0.02 + 2.0 * open_water[None] + bottom * (grounded * friction)[None]


def build_operator(eta_level, react_level, level_index):
    scale = horizontal_scale / 4.0**level_index
    weight_x = jnp.array([4.0, 1.0], jnp.float32).reshape(2, 1, 1, 1) * scale
    weight_y = jnp.array([1.0, 4.0], jnp.float32).reshape(2, 1, 1, 1) * scale
    inner = eta_level[:, 1:-1, :]
    face_x = weight_x * (0.5 * (eta_level[:, 1:, :] + eta_level[:, :-1, :]))[None]
    padded = jnp.pad(inner, ((0, 0), (0, 0), (1, 1)))
    face_y = weight_y * (0.5 * (padded[:, :, 1:] + padded[:, :, :-1]))[None]
    face_z = vertical_scale * 0.5 * (inner[1:] + inner[:-1])
    vertical = jnp.pad(face_z, ((1, 1), (0, 0), (0, 0)))
    diagonal = face_x[:, :, 1:] + face_x[:, :, :-1] + face_y[..., 1:] + face_y[..., :-1]
    diagonal = diagonal + (vertical[1:] + vertical[:-1] + react_level)[None]
    layers = diagonal.shape[1]
    inverses = []
    ratios = []
    for layer in range(layers):
        pivot = diagonal[:, layer]
        if layer > 0:
            pivot = pivot - face_z[layer - 1] * ratios[-1]
        inverse = 1.0 / pivot
        inverses.append(inverse)
        if layer < layers - 1:
            ratios.append(face_z[layer] * inverse)
    return (face_x, face_y, face_z, react_level, jnp.stack(inverses, 1), jnp.stack(ratios, 1))


def lane_ops(operator):
    face_x, face_y, face_z, react_level, inverses, ratios = operator
    return (face_x[:, :, :-1], face_x[:, :, 1:], face_y[..., :-1], face_y[..., 1:], face_z, react_level, inverses, ratios)


def sweep_kernel(w_ref, b_ref, fxl_ref, fxr_ref, fyl_ref, fyr_ref, fz_ref, re_ref, inv_ref, rat_ref, mask_ref, out_ref,
                 *, rows, cut_w, cut_b, cut_op, mode):
    relax(w_ref, b_ref, (fxl_ref, fxr_ref, fyl_ref, fyr_ref, fz_ref, re_ref, inv_ref, rat_ref), mask_ref, out_ref,
          rows=rows, cut_w=cut_w, cut_b=cut_b, cut_op=cut_op, mode=mode)


def coarse_kernel(b_ref, fxl_ref, fxr_ref, fyl_ref, fyr_ref, fz_ref, re_ref, inv_ref, rat_ref, mask_ref, out_ref, w_ref,
                  *, rows, turns):
    lanes = (fxl_ref, fxr_ref, fyl_ref, fyr_ref, fz_ref, re_ref, inv_ref, rat_ref)
    w_ref[...] = jnp.zeros(w_ref.shape, jnp.float32)
    for turn in range(turns):
        relax(w_ref, b_ref, lanes, mask_ref, out_ref, rows=rows, cut_w=7, cut_b=0, cut_op=0, mode="sweep")
        if turn < turns - 1:
            for k in range(out_ref.shape[1]):
                w_ref[0, k, pl.ds(8, rows), :] = out_ref[0, k]


def relax(w_ref, b_ref, lanes, mask_ref, out_ref, *, rows, cut_w, cut_b, cut_op, mode):
    fxl_ref, fxr_ref, fyl_ref, fyr_ref, fz_ref, re_ref, inv_ref, rat_ref = lanes
    layers = out_ref.shape[1]
    cols = out_ref.shape[3]
    lane = lax.broadcasted_iota(jnp.int32, (rows, cols), 1)
    probe = pltpu.roll(lane, 1, 1)
    forward_roll = probe == jnp.where(lane == 0, cols - 1, lane - 1)
    first_col = lane == 0
    last_col = lane == cols - 1

    def cell(ref, k, cut):
        return ref[0, k, pl.ds(cut, rows), :]

    def field(k):
        return w_ref[0, k, pl.ds(cut_w + 1, rows), :]

    def applied(k):
        w = field(k)
        west = w_ref[0, k, pl.ds(cut_w, rows), :]
        east = w_ref[0, k, pl.ds(cut_w + 2, rows), :]
        result = -(cell(fxr_ref, k, cut_op) * (east - w) - cell(fxl_ref, k, cut_op) * (w - west))
        ahead = pltpu.roll(w, 1, 1)
        behind = pltpu.roll(w, cols - 1, 1)
        south = jnp.where(forward_roll, ahead, behind)
        north = jnp.where(forward_roll, behind, ahead)
        south = jnp.where(first_col, 0.0, south)
        north = jnp.where(last_col, 0.0, north)
        result = result - (cell(fyr_ref, k, cut_op) * (north - w) - cell(fyl_ref, k, cut_op) * (w - south))
        up = fz_ref[k, pl.ds(cut_op, rows), :] * (field(k + 1) - w) if k < layers - 1 else 0.0
        down = fz_ref[k - 1, pl.ds(cut_op, rows), :] * (w - field(k - 1)) if k > 0 else 0.0
        result = result - (up - down)
        return result + re_ref[k, pl.ds(cut_op, rows), :] * w

    if mode == "residual":
        for k in range(layers):
            out_ref[0, k] = cell(b_ref, k, cut_b) - applied(k)
        return
    keep = mask_ref[...] > 0.5
    previous = None
    for k in range(layers):
        residual = cell(b_ref, k, cut_b)
        if mode == "sweep":
            residual = residual - applied(k)
        if k == 0:
            forward = residual * cell(inv_ref, 0, cut_op)
        else:
            forward = (residual + fz_ref[k - 1, pl.ds(cut_op, rows), :] * previous) * cell(inv_ref, k, cut_op)
        out_ref[0, k] = forward
        previous = forward
    back = previous
    for k in range(layers - 1, -1, -1):
        if k < layers - 1:
            back = out_ref[0, k] + rat_ref[0, k, pl.ds(cut_op, rows), :] * back
        if mode == "sweep":
            value = field(k) + relax_weight * back
        else:
            value = relax_weight * back
        out_ref[0, k] = jnp.where(keep, value, 0.0)


def kernel_sweep(field_rim, target, lanes, cut_b, cut_op, mask, mode="sweep", cut_w=0, rows=None):
    parts, layers, rows_rim, cols = field_rim.shape
    rows = rows_rim - 2 if rows is None else rows
    fxl, fxr, fyl, fyr, fz, re, inv, rat = lanes
    per_part = lambda a: pl.BlockSpec((1,) + a.shape[1:], lambda c: (c,) + (0,) * (a.ndim - 1))
    whole = lambda a: pl.BlockSpec(a.shape, lambda c: (0,) * a.ndim)
    operands = [field_rim, target, fxl, fxr, fyl, fyr, fz, re, inv, rat, mask]
    specs = [per_part(field_rim), per_part(target), per_part(fxl), per_part(fxr), per_part(fyl), per_part(fyr),
             whole(fz), whole(re), per_part(inv), per_part(rat), whole(mask)]
    body = functools.partial(sweep_kernel, rows=rows, cut_w=cut_w, cut_b=cut_b, cut_op=cut_op, mode=mode)
    return pl.pallas_call(
        body,
        grid=(parts,),
        in_specs=specs,
        out_specs=pl.BlockSpec((1, layers, rows, cols), lambda c: (c, 0, 0, 0)),
        out_shape=jax.ShapeDtypeStruct((parts, layers, rows, cols), jnp.float32),
    )(*operands)


def build_kernel(eta_ref, re_ref, fxl_ref, fxr_ref, fyl_ref, fyr_ref, fz_ref, reo_ref, inv_ref, rat_ref,
                 *, rows, cut_re, scale):
    component = pl.program_id(0)
    layers = eta_ref.shape[0]
    cols = eta_ref.shape[2]
    lane = lax.broadcasted_iota(jnp.int32, (rows, cols), 1)
    probe = pltpu.roll(lane, 1, 1)
    forward_roll = probe == jnp.where(lane == 0, cols - 1, lane - 1)
    first_col = lane == 0
    last_col = lane == cols - 1
    weight_x = jnp.where(component == 0, 4.0, 1.0) * scale
    weight_y = jnp.where(component == 0, 1.0, 4.0) * scale

    def inner(k):
        return eta_ref[k, pl.ds(1, rows), :]

    faces_z = [vertical_scale * 0.5 * (inner(k + 1) + inner(k)) for k in range(layers - 1)]
    ratio = None
    for k in range(layers):
        middle = inner(k)
        west = eta_ref[k, pl.ds(0, rows), :]
        east = eta_ref[k, pl.ds(2, rows), :]
        ahead = pltpu.roll(middle, 1, 1)
        behind = pltpu.roll(middle, cols - 1, 1)
        south = jnp.where(first_col, 0.0, jnp.where(forward_roll, ahead, behind))
        north = jnp.where(last_col, 0.0, jnp.where(forward_roll, behind, ahead))
        face_w = weight_x * (0.5 * (middle + west))
        face_e = weight_x * (0.5 * (east + middle))
        face_s = weight_y * (0.5 * (middle + south))
        face_n = weight_y * (0.5 * (north + middle))
        react = re_ref[min(k, re_ref.shape[0] - 1), pl.ds(cut_re, rows), :]
        up = faces_z[k] if k < layers - 1 else 0.0
        down = faces_z[k - 1] if k > 0 else 0.0
        diagonal = face_e + face_w + face_n + face_s
        diagonal = diagonal + (up + down + react)
        if k > 0:
            diagonal = diagonal - faces_z[k - 1] * ratio
        inverse = 1.0 / diagonal
        fxl_ref[0, k] = face_w
        fxr_ref[0, k] = face_e
        fyl_ref[0, k] = face_s
        fyr_ref[0, k] = face_n
        reo_ref[k] = react
        inv_ref[0, k] = inverse
        if k < layers - 1:
            ratio = faces_z[k] * inverse
            fz_ref[k] = faces_z[k]
            rat_ref[0, k] = ratio


def kernel_operator(eta_level, react_level, level_index, cut_re=0):
    layers, rows_eta, cols = eta_level.shape
    rows = rows_eta - 2
    whole = lambda a: pl.BlockSpec(a.shape, lambda c: (0,) * a.ndim)
    per_part = lambda shape: pl.BlockSpec((1,) + shape, lambda c: (c,) + (0,) * len(shape))
    cell = (layers, rows, cols)
    faces = (layers - 1, rows, cols)
    body = functools.partial(build_kernel, rows=rows, cut_re=cut_re, scale=horizontal_scale / 4.0**level_index)
    shapes = [(2,) + cell] * 4 + [faces, cell, (2,) + cell, (2,) + faces]
    specs = [per_part(cell)] * 4 + [
        pl.BlockSpec(faces, lambda c: (0, 0, 0)),
        pl.BlockSpec(cell, lambda c: (0, 0, 0)),
        per_part(cell),
        per_part(faces),
    ]
    return tuple(
        pl.pallas_call(
            body,
            grid=(2,),
            in_specs=[whole(eta_level), whole(react_level)],
            out_specs=specs,
            out_shape=[jax.ShapeDtypeStruct(s, jnp.float32) for s in shapes],
        )(eta_level, react_level)
    )


def kernel_coarse(target, lanes, mask, turns):
    parts, layers, rows, cols = target.shape
    fxl, fxr, fyl, fyr, fz, re, inv, rat = lanes
    per_part = lambda a: pl.BlockSpec((1,) + a.shape[1:], lambda c: (c,) + (0,) * (a.ndim - 1))
    whole = lambda a: pl.BlockSpec(a.shape, lambda c: (0,) * a.ndim)
    operands = [target, fxl, fxr, fyl, fyr, fz, re, inv, rat, mask]
    specs = [per_part(target), per_part(fxl), per_part(fxr), per_part(fyl), per_part(fyr),
             whole(fz), whole(re), per_part(inv), per_part(rat), whole(mask)]
    body = functools.partial(coarse_kernel, rows=rows, turns=turns)
    return pl.pallas_call(
        body,
        grid=(parts,),
        in_specs=specs,
        out_specs=pl.BlockSpec((1, layers, rows, cols), lambda c: (c, 0, 0, 0)),
        out_shape=jax.ShapeDtypeStruct((parts, layers, rows, cols), jnp.float32),
        scratch_shapes=[pltpu.VMEM((1, layers, rows + 16, cols), jnp.float32)],
    )(*operands)


def rows_inside(cells, halo, extent, cols):
    return jnp.broadcast_to(inside(cells, halo, extent)[0, 0], (extent, cols)).astype(jnp.float32)


def shrink(operator, cut):
    if cut == 0:
        return operator
    face_x, face_y, face_z, react_level, inverses, ratios = operator
    rows = face_y.shape[2]
    return (
        face_x[:, :, cut : rows + 1 - cut],
        face_y[:, :, cut : rows - cut],
        face_z[:, cut : rows - cut],
        react_level[:, cut : rows - cut],
        inverses[:, :, cut : rows - cut],
        ratios[:, :, cut : rows - cut],
    )


def apply_operator(field_rim, operator):
    face_x, face_y, face_z, react_level, inverses, ratios = operator
    field = field_rim[:, :, 1:-1, :]
    flux_x = face_x * (field_rim[:, :, 1:, :] - field_rim[:, :, :-1, :])
    result = -(flux_x[:, :, 1:] - flux_x[:, :, :-1])
    padded = jnp.pad(field, ((0, 0), (0, 0), (0, 0), (1, 1)))
    flux_y = face_y * (padded[..., 1:] - padded[..., :-1])
    result = result - (flux_y[..., 1:] - flux_y[..., :-1])
    flux_z = face_z[None] * (field[:, 1:] - field[:, :-1])
    flux_z = jnp.pad(flux_z, ((0, 0), (1, 1), (0, 0), (0, 0)))
    result = result - (flux_z[:, 1:] - flux_z[:, :-1])
    return result + react_level[None] * field


def line_solve(residual, operator):
    face_z, inverses, ratios = (operator[2], operator[4], operator[5])
    layers = residual.shape[1]
    forward = [residual[:, 0] * inverses[:, 0]]
    for layer in range(1, layers):
        forward.append((residual[:, layer] + face_z[layer - 1] * forward[-1]) * inverses[:, layer])
    backward = [forward[-1]]
    for layer in range(layers - 2, -1, -1):
        backward.append(forward[layer] + ratios[:, layer] * backward[-1])
    return jnp.stack(backward[::-1], 1)


def sweep(field_rim, target, operator):
    field = field_rim[:, :, 1:-1, :]
    return field + relax_weight * line_solve(target - apply_operator(field_rim, operator), operator)


def restrict(field):
    return block_mean(field, 2)


def prolong(field):
    cols = field.shape[3]
    spread = (jnp.arange(cols)[:, None] == jnp.arange(2 * cols)[None, :] // 2).astype(jnp.float32)
    wide = jnp.einsum("ckxy,yz->ckxz", field, spread, precision=lax.Precision.HIGHEST)
    return jnp.repeat(wide, 2, axis=2)


def pad_rim(field):
    return jnp.pad(field, ((0, 0), (0, 0), (1, 1), (0, 0)))


def inside(cells, halo, extent):
    count = lax.axis_size("gx")
    first = lax.axis_index("gx") * cells - halo
    index = first + jnp.arange(extent)
    return ((index >= 0) & (index < count * cells)).reshape(1, 1, extent, 1)


def keep_inside(field, cells, halo):
    return jnp.where(inside(cells, halo, field.shape[2]), field, 0.0)


def window(full, dim, start, size, pad):
    widths = [(0, 0)] * full.ndim
    widths[dim] = (pad, pad)
    return lax.dynamic_slice_in_dim(jnp.pad(full, widths), start, size, axis=dim)


def nearby(cells, dim, hops):
    count = lax.axis_size("gx")
    lows = []
    highs = []
    for step in range(1, hops + 1):
        lows.insert(0, lax.ppermute(cells, "gx", [(i, i + step) for i in range(count - step)]))
        highs.append(lax.ppermute(cells, "gx", [(i + step, i) for i in range(count - step)]))
    return jnp.concatenate(lows + [cells] + highs, axis=dim)


def shards(misfit, adjoint_guess, viscosity, friction, ice_mask, forward_bed):
    layers, cells, cols = viscosity.shape
    where = lax.axis_index("gx")
    react_fine = reaction_field(friction, ice_mask, layers)
    react_pair = react_fine[:2]

    eta_1 = block_mean(viscosity, 2)
    eta_2 = block_mean(viscosity, 4)
    react_1 = block_mean(react_pair, 2)
    react_2 = block_mean(react_pair, 4)
    pieces = [eta_1, react_1, eta_2, react_2]
    packed = jnp.concatenate([p.reshape(-1) for p in pieces])
    gathered = lax.all_gather(packed[None], "gx", axis=0, tiled=True)
    count = gathered.shape[0]
    unpacked = []
    offset = 0
    for p in pieces:
        block = gathered[:, offset : offset + p.size].reshape((count,) + p.shape)
        offset += p.size
        unpacked.append(jnp.moveaxis(block, 0, 1).reshape((p.shape[0], count * p.shape[1], p.shape[2])))
    eta_1_all, react_1_all, eta_2_all, react_2_all = unpacked

    halo = 4
    eta_wide, guess_wide, misfit_wide, react_wide = trade(
        [(viscosity, 1), (adjoint_guess, 2), (misfit, 2), (react_pair, 1)], halo
    )
    op_0 = kernel_operator(eta_wide, react_wide, 0, 1)
    fine = kernel_sweep(guess_wide, misfit_wide, op_0, 1, 0, rows_inside(cells, 3, cells + 6, cols))
    fine = kernel_sweep(fine, misfit_wide, op_0, 2, 1, rows_inside(cells, 2, cells + 4, cols))
    residual = kernel_sweep(fine, misfit_wide, op_0, 4, 3, rows_inside(cells, 0, cells, cols), "residual", 1, cells)
    middle_rhs = restrict(residual)

    half = cells // 2
    wide = cols // 2
    rhs_wide = with_halo(middle_rhs, (("gx", 2),), half)
    eta_1_wide = window(eta_1_all, 1, where * half, 3 * half + 2, half + 1)
    react_1_wide = window(react_1_all, 1, where * half, 3 * half, half)
    op_1 = kernel_operator(eta_1_wide, react_1_wide, 1)
    middle = kernel_sweep(rhs_wide, rhs_wide, op_1, 0, 0, rows_inside(half, half, 3 * half, wide), "zero", 0, 3 * half)
    middle = kernel_sweep(middle, rhs_wide, op_1, 1, 1, rows_inside(half, half - 1, 3 * half - 2, wide))
    residual = kernel_sweep(middle, rhs_wide, op_1, half, half, rows_inside(half, 0, half, wide), "residual", half - 2, half)
    coarse_rhs = restrict(residual)

    quarter = cells // 4
    narrow = cols // 4
    reach = 3
    span = reach + COARSE_SWEEPS - 1
    coarse_rhs_near = nearby(coarse_rhs, 2, span // quarter)
    eta_2_near = window(eta_2_all, 1, where * quarter, quarter + 2 * span + 2, span + 1)
    react_2_near = window(react_2_all, 1, where * quarter, quarter + 2 * span, span)
    op_2 = kernel_operator(eta_2_near, react_2_near, 2)
    extent = quarter + 2 * span
    coarse_mask = rows_inside(quarter, span, extent, narrow)
    coarse = kernel_coarse(coarse_rhs_near, op_2, coarse_mask, COARSE_SWEEPS)
    coarse_near = coarse[:, :, span - reach : span + quarter + reach]

    lift = prolong(coarse_near)
    trim = 2 * reach - (half - 1)
    middle = middle + lift[:, :, trim : lift.shape[2] - trim]
    middle = kernel_sweep(middle, rhs_wide, op_1, 2, 2, rows_inside(half, half - 2, 3 * half - 4, wide))
    middle = kernel_sweep(middle, rhs_wide, op_1, 3, 3, rows_inside(half, half - 3, 3 * half - 6, wide))
    fine = fine + prolong(middle)
    fine = kernel_sweep(fine, misfit_wide, op_0, 3, 2, rows_inside(cells, 1, cells + 2, cols))
    fine = kernel_sweep(fine, misfit_wide, op_0, 4, 3, rows_inside(cells, 0, cells, cols))
    grounded = (ice_mask == 2).astype(jnp.float32)
    gradient = -grounded * (forward_bed[0] * fine[0, 0] + forward_bed[1] * fine[1, 0])
    return (fine, gradient)


def solution(mesh):
    placed = (
        P("ens", None, "gx", None),
        P("ens", None, "gx", None),
        P("ens", "gx", None),
        P("gx", "ens"),
        P("gx", "ens"),
        P("ens", "gx", None),
    )
    return jax.shard_map(
        shards,
        mesh=mesh,
        in_specs=placed,
        out_specs=(P("ens", None, "gx", None), P("gx", "ens")),
        check_vma=False,
    )
```

```python
import functools

import jax
import jax.numpy as jnp
from jax import lax
from jax.experimental import pallas as pl
from jax.experimental.pallas import tpu as pltpu
from jax.sharding import PartitionSpec as P

NU = 2
COARSE_SWEEPS = 6


horizontal_scale = 1.0
vertical_scale = 4.0
relax_weight = 0.8


def with_halo(cells, sides, width):
    for axis, dim in sides:
        count = lax.axis_size(axis)
        ends = count - 1
        head = lax.slice_in_dim(cells, 0, width, axis=dim)
        tail = lax.slice_in_dim(cells, cells.shape[dim] - width, cells.shape[dim], axis=dim)
        cells = jnp.concatenate(
            [
                lax.ppermute(tail, axis, [(i, (i + 1) % count) for i in range(ends)]),
                cells,
                lax.ppermute(head, axis, [((i + 1) % count, i) for i in range(ends)]),
            ],
            axis=dim,
        )
    return cells


def trade(parts, width):
    count = lax.axis_size("gx")
    ends = count - 1
    heads = [lax.slice_in_dim(a, 0, width, axis=dim) for a, dim in parts]
    tails = [lax.slice_in_dim(a, a.shape[dim] - width, a.shape[dim], axis=dim) for a, dim in parts]
    pack = lambda pieces: jnp.concatenate([p.reshape(-1) for p in pieces])
    from_left = lax.ppermute(pack(tails), "gx", [(i, i + 1) for i in range(ends)])
    from_right = lax.ppermute(pack(heads), "gx", [(i + 1, i) for i in range(ends)])
    out = []
    offset = 0
    for (a, dim), h in zip(parts, heads):
        size = h.size
        left = from_left[offset : offset + size].reshape(h.shape)
        right = from_right[offset : offset + size].reshape(h.shape)
        offset += size
        out.append(jnp.concatenate([left, a, right], axis=dim))
    return out


def block_mean(field, factor):
    while factor > 1:
        lead = field.shape[:-2]
        rows, cols = (field.shape[-2], field.shape[-1])
        pairs = (jnp.arange(cols)[:, None] // 2 == jnp.arange(cols // 2)[None, :]).astype(jnp.float32)
        field = jnp.einsum("...y,yz->...z", field, pairs, precision=lax.Precision.HIGHEST)
        field = 0.25 * field.reshape(lead + (rows // 2, 2, cols // 2)).sum(axis=-2)
        factor //= 2
    return field


def reaction_field(friction, ice_mask, layers):
    open_water = (ice_mask == 0).astype(jnp.float32)
    grounded = (ice_mask == 2).astype(jnp.float32)
    bottom = (jnp.arange(layers) == 0).astype(jnp.float32).reshape(layers, 1, 1)
    return 0.02 + 2.0 * open_water[None] + bottom * (grounded * friction)[None]


def build_operator(eta_level, react_level, level_index):
    scale = horizontal_scale / 4.0**level_index
    weight_x = jnp.array([4.0, 1.0], jnp.float32).reshape(2, 1, 1, 1) * scale
    weight_y = jnp.array([1.0, 4.0], jnp.float32).reshape(2, 1, 1, 1) * scale
    inner = eta_level[:, 1:-1, :]
    face_x = weight_x * (0.5 * (eta_level[:, 1:, :] + eta_level[:, :-1, :]))[None]
    padded = jnp.pad(inner, ((0, 0), (0, 0), (1, 1)))
    face_y = weight_y * (0.5 * (padded[:, :, 1:] + padded[:, :, :-1]))[None]
    face_z = vertical_scale * 0.5 * (inner[1:] + inner[:-1])
    vertical = jnp.pad(face_z, ((1, 1), (0, 0), (0, 0)))
    diagonal = face_x[:, :, 1:] + face_x[:, :, :-1] + face_y[..., 1:] + face_y[..., :-1]
    diagonal = diagonal + (vertical[1:] + vertical[:-1] + react_level)[None]
    layers = diagonal.shape[1]
    inverses = []
    ratios = []
    for layer in range(layers):
        pivot = diagonal[:, layer]
        if layer > 0:
            pivot = pivot - face_z[layer - 1] * ratios[-1]
        inverse = 1.0 / pivot
        inverses.append(inverse)
        if layer < layers - 1:
            ratios.append(face_z[layer] * inverse)
    return (face_x, face_y, face_z, react_level, jnp.stack(inverses, 1), jnp.stack(ratios, 1))


def lane_ops(operator):
    face_x, face_y, face_z, react_level, inverses, ratios = operator
    return (face_x[:, :, :-1], face_x[:, :, 1:], face_y[..., :-1], face_y[..., 1:], face_z, react_level, inverses, ratios)


def sweep_kernel(w_ref, b_ref, fxl_ref, fxr_ref, fyl_ref, fyr_ref, fz_ref, re_ref, inv_ref, rat_ref, mask_ref, out_ref,
                 *, rows, cut_w, cut_b, cut_op, mode):
    relax(w_ref, b_ref, (fxl_ref, fxr_ref, fyl_ref, fyr_ref, fz_ref, re_ref, inv_ref, rat_ref), mask_ref, out_ref,
          rows=rows, cut_w=cut_w, cut_b=cut_b, cut_op=cut_op, mode=mode)


def coarse_kernel(b_ref, fxl_ref, fxr_ref, fyl_ref, fyr_ref, fz_ref, re_ref, inv_ref, rat_ref, mask_ref, out_ref, w_ref,
                  *, rows, turns):
    lanes = (fxl_ref, fxr_ref, fyl_ref, fyr_ref, fz_ref, re_ref, inv_ref, rat_ref)
    w_ref[...] = jnp.zeros(w_ref.shape, jnp.float32)
    for turn in range(turns):
        relax(w_ref, b_ref, lanes, mask_ref, out_ref, rows=rows, cut_w=7, cut_b=0, cut_op=0, mode="sweep")
        if turn < turns - 1:
            for k in range(out_ref.shape[1]):
                w_ref[0, k, pl.ds(8, rows), :] = out_ref[0, k]


def relax(w_ref, b_ref, lanes, mask_ref, out_ref, *, rows, cut_w, cut_b, cut_op, mode):
    fxl_ref, fxr_ref, fyl_ref, fyr_ref, fz_ref, re_ref, inv_ref, rat_ref = lanes
    layers = out_ref.shape[1]
    cols = out_ref.shape[3]
    lane = lax.broadcasted_iota(jnp.int32, (rows, cols), 1)
    probe = pltpu.roll(lane, 1, 1)
    forward_roll = probe == jnp.where(lane == 0, cols - 1, lane - 1)
    first_col = lane == 0
    last_col = lane == cols - 1

    def cell(ref, k, cut):
        return ref[0, k, pl.ds(cut, rows), :]

    def field(k):
        return w_ref[0, k, pl.ds(cut_w + 1, rows), :]

    def applied(k):
        w = field(k)
        west = w_ref[0, k, pl.ds(cut_w, rows), :]
        east = w_ref[0, k, pl.ds(cut_w + 2, rows), :]
        result = -(cell(fxr_ref, k, cut_op) * (east - w) - cell(fxl_ref, k, cut_op) * (w - west))
        ahead = pltpu.roll(w, 1, 1)
        behind = pltpu.roll(w, cols - 1, 1)
        south = jnp.where(forward_roll, ahead, behind)
        north = jnp.where(forward_roll, behind, ahead)
        south = jnp.where(first_col, 0.0, south)
        north = jnp.where(last_col, 0.0, north)
        result = result - (cell(fyr_ref, k, cut_op) * (north - w) - cell(fyl_ref, k, cut_op) * (w - south))
        up = fz_ref[k, pl.ds(cut_op, rows), :] * (field(k + 1) - w) if k < layers - 1 else 0.0
        down = fz_ref[k - 1, pl.ds(cut_op, rows), :] * (w - field(k - 1)) if k > 0 else 0.0
        result = result - (up - down)
        return result + re_ref[k, pl.ds(cut_op, rows), :] * w

    if mode == "residual":
        for k in range(layers):
            out_ref[0, k] = cell(b_ref, k, cut_b) - applied(k)
        return
    keep = mask_ref[...] > 0.5
    previous = None
    for k in range(layers):
        residual = cell(b_ref, k, cut_b)
        if mode == "sweep":
            residual = residual - applied(k)
        if k == 0:
            forward = residual * cell(inv_ref, 0, cut_op)
        else:
            forward = (residual + fz_ref[k - 1, pl.ds(cut_op, rows), :] * previous) * cell(inv_ref, k, cut_op)
        out_ref[0, k] = forward
        previous = forward
    back = previous
    for k in range(layers - 1, -1, -1):
        if k < layers - 1:
            back = out_ref[0, k] + rat_ref[0, k, pl.ds(cut_op, rows), :] * back
        if mode == "sweep":
            value = field(k) + relax_weight * back
        else:
            value = relax_weight * back
        out_ref[0, k] = jnp.where(keep, value, 0.0)


def kernel_sweep(field_rim, target, lanes, cut_b, cut_op, mask, mode="sweep", cut_w=0, rows=None):
    parts, layers, rows_rim, cols = field_rim.shape
    rows = rows_rim - 2 if rows is None else rows
    fxl, fxr, fyl, fyr, fz, re, inv, rat = lanes
    per_part = lambda a: pl.BlockSpec((1,) + a.shape[1:], lambda c: (c,) + (0,) * (a.ndim - 1))
    whole = lambda a: pl.BlockSpec(a.shape, lambda c: (0,) * a.ndim)
    operands = [field_rim, target, fxl, fxr, fyl, fyr, fz, re, inv, rat, mask]
    specs = [per_part(field_rim), per_part(target), per_part(fxl), per_part(fxr), per_part(fyl), per_part(fyr),
             whole(fz), whole(re), per_part(inv), per_part(rat), whole(mask)]
    body = functools.partial(sweep_kernel, rows=rows, cut_w=cut_w, cut_b=cut_b, cut_op=cut_op, mode=mode)
    return pl.pallas_call(
        body,
        grid=(parts,),
        in_specs=specs,
        out_specs=pl.BlockSpec((1, layers, rows, cols), lambda c: (c, 0, 0, 0)),
        out_shape=jax.ShapeDtypeStruct((parts, layers, rows, cols), jnp.float32),
    )(*operands)


def build_kernel(eta_ref, re_ref, fxl_ref, fxr_ref, fyl_ref, fyr_ref, fz_ref, reo_ref, inv_ref, rat_ref,
                 *, rows, cut_re, scale):
    component = pl.program_id(0)
    layers = eta_ref.shape[0]
    cols = eta_ref.shape[2]
    lane = lax.broadcasted_iota(jnp.int32, (rows, cols), 1)
    probe = pltpu.roll(lane, 1, 1)
    forward_roll = probe == jnp.where(lane == 0, cols - 1, lane - 1)
    first_col = lane == 0
    last_col = lane == cols - 1
    weight_x = jnp.where(component == 0, 4.0, 1.0) * scale
    weight_y = jnp.where(component == 0, 1.0, 4.0) * scale

    def inner(k):
        return eta_ref[k, pl.ds(1, rows), :]

    faces_z = [vertical_scale * 0.5 * (inner(k + 1) + inner(k)) for k in range(layers - 1)]
    ratio = None
    for k in range(layers):
        middle = inner(k)
        west = eta_ref[k, pl.ds(0, rows), :]
        east = eta_ref[k, pl.ds(2, rows), :]
        ahead = pltpu.roll(middle, 1, 1)
        behind = pltpu.roll(middle, cols - 1, 1)
        south = jnp.where(first_col, 0.0, jnp.where(forward_roll, ahead, behind))
        north = jnp.where(last_col, 0.0, jnp.where(forward_roll, behind, ahead))
        face_w = weight_x * (0.5 * (middle + west))
        face_e = weight_x * (0.5 * (east + middle))
        face_s = weight_y * (0.5 * (middle + south))
        face_n = weight_y * (0.5 * (north + middle))
        react = re_ref[min(k, re_ref.shape[0] - 1), pl.ds(cut_re, rows), :]
        up = faces_z[k] if k < layers - 1 else 0.0
        down = faces_z[k - 1] if k > 0 else 0.0
        diagonal = face_e + face_w + face_n + face_s
        diagonal = diagonal + (up + down + react)
        if k > 0:
            diagonal = diagonal - faces_z[k - 1] * ratio
        inverse = 1.0 / diagonal
        fxl_ref[0, k] = face_w
        fxr_ref[0, k] = face_e
        fyl_ref[0, k] = face_s
        fyr_ref[0, k] = face_n
        reo_ref[k] = react
        inv_ref[0, k] = inverse
        if k < layers - 1:
            ratio = faces_z[k] * inverse
            fz_ref[k] = faces_z[k]
            rat_ref[0, k] = ratio


def kernel_operator(eta_level, react_level, level_index, cut_re=0):
    layers, rows_eta, cols = eta_level.shape
    rows = rows_eta - 2
    whole = lambda a: pl.BlockSpec(a.shape, lambda c: (0,) * a.ndim)
    per_part = lambda shape: pl.BlockSpec((1,) + shape, lambda c: (c,) + (0,) * len(shape))
    cell = (layers, rows, cols)
    faces = (layers - 1, rows, cols)
    body = functools.partial(build_kernel, rows=rows, cut_re=cut_re, scale=horizontal_scale / 4.0**level_index)
    shapes = [(2,) + cell] * 4 + [faces, cell, (2,) + cell, (2,) + faces]
    specs = [per_part(cell)] * 4 + [
        pl.BlockSpec(faces, lambda c: (0, 0, 0)),
        pl.BlockSpec(cell, lambda c: (0, 0, 0)),
        per_part(cell),
        per_part(faces),
    ]
    return tuple(
        pl.pallas_call(
            body,
            grid=(2,),
            in_specs=[whole(eta_level), whole(react_level)],
            out_specs=specs,
            out_shape=[jax.ShapeDtypeStruct(s, jnp.float32) for s in shapes],
        )(eta_level, react_level)
    )


def kernel_coarse(target, lanes, mask, turns):
    parts, layers, rows, cols = target.shape
    fxl, fxr, fyl, fyr, fz, re, inv, rat = lanes
    per_part = lambda a: pl.BlockSpec((1,) + a.shape[1:], lambda c: (c,) + (0,) * (a.ndim - 1))
    whole = lambda a: pl.BlockSpec(a.shape, lambda c: (0,) * a.ndim)
    operands = [target, fxl, fxr, fyl, fyr, fz, re, inv, rat, mask]
    specs = [per_part(target), per_part(fxl), per_part(fxr), per_part(fyl), per_part(fyr),
             whole(fz), whole(re), per_part(inv), per_part(rat), whole(mask)]
    body = functools.partial(coarse_kernel, rows=rows, turns=turns)
    return pl.pallas_call(
        body,
        grid=(parts,),
        in_specs=specs,
        out_specs=pl.BlockSpec((1, layers, rows, cols), lambda c: (c, 0, 0, 0)),
        out_shape=jax.ShapeDtypeStruct((parts, layers, rows, cols), jnp.float32),
        scratch_shapes=[pltpu.VMEM((1, layers, rows + 16, cols), jnp.float32)],
    )(*operands)


def rows_inside(cells, halo, extent, cols):
    return jnp.broadcast_to(inside(cells, halo, extent)[0, 0], (extent, cols)).astype(jnp.float32)


def shrink(operator, cut):
    if cut == 0:
        return operator
    face_x, face_y, face_z, react_level, inverses, ratios = operator
    rows = face_y.shape[2]
    return (
        face_x[:, :, cut : rows + 1 - cut],
        face_y[:, :, cut : rows - cut],
        face_z[:, cut : rows - cut],
        react_level[:, cut : rows - cut],
        inverses[:, :, cut : rows - cut],
        ratios[:, :, cut : rows - cut],
    )


def apply_operator(field_rim, operator):
    face_x, face_y, face_z, react_level, inverses, ratios = operator
    field = field_rim[:, :, 1:-1, :]
    flux_x = face_x * (field_rim[:, :, 1:, :] - field_rim[:, :, :-1, :])
    result = -(flux_x[:, :, 1:] - flux_x[:, :, :-1])
    padded = jnp.pad(field, ((0, 0), (0, 0), (0, 0), (1, 1)))
    flux_y = face_y * (padded[..., 1:] - padded[..., :-1])
    result = result - (flux_y[..., 1:] - flux_y[..., :-1])
    flux_z = face_z[None] * (field[:, 1:] - field[:, :-1])
    flux_z = jnp.pad(flux_z, ((0, 0), (1, 1), (0, 0), (0, 0)))
    result = result - (flux_z[:, 1:] - flux_z[:, :-1])
    return result + react_level[None] * field


def line_solve(residual, operator):
    face_z, inverses, ratios = (operator[2], operator[4], operator[5])
    layers = residual.shape[1]
    forward = [residual[:, 0] * inverses[:, 0]]
    for layer in range(1, layers):
        forward.append((residual[:, layer] + face_z[layer - 1] * forward[-1]) * inverses[:, layer])
    backward = [forward[-1]]
    for layer in range(layers - 2, -1, -1):
        backward.append(forward[layer] + ratios[:, layer] * backward[-1])
    return jnp.stack(backward[::-1], 1)


def sweep(field_rim, target, operator):
    field = field_rim[:, :, 1:-1, :]
    return field + relax_weight * line_solve(target - apply_operator(field_rim, operator), operator)


def restrict(field):
    return block_mean(field, 2)


def prolong(field):
    cols = field.shape[3]
    spread = (jnp.arange(cols)[:, None] == jnp.arange(2 * cols)[None, :] // 2).astype(jnp.float32)
    wide = jnp.einsum("ckxy,yz->ckxz", field, spread, precision=lax.Precision.HIGHEST)
    return jnp.repeat(wide, 2, axis=2)


def pad_rim(field):
    return jnp.pad(field, ((0, 0), (0, 0), (1, 1), (0, 0)))


def inside(cells, halo, extent):
    count = lax.axis_size("gx")
    first = lax.axis_index("gx") * cells - halo
    index = first + jnp.arange(extent)
    return ((index >= 0) & (index < count * cells)).reshape(1, 1, extent, 1)


def keep_inside(field, cells, halo):
    return jnp.where(inside(cells, halo, field.shape[2]), field, 0.0)


def window(full, dim, start, size, pad):
    widths = [(0, 0)] * full.ndim
    widths[dim] = (pad, pad)
    return lax.dynamic_slice_in_dim(jnp.pad(full, widths), start, size, axis=dim)


def nearby(cells, dim, hops):
    count = lax.axis_size("gx")
    lows = []
    highs = []
    for step in range(1, hops + 1):
        lows.insert(0, lax.ppermute(cells, "gx", [(i, i + step) for i in range(count - step)]))
        highs.append(lax.ppermute(cells, "gx", [(i + step, i) for i in range(count - step)]))
    return jnp.concatenate(lows + [cells] + highs, axis=dim)


def shards(misfit, adjoint_guess, viscosity, friction, ice_mask, forward_bed):
    layers, cells, cols = viscosity.shape
    where = lax.axis_index("gx")
    react_fine = reaction_field(friction, ice_mask, layers)
    react_pair = react_fine[:2]

    eta_1 = block_mean(viscosity, 2)
    eta_2 = block_mean(viscosity, 4)
    react_1 = block_mean(react_pair, 2)
    react_2 = block_mean(react_pair, 4)
    pieces = [eta_1, react_1, eta_2, react_2]
    packed = jnp.concatenate([p.reshape(-1) for p in pieces])
    gathered = lax.all_gather(packed[None], "gx", axis=0, tiled=True)
    count = gathered.shape[0]
    unpacked = []
    offset = 0
    for p in pieces:
        block = gathered[:, offset : offset + p.size].reshape((count,) + p.shape)
        offset += p.size
        unpacked.append(jnp.moveaxis(block, 0, 1).reshape((p.shape[0], count * p.shape[1], p.shape[2])))
    eta_1_all, react_1_all, eta_2_all, react_2_all = unpacked

    halo = 4
    eta_wide, guess_wide, misfit_wide, react_wide = trade(
        [(viscosity, 1), (adjoint_guess, 2), (misfit, 2), (react_pair, 1)], halo
    )
    op_0 = kernel_operator(eta_wide, react_wide, 0, 1)
    fine = kernel_sweep(guess_wide, misfit_wide, op_0, 1, 0, rows_inside(cells, 3, cells + 6, cols))
    fine = kernel_sweep(fine, misfit_wide, op_0, 2, 1, rows_inside(cells, 2, cells + 4, cols))
    residual = kernel_sweep(fine, misfit_wide, op_0, 4, 3, rows_inside(cells, 0, cells, cols), "residual", 1, cells)
    middle_rhs = restrict(residual)

    half = cells // 2
    wide = cols // 2
    rhs_wide = with_halo(middle_rhs, (("gx", 2),), half)
    eta_1_wide = window(eta_1_all, 1, where * half, 3 * half + 2, half + 1)
    react_1_wide = window(react_1_all, 1, where * half, 3 * half, half)
    op_1 = kernel_operator(eta_1_wide, react_1_wide, 1)
    middle = kernel_sweep(rhs_wide, rhs_wide, op_1, 0, 0, rows_inside(half, half, 3 * half, wide), "zero", 0, 3 * half)
    middle = kernel_sweep(middle, rhs_wide, op_1, 1, 1, rows_inside(half, half - 1, 3 * half - 2, wide))
    residual = kernel_sweep(middle, rhs_wide, op_1, half, half, rows_inside(half, 0, half, wide), "residual", half - 2, half)
    coarse_rhs = restrict(residual)

    quarter = cells // 4
    narrow = cols // 4
    reach = 3
    span = reach + COARSE_SWEEPS - 1
    coarse_rhs_near = nearby(coarse_rhs, 2, span // quarter)
    eta_2_near = window(eta_2_all, 1, where * quarter, quarter + 2 * span + 2, span + 1)
    react_2_near = window(react_2_all, 1, where * quarter, quarter + 2 * span, span)
    op_2 = kernel_operator(eta_2_near, react_2_near, 2)
    extent = quarter + 2 * span
    coarse_mask = rows_inside(quarter, span, extent, narrow)
    coarse = kernel_coarse(coarse_rhs_near, op_2, coarse_mask, COARSE_SWEEPS)
    coarse_near = coarse[:, :, span - reach : span + quarter + reach]

    lift = prolong(coarse_near)
    trim = 2 * reach - (half - 1)
    middle = middle + lift[:, :, trim : lift.shape[2] - trim]
    middle = kernel_sweep(middle, rhs_wide, op_1, 2, 2, rows_inside(half, half - 2, 3 * half - 4, wide))
    middle = kernel_sweep(middle, rhs_wide, op_1, 3, 3, rows_inside(half, half - 3, 3 * half - 6, wide))
    fine = fine + prolong(middle)
    fine = kernel_sweep(fine, misfit_wide, op_0, 3, 2, rows_inside(cells, 1, cells + 2, cols))
    fine = kernel_sweep(fine, misfit_wide, op_0, 4, 3, rows_inside(cells, 0, cells, cols))
    grounded = (ice_mask == 2).astype(jnp.float32)
    gradient = -grounded * (forward_bed[0] * fine[0, 0] + forward_bed[1] * fine[1, 0])
    return (fine, gradient)


def solution(mesh):
    placed = (
        P("ens", None, "gx", None),
        P("ens", None, "gx", None),
        P("ens", "gx", None),
        P("gx", "ens"),
        P("gx", "ens"),
        P("ens", "gx", None),
    )
    return jax.shard_map(
        shards,
        mesh=mesh,
        in_specs=placed,
        out_specs=(P("ens", None, "gx", None), P("gx", "ens")),
        check_vma=False,
    )
```

```python
import functools

import jax
import jax.numpy as jnp
from jax import lax
from jax.experimental import pallas as pl
from jax.experimental.pallas import tpu as pltpu
from jax.sharding import PartitionSpec as P

NU = 2
COARSE_SWEEPS = 6


horizontal_scale = 1.0
vertical_scale = 4.0
relax_weight = 0.8


def with_halo(cells, sides, width):
    for axis, dim in sides:
        count = lax.axis_size(axis)
        ends = count - 1
        head = lax.slice_in_dim(cells, 0, width, axis=dim)
        tail = lax.slice_in_dim(cells, cells.shape[dim] - width, cells.shape[dim], axis=dim)
        cells = jnp.concatenate(
            [
                lax.ppermute(tail, axis, [(i, (i + 1) % count) for i in range(ends)]),
                cells,
                lax.ppermute(head, axis, [((i + 1) % count, i) for i in range(ends)]),
            ],
            axis=dim,
        )
    return cells


def trade(parts, width):
    count = lax.axis_size("gx")
    ends = count - 1
    heads = [lax.slice_in_dim(a, 0, width, axis=dim) for a, dim in parts]
    tails = [lax.slice_in_dim(a, a.shape[dim] - width, a.shape[dim], axis=dim) for a, dim in parts]
    pack = lambda pieces: jnp.concatenate([p.reshape(-1) for p in pieces])
    from_left = lax.ppermute(pack(tails), "gx", [(i, i + 1) for i in range(ends)])
    from_right = lax.ppermute(pack(heads), "gx", [(i + 1, i) for i in range(ends)])
    out = []
    offset = 0
    for (a, dim), h in zip(parts, heads):
        size = h.size
        left = from_left[offset : offset + size].reshape(h.shape)
        right = from_right[offset : offset + size].reshape(h.shape)
        offset += size
        out.append(jnp.concatenate([left, a, right], axis=dim))
    return out


def block_mean(field, factor):
    while factor > 1:
        lead = field.shape[:-2]
        rows, cols = (field.shape[-2], field.shape[-1])
        pairs = (jnp.arange(cols)[:, None] // 2 == jnp.arange(cols // 2)[None, :]).astype(jnp.float32)
        field = jnp.einsum("...y,yz->...z", field, pairs, precision=lax.Precision.HIGHEST)
        field = 0.25 * field.reshape(lead + (rows // 2, 2, cols // 2)).sum(axis=-2)
        factor //= 2
    return field


def reaction_field(friction, ice_mask, layers):
    open_water = (ice_mask == 0).astype(jnp.float32)
    grounded = (ice_mask == 2).astype(jnp.float32)
    bottom = (jnp.arange(layers) == 0).astype(jnp.float32).reshape(layers, 1, 1)
    return 0.02 + 2.0 * open_water[None] + bottom * (grounded * friction)[None]


def build_operator(eta_level, react_level, level_index):
    scale = horizontal_scale / 4.0**level_index
    weight_x = jnp.array([4.0, 1.0], jnp.float32).reshape(2, 1, 1, 1) * scale
    weight_y = jnp.array([1.0, 4.0], jnp.float32).reshape(2, 1, 1, 1) * scale
    inner = eta_level[:, 1:-1, :]
    face_x = weight_x * (0.5 * (eta_level[:, 1:, :] + eta_level[:, :-1, :]))[None]
    padded = jnp.pad(inner, ((0, 0), (0, 0), (1, 1)))
    face_y = weight_y * (0.5 * (padded[:, :, 1:] + padded[:, :, :-1]))[None]
    face_z = vertical_scale * 0.5 * (inner[1:] + inner[:-1])
    vertical = jnp.pad(face_z, ((1, 1), (0, 0), (0, 0)))
    diagonal = face_x[:, :, 1:] + face_x[:, :, :-1] + face_y[..., 1:] + face_y[..., :-1]
    diagonal = diagonal + (vertical[1:] + vertical[:-1] + react_level)[None]
    layers = diagonal.shape[1]
    inverses = []
    ratios = []
    for layer in range(layers):
        pivot = diagonal[:, layer]
        if layer > 0:
            pivot = pivot - face_z[layer - 1] * ratios[-1]
        inverse = 1.0 / pivot
        inverses.append(inverse)
        if layer < layers - 1:
            ratios.append(face_z[layer] * inverse)
    return (face_x, face_y, face_z, react_level, jnp.stack(inverses, 1), jnp.stack(ratios, 1))


def lane_ops(operator):
    face_x, face_y, face_z, react_level, inverses, ratios = operator
    return (face_x[:, :, :-1], face_x[:, :, 1:], face_y[..., :-1], face_y[..., 1:], face_z, react_level, inverses, ratios)


def sweep_kernel(w_ref, b_ref, fxl_ref, fxr_ref, fyl_ref, fyr_ref, fz_ref, re_ref, inv_ref, rat_ref, mask_ref, out_ref,
                 *, rows, cut_w, cut_b, cut_op, mode):
    relax(w_ref, b_ref, (fxl_ref, fxr_ref, fyl_ref, fyr_ref, fz_ref, re_ref, inv_ref, rat_ref), mask_ref, out_ref,
          rows=rows, cut_w=cut_w, cut_b=cut_b, cut_op=cut_op, mode=mode)


def coarse_kernel(b_ref, fxl_ref, fxr_ref, fyl_ref, fyr_ref, fz_ref, re_ref, inv_ref, rat_ref, mask_ref, out_ref, w_ref,
                  *, rows, turns):
    lanes = (fxl_ref, fxr_ref, fyl_ref, fyr_ref, fz_ref, re_ref, inv_ref, rat_ref)
    w_ref[...] = jnp.zeros(w_ref.shape, jnp.float32)
    for turn in range(turns):
        relax(w_ref, b_ref, lanes, mask_ref, out_ref, rows=rows, cut_w=7, cut_b=0, cut_op=0, mode="sweep")
        if turn < turns - 1:
            for k in range(out_ref.shape[1]):
                w_ref[0, k, pl.ds(8, rows), :] = out_ref[0, k]


def relax(w_ref, b_ref, lanes, mask_ref, out_ref, *, rows, cut_w, cut_b, cut_op, mode):
    fxl_ref, fxr_ref, fyl_ref, fyr_ref, fz_ref, re_ref, inv_ref, rat_ref = lanes
    layers = out_ref.shape[1]
    cols = out_ref.shape[3]
    lane = lax.broadcasted_iota(jnp.int32, (rows, cols), 1)
    probe = pltpu.roll(lane, 1, 1)
    forward_roll = probe == jnp.where(lane == 0, cols - 1, lane - 1)
    first_col = lane == 0
    last_col = lane == cols - 1

    def cell(ref, k, cut):
        return ref[0, k, pl.ds(cut, rows), :]

    def field(k):
        return w_ref[0, k, pl.ds(cut_w + 1, rows), :]

    def applied(k):
        w = field(k)
        west = w_ref[0, k, pl.ds(cut_w, rows), :]
        east = w_ref[0, k, pl.ds(cut_w + 2, rows), :]
        result = -(cell(fxr_ref, k, cut_op) * (east - w) - cell(fxl_ref, k, cut_op) * (w - west))
        ahead = pltpu.roll(w, 1, 1)
        behind = pltpu.roll(w, cols - 1, 1)
        south = jnp.where(forward_roll, ahead, behind)
        north = jnp.where(forward_roll, behind, ahead)
        south = jnp.where(first_col, 0.0, south)
        north = jnp.where(last_col, 0.0, north)
        result = result - (cell(fyr_ref, k, cut_op) * (north - w) - cell(fyl_ref, k, cut_op) * (w - south))
        up = fz_ref[k, pl.ds(cut_op, rows), :] * (field(k + 1) - w) if k < layers - 1 else 0.0
        down = fz_ref[k - 1, pl.ds(cut_op, rows), :] * (w - field(k - 1)) if k > 0 else 0.0
        result = result - (up - down)
        return result + re_ref[k, pl.ds(cut_op, rows), :] * w

    if mode == "residual":
        for k in range(layers):
            out_ref[0, k] = cell(b_ref, k, cut_b) - applied(k)
        return
    keep = mask_ref[...] > 0.5
    previous = None
    for k in range(layers):
        residual = cell(b_ref, k, cut_b)
        if mode == "sweep":
            residual = residual - applied(k)
        if k == 0:
            forward = residual * cell(inv_ref, 0, cut_op)
        else:
            forward = (residual + fz_ref[k - 1, pl.ds(cut_op, rows), :] * previous) * cell(inv_ref, k, cut_op)
        out_ref[0, k] = forward
        previous = forward
    back = previous
    for k in range(layers - 1, -1, -1):
        if k < layers - 1:
            back = out_ref[0, k] + rat_ref[0, k, pl.ds(cut_op, rows), :] * back
        if mode == "sweep":
            value = field(k) + relax_weight * back
        else:
            value = relax_weight * back
        out_ref[0, k] = jnp.where(keep, value, 0.0)


def kernel_sweep(field_rim, target, lanes, cut_b, cut_op, mask, mode="sweep", cut_w=0, rows=None):
    parts, layers, rows_rim, cols = field_rim.shape
    rows = rows_rim - 2 if rows is None else rows
    fxl, fxr, fyl, fyr, fz, re, inv, rat = lanes
    per_part = lambda a: pl.BlockSpec((1,) + a.shape[1:], lambda c: (c,) + (0,) * (a.ndim - 1))
    whole = lambda a: pl.BlockSpec(a.shape, lambda c: (0,) * a.ndim)
    operands = [field_rim, target, fxl, fxr, fyl, fyr, fz, re, inv, rat, mask]
    specs = [per_part(field_rim), per_part(target), per_part(fxl), per_part(fxr), per_part(fyl), per_part(fyr),
             whole(fz), whole(re), per_part(inv), per_part(rat), whole(mask)]
    body = functools.partial(sweep_kernel, rows=rows, cut_w=cut_w, cut_b=cut_b, cut_op=cut_op, mode=mode)
    return pl.pallas_call(
        body,
        grid=(parts,),
        in_specs=specs,
        out_specs=pl.BlockSpec((1, layers, rows, cols), lambda c: (c, 0, 0, 0)),
        out_shape=jax.ShapeDtypeStruct((parts, layers, rows, cols), jnp.float32),
    )(*operands)


def build_kernel(eta_ref, re_ref, fxl_ref, fxr_ref, fyl_ref, fyr_ref, fz_ref, reo_ref, inv_ref, rat_ref,
                 *, rows, cut_re, scale):
    component = pl.program_id(0)
    layers = eta_ref.shape[0]
    cols = eta_ref.shape[2]
    lane = lax.broadcasted_iota(jnp.int32, (rows, cols), 1)
    probe = pltpu.roll(lane, 1, 1)
    forward_roll = probe == jnp.where(lane == 0, cols - 1, lane - 1)
    first_col = lane == 0
    last_col = lane == cols - 1
    weight_x = jnp.where(component == 0, 4.0, 1.0) * scale
    weight_y = jnp.where(component == 0, 1.0, 4.0) * scale

    def inner(k):
        return eta_ref[k, pl.ds(1, rows), :]

    faces_z = [vertical_scale * 0.5 * (inner(k + 1) + inner(k)) for k in range(layers - 1)]
    ratio = None
    for k in range(layers):
        middle = inner(k)
        west = eta_ref[k, pl.ds(0, rows), :]
        east = eta_ref[k, pl.ds(2, rows), :]
        ahead = pltpu.roll(middle, 1, 1)
        behind = pltpu.roll(middle, cols - 1, 1)
        south = jnp.where(first_col, 0.0, jnp.where(forward_roll, ahead, behind))
        north = jnp.where(last_col, 0.0, jnp.where(forward_roll, behind, ahead))
        face_w = weight_x * (0.5 * (middle + west))
        face_e = weight_x * (0.5 * (east + middle))
        face_s = weight_y * (0.5 * (middle + south))
        face_n = weight_y * (0.5 * (north + middle))
        react = re_ref[min(k, re_ref.shape[0] - 1), pl.ds(cut_re, rows), :]
        up = faces_z[k] if k < layers - 1 else 0.0
        down = faces_z[k - 1] if k > 0 else 0.0
        diagonal = face_e + face_w + face_n + face_s
        diagonal = diagonal + (up + down + react)
        if k > 0:
            diagonal = diagonal - faces_z[k - 1] * ratio
        inverse = 1.0 / diagonal
        fxl_ref[0, k] = face_w
        fxr_ref[0, k] = face_e
        fyl_ref[0, k] = face_s
        fyr_ref[0, k] = face_n
        reo_ref[k] = react
        inv_ref[0, k] = inverse
        if k < layers - 1:
            ratio = faces_z[k] * inverse
            fz_ref[k] = faces_z[k]
            rat_ref[0, k] = ratio


def kernel_operator(eta_level, react_level, level_index, cut_re=0):
    layers, rows_eta, cols = eta_level.shape
    rows = rows_eta - 2
    whole = lambda a: pl.BlockSpec(a.shape, lambda c: (0,) * a.ndim)
    per_part = lambda shape: pl.BlockSpec((1,) + shape, lambda c: (c,) + (0,) * len(shape))
    cell = (layers, rows, cols)
    faces = (layers - 1, rows, cols)
    body = functools.partial(build_kernel, rows=rows, cut_re=cut_re, scale=horizontal_scale / 4.0**level_index)
    shapes = [(2,) + cell] * 4 + [faces, cell, (2,) + cell, (2,) + faces]
    specs = [per_part(cell)] * 4 + [
        pl.BlockSpec(faces, lambda c: (0, 0, 0)),
        pl.BlockSpec(cell, lambda c: (0, 0, 0)),
        per_part(cell),
        per_part(faces),
    ]
    return tuple(
        pl.pallas_call(
            body,
            grid=(2,),
            in_specs=[whole(eta_level), whole(react_level)],
            out_specs=specs,
            out_shape=[jax.ShapeDtypeStruct(s, jnp.float32) for s in shapes],
        )(eta_level, react_level)
    )


def kernel_coarse(target, lanes, mask, turns):
    parts, layers, rows, cols = target.shape
    fxl, fxr, fyl, fyr, fz, re, inv, rat = lanes
    per_part = lambda a: pl.BlockSpec((1,) + a.shape[1:], lambda c: (c,) + (0,) * (a.ndim - 1))
    whole = lambda a: pl.BlockSpec(a.shape, lambda c: (0,) * a.ndim)
    operands = [target, fxl, fxr, fyl, fyr, fz, re, inv, rat, mask]
    specs = [per_part(target), per_part(fxl), per_part(fxr), per_part(fyl), per_part(fyr),
             whole(fz), whole(re), per_part(inv), per_part(rat), whole(mask)]
    body = functools.partial(coarse_kernel, rows=rows, turns=turns)
    return pl.pallas_call(
        body,
        grid=(parts,),
        in_specs=specs,
        out_specs=pl.BlockSpec((1, layers, rows, cols), lambda c: (c, 0, 0, 0)),
        out_shape=jax.ShapeDtypeStruct((parts, layers, rows, cols), jnp.float32),
        scratch_shapes=[pltpu.VMEM((1, layers, rows + 16, cols), jnp.float32)],
    )(*operands)


def rows_inside(cells, halo, extent, cols):
    return jnp.broadcast_to(inside(cells, halo, extent)[0, 0], (extent, cols)).astype(jnp.float32)


def shrink(operator, cut):
    if cut == 0:
        return operator
    face_x, face_y, face_z, react_level, inverses, ratios = operator
    rows = face_y.shape[2]
    return (
        face_x[:, :, cut : rows + 1 - cut],
        face_y[:, :, cut : rows - cut],
        face_z[:, cut : rows - cut],
        react_level[:, cut : rows - cut],
        inverses[:, :, cut : rows - cut],
        ratios[:, :, cut : rows - cut],
    )


def apply_operator(field_rim, operator):
    face_x, face_y, face_z, react_level, inverses, ratios = operator
    field = field_rim[:, :, 1:-1, :]
    flux_x = face_x * (field_rim[:, :, 1:, :] - field_rim[:, :, :-1, :])
    result = -(flux_x[:, :, 1:] - flux_x[:, :, :-1])
    padded = jnp.pad(field, ((0, 0), (0, 0), (0, 0), (1, 1)))
    flux_y = face_y * (padded[..., 1:] - padded[..., :-1])
    result = result - (flux_y[..., 1:] - flux_y[..., :-1])
    flux_z = face_z[None] * (field[:, 1:] - field[:, :-1])
    flux_z = jnp.pad(flux_z, ((0, 0), (1, 1), (0, 0), (0, 0)))
    result = result - (flux_z[:, 1:] - flux_z[:, :-1])
    return result + react_level[None] * field


def line_solve(residual, operator):
    face_z, inverses, ratios = (operator[2], operator[4], operator[5])
    layers = residual.shape[1]
    forward = [residual[:, 0] * inverses[:, 0]]
    for layer in range(1, layers):
        forward.append((residual[:, layer] + face_z[layer - 1] * forward[-1]) * inverses[:, layer])
    backward = [forward[-1]]
    for layer in range(layers - 2, -1, -1):
        backward.append(forward[layer] + ratios[:, layer] * backward[-1])
    return jnp.stack(backward[::-1], 1)


def sweep(field_rim, target, operator):
    field = field_rim[:, :, 1:-1, :]
    return field + relax_weight * line_solve(target - apply_operator(field_rim, operator), operator)


def restrict(field):
    return block_mean(field, 2)


def prolong(field):
    cols = field.shape[3]
    spread = (jnp.arange(cols)[:, None] == jnp.arange(2 * cols)[None, :] // 2).astype(jnp.float32)
    wide = jnp.einsum("ckxy,yz->ckxz", field, spread, precision=lax.Precision.HIGHEST)
    return jnp.repeat(wide, 2, axis=2)


def pad_rim(field):
    return jnp.pad(field, ((0, 0), (0, 0), (1, 1), (0, 0)))


def inside(cells, halo, extent):
    count = lax.axis_size("gx")
    first = lax.axis_index("gx") * cells - halo
    index = first + jnp.arange(extent)
    return ((index >= 0) & (index < count * cells)).reshape(1, 1, extent, 1)


def keep_inside(field, cells, halo):
    return jnp.where(inside(cells, halo, field.shape[2]), field, 0.0)


def window(full, dim, start, size, pad):
    widths = [(0, 0)] * full.ndim
    widths[dim] = (pad, pad)
    return lax.dynamic_slice_in_dim(jnp.pad(full, widths), start, size, axis=dim)


def nearby(cells, dim, hops):
    count = lax.axis_size("gx")
    lows = []
    highs = []
    for step in range(1, hops + 1):
        lows.insert(0, lax.ppermute(cells, "gx", [(i, i + step) for i in range(count - step)]))
        highs.append(lax.ppermute(cells, "gx", [(i + step, i) for i in range(count - step)]))
    return jnp.concatenate(lows + [cells] + highs, axis=dim)


def shards(misfit, adjoint_guess, viscosity, friction, ice_mask, forward_bed):
    layers, cells, cols = viscosity.shape
    where = lax.axis_index("gx")
    react_fine = reaction_field(friction, ice_mask, layers)
    react_pair = react_fine[:2]

    eta_1 = block_mean(viscosity, 2)
    react_1 = block_mean(react_pair, 2)
    pieces = [eta_1, react_1]
    packed = jnp.concatenate([p.reshape(-1) for p in pieces])
    gathered = lax.all_gather(packed[None], "gx", axis=0, tiled=True)
    count = gathered.shape[0]
    unpacked = []
    offset = 0
    for p in pieces:
        block = gathered[:, offset : offset + p.size].reshape((count,) + p.shape)
        offset += p.size
        unpacked.append(jnp.moveaxis(block, 0, 1).reshape((p.shape[0], count * p.shape[1], p.shape[2])))
    eta_1_all, react_1_all = unpacked
    eta_2_all = block_mean(eta_1_all, 2)
    react_2_all = block_mean(react_1_all, 2)

    halo = 4
    eta_wide, guess_wide, misfit_wide, react_wide = trade(
        [(viscosity, 1), (adjoint_guess, 2), (misfit, 2), (react_pair, 1)], halo
    )
    op_0 = kernel_operator(eta_wide, react_wide, 0, 1)
    fine = kernel_sweep(guess_wide, misfit_wide, op_0, 1, 0, rows_inside(cells, 3, cells + 6, cols))
    fine = kernel_sweep(fine, misfit_wide, op_0, 2, 1, rows_inside(cells, 2, cells + 4, cols))
    residual = kernel_sweep(fine, misfit_wide, op_0, 4, 3, rows_inside(cells, 0, cells, cols), "residual", 1, cells)
    middle_rhs = restrict(residual)

    half = cells // 2
    wide = cols // 2
    rhs_wide = with_halo(middle_rhs, (("gx", 2),), half)
    eta_1_wide = window(eta_1_all, 1, where * half, 3 * half + 2, half + 1)
    react_1_wide = window(react_1_all, 1, where * half, 3 * half, half)
    op_1 = kernel_operator(eta_1_wide, react_1_wide, 1)
    middle = kernel_sweep(rhs_wide, rhs_wide, op_1, 0, 0, rows_inside(half, half, 3 * half, wide), "zero", 0, 3 * half)
    middle = kernel_sweep(middle, rhs_wide, op_1, 1, 1, rows_inside(half, half - 1, 3 * half - 2, wide))
    residual = kernel_sweep(middle, rhs_wide, op_1, half, half, rows_inside(half, 0, half, wide), "residual", half - 2, half)
    coarse_rhs = restrict(residual)

    quarter = cells // 4
    narrow = cols // 4
    reach = 3
    span = reach + COARSE_SWEEPS - 1
    coarse_rhs_near = nearby(coarse_rhs, 2, span // quarter)
    eta_2_near = window(eta_2_all, 1, where * quarter, quarter + 2 * span + 2, span + 1)
    react_2_near = window(react_2_all, 1, where * quarter, quarter + 2 * span, span)
    op_2 = kernel_operator(eta_2_near, react_2_near, 2)
    extent = quarter + 2 * span
    coarse_mask = rows_inside(quarter, span, extent, narrow)
    coarse = kernel_coarse(coarse_rhs_near, op_2, coarse_mask, COARSE_SWEEPS)
    coarse_near = coarse[:, :, span - reach : span + quarter + reach]

    lift = prolong(coarse_near)
    trim = 2 * reach - (half - 1)
    middle = middle + lift[:, :, trim : lift.shape[2] - trim]
    middle = kernel_sweep(middle, rhs_wide, op_1, 2, 2, rows_inside(half, half - 2, 3 * half - 4, wide))
    middle = kernel_sweep(middle, rhs_wide, op_1, 3, 3, rows_inside(half, half - 3, 3 * half - 6, wide))
    fine = fine + prolong(middle)
    fine = kernel_sweep(fine, misfit_wide, op_0, 3, 2, rows_inside(cells, 1, cells + 2, cols))
    fine = kernel_sweep(fine, misfit_wide, op_0, 4, 3, rows_inside(cells, 0, cells, cols))
    grounded = (ice_mask == 2).astype(jnp.float32)
    gradient = -grounded * (forward_bed[0] * fine[0, 0] + forward_bed[1] * fine[1, 0])
    return (fine, gradient)


def solution(mesh):
    placed = (
        P("ens", None, "gx", None),
        P("ens", None, "gx", None),
        P("ens", "gx", None),
        P("gx", "ens"),
        P("gx", "ens"),
        P("ens", "gx", None),
    )
    return jax.shard_map(
        shards,
        mesh=mesh,
        in_specs=placed,
        out_specs=(P("ens", None, "gx", None), P("gx", "ens")),
        check_vma=False,
    )
```

```python
import functools

import jax
import jax.numpy as jnp
from jax import lax
from jax.experimental import pallas as pl
from jax.experimental.pallas import tpu as pltpu
from jax.sharding import PartitionSpec as P

NU = 2
COARSE_SWEEPS = 6


horizontal_scale = 1.0
vertical_scale = 4.0
relax_weight = 0.8


def with_halo(cells, sides, width):
    for axis, dim in sides:
        count = lax.axis_size(axis)
        ends = count - 1
        head = lax.slice_in_dim(cells, 0, width, axis=dim)
        tail = lax.slice_in_dim(cells, cells.shape[dim] - width, cells.shape[dim], axis=dim)
        cells = jnp.concatenate(
            [
                lax.ppermute(tail, axis, [(i, (i + 1) % count) for i in range(ends)]),
                cells,
                lax.ppermute(head, axis, [((i + 1) % count, i) for i in range(ends)]),
            ],
            axis=dim,
        )
    return cells


def trade(parts, width):
    count = lax.axis_size("gx")
    ends = count - 1
    heads = [lax.slice_in_dim(a, 0, width, axis=dim) for a, dim in parts]
    tails = [lax.slice_in_dim(a, a.shape[dim] - width, a.shape[dim], axis=dim) for a, dim in parts]
    pack = lambda pieces: jnp.concatenate([p.reshape(-1) for p in pieces])
    from_left = lax.ppermute(pack(tails), "gx", [(i, i + 1) for i in range(ends)])
    from_right = lax.ppermute(pack(heads), "gx", [(i + 1, i) for i in range(ends)])
    out = []
    offset = 0
    for (a, dim), h in zip(parts, heads):
        size = h.size
        left = from_left[offset : offset + size].reshape(h.shape)
        right = from_right[offset : offset + size].reshape(h.shape)
        offset += size
        out.append(jnp.concatenate([left, a, right], axis=dim))
    return out


def block_mean(field, factor):
    while factor > 1:
        lead = field.shape[:-2]
        rows, cols = (field.shape[-2], field.shape[-1])
        pairs = (jnp.arange(cols)[:, None] // 2 == jnp.arange(cols // 2)[None, :]).astype(jnp.float32)
        field = jnp.einsum("...y,yz->...z", field, pairs, precision=lax.Precision.HIGHEST)
        field = 0.25 * field.reshape(lead + (rows // 2, 2, cols // 2)).sum(axis=-2)
        factor //= 2
    return field


def reaction_field(friction, ice_mask, layers):
    open_water = (ice_mask == 0).astype(jnp.float32)
    grounded = (ice_mask == 2).astype(jnp.float32)
    bottom = (jnp.arange(layers) == 0).astype(jnp.float32).reshape(layers, 1, 1)
    return 0.02 + 2.0 * open_water[None] + bottom * (grounded * friction)[None]


def build_operator(eta_level, react_level, level_index):
    scale = horizontal_scale / 4.0**level_index
    weight_x = jnp.array([4.0, 1.0], jnp.float32).reshape(2, 1, 1, 1) * scale
    weight_y = jnp.array([1.0, 4.0], jnp.float32).reshape(2, 1, 1, 1) * scale
    inner = eta_level[:, 1:-1, :]
    face_x = weight_x * (0.5 * (eta_level[:, 1:, :] + eta_level[:, :-1, :]))[None]
    padded = jnp.pad(inner, ((0, 0), (0, 0), (1, 1)))
    face_y = weight_y * (0.5 * (padded[:, :, 1:] + padded[:, :, :-1]))[None]
    face_z = vertical_scale * 0.5 * (inner[1:] + inner[:-1])
    vertical = jnp.pad(face_z, ((1, 1), (0, 0), (0, 0)))
    diagonal = face_x[:, :, 1:] + face_x[:, :, :-1] + face_y[..., 1:] + face_y[..., :-1]
    diagonal = diagonal + (vertical[1:] + vertical[:-1] + react_level)[None]
    layers = diagonal.shape[1]
    inverses = []
    ratios = []
    for layer in range(layers):
        pivot = diagonal[:, layer]
        if layer > 0:
            pivot = pivot - face_z[layer - 1] * ratios[-1]
        inverse = 1.0 / pivot
        inverses.append(inverse)
        if layer < layers - 1:
            ratios.append(face_z[layer] * inverse)
    return (face_x, face_y, face_z, react_level, jnp.stack(inverses, 1), jnp.stack(ratios, 1))


def lane_ops(operator):
    face_x, face_y, face_z, react_level, inverses, ratios = operator
    return (face_x[:, :, :-1], face_x[:, :, 1:], face_y[..., :-1], face_y[..., 1:], face_z, react_level, inverses, ratios)


def sweep_kernel(w_ref, b_ref, fxl_ref, fxr_ref, fyl_ref, fyr_ref, fz_ref, re_ref, inv_ref, rat_ref, mask_ref, out_ref,
                 *, rows, cut_w, cut_b, cut_op, mode, scale):
    relax(w_ref, b_ref, (fxl_ref, fxr_ref, fyl_ref, fyr_ref, fz_ref, re_ref, inv_ref, rat_ref, scale), mask_ref, out_ref,
          rows=rows, cut_w=cut_w, cut_b=cut_b, cut_op=cut_op, mode=mode)


def coarse_kernel(b_ref, fxl_ref, fxr_ref, fyl_ref, fyr_ref, fz_ref, re_ref, inv_ref, rat_ref, mask_ref, out_ref, w_ref,
                  *, rows, turns, scale):
    lanes = (fxl_ref, fxr_ref, fyl_ref, fyr_ref, fz_ref, re_ref, inv_ref, rat_ref, scale)
    w_ref[...] = jnp.zeros(w_ref.shape, jnp.float32)
    for turn in range(turns):
        relax(w_ref, b_ref, lanes, mask_ref, out_ref, rows=rows, cut_w=7, cut_b=0, cut_op=0, mode="sweep")
        if turn < turns - 1:
            for k in range(out_ref.shape[1]):
                w_ref[0, k, pl.ds(8, rows), :] = out_ref[0, k]


def relax(w_ref, b_ref, lanes, mask_ref, out_ref, *, rows, cut_w, cut_b, cut_op, mode):
    fxl_ref, fxr_ref, fyl_ref, fyr_ref, fz_ref, re_ref, inv_ref, rat_ref, scale = lanes
    layers = out_ref.shape[1]
    cols = out_ref.shape[3]
    lane = lax.broadcasted_iota(jnp.int32, (rows, cols), 1)
    probe = pltpu.roll(lane, 1, 1)
    forward_roll = probe == jnp.where(lane == 0, cols - 1, lane - 1)
    first_col = lane == 0
    last_col = lane == cols - 1

    def cell(ref, k, cut):
        return ref[0, k, pl.ds(cut, rows), :]

    component = pl.program_id(0)
    weight_x = jnp.where(component == 0, 4.0, 1.0) * scale
    weight_y = jnp.where(component == 0, 1.0, 4.0) * scale

    def face(ref, weight, k):
        return weight * ref[k, pl.ds(cut_op, rows), :]

    def field(k):
        return w_ref[0, k, pl.ds(cut_w + 1, rows), :]

    def applied(k):
        w = field(k)
        west = w_ref[0, k, pl.ds(cut_w, rows), :]
        east = w_ref[0, k, pl.ds(cut_w + 2, rows), :]
        result = -(face(fxr_ref, weight_x, k) * (east - w) - face(fxl_ref, weight_x, k) * (w - west))
        ahead = pltpu.roll(w, 1, 1)
        behind = pltpu.roll(w, cols - 1, 1)
        south = jnp.where(forward_roll, ahead, behind)
        north = jnp.where(forward_roll, behind, ahead)
        south = jnp.where(first_col, 0.0, south)
        north = jnp.where(last_col, 0.0, north)
        result = result - (face(fyr_ref, weight_y, k) * (north - w) - face(fyl_ref, weight_y, k) * (w - south))
        up = fz_ref[k, pl.ds(cut_op, rows), :] * (field(k + 1) - w) if k < layers - 1 else 0.0
        down = fz_ref[k - 1, pl.ds(cut_op, rows), :] * (w - field(k - 1)) if k > 0 else 0.0
        result = result - (up - down)
        return result + re_ref[k, pl.ds(cut_op, rows), :] * w

    if mode == "residual":
        for k in range(layers):
            out_ref[0, k] = cell(b_ref, k, cut_b) - applied(k)
        return
    keep = mask_ref[...] > 0.5
    previous = None
    for k in range(layers):
        residual = cell(b_ref, k, cut_b)
        if mode == "sweep":
            residual = residual - applied(k)
        if k == 0:
            forward = residual * cell(inv_ref, 0, cut_op)
        else:
            forward = (residual + fz_ref[k - 1, pl.ds(cut_op, rows), :] * previous) * cell(inv_ref, k, cut_op)
        out_ref[0, k] = forward
        previous = forward
    back = previous
    for k in range(layers - 1, -1, -1):
        if k < layers - 1:
            back = out_ref[0, k] + rat_ref[0, k, pl.ds(cut_op, rows), :] * back
        if mode == "sweep":
            value = field(k) + relax_weight * back
        else:
            value = relax_weight * back
        out_ref[0, k] = jnp.where(keep, value, 0.0)


def kernel_sweep(field_rim, target, lanes, cut_b, cut_op, mask, mode="sweep", cut_w=0, rows=None):
    parts, layers, rows_rim, cols = field_rim.shape
    rows = rows_rim - 2 if rows is None else rows
    fxl, fxr, fyl, fyr, fz, re, inv, rat, scale = lanes
    per_part = lambda a: pl.BlockSpec((1,) + a.shape[1:], lambda c: (c,) + (0,) * (a.ndim - 1))
    whole = lambda a: pl.BlockSpec(a.shape, lambda c: (0,) * a.ndim)
    operands = [field_rim, target, fxl, fxr, fyl, fyr, fz, re, inv, rat, mask]
    specs = [per_part(field_rim), per_part(target), whole(fxl), whole(fxr), whole(fyl), whole(fyr),
             whole(fz), whole(re), per_part(inv), per_part(rat), whole(mask)]
    body = functools.partial(sweep_kernel, rows=rows, cut_w=cut_w, cut_b=cut_b, cut_op=cut_op, mode=mode, scale=scale)
    return pl.pallas_call(
        body,
        grid=(parts,),
        in_specs=specs,
        out_specs=pl.BlockSpec((1, layers, rows, cols), lambda c: (c, 0, 0, 0)),
        out_shape=jax.ShapeDtypeStruct((parts, layers, rows, cols), jnp.float32),
    )(*operands)


def build_kernel(eta_ref, re_ref, fxl_ref, fxr_ref, fyl_ref, fyr_ref, fz_ref, reo_ref, inv_ref, rat_ref,
                 *, rows, cut_re, scale):
    component = pl.program_id(0)
    layers = eta_ref.shape[0]
    cols = eta_ref.shape[2]
    lane = lax.broadcasted_iota(jnp.int32, (rows, cols), 1)
    probe = pltpu.roll(lane, 1, 1)
    forward_roll = probe == jnp.where(lane == 0, cols - 1, lane - 1)
    first_col = lane == 0
    last_col = lane == cols - 1
    weight_x = jnp.where(component == 0, 4.0, 1.0) * scale
    weight_y = jnp.where(component == 0, 1.0, 4.0) * scale

    def inner(k):
        return eta_ref[k, pl.ds(1, rows), :]

    faces_z = [vertical_scale * 0.5 * (inner(k + 1) + inner(k)) for k in range(layers - 1)]
    ratio = None
    for k in range(layers):
        middle = inner(k)
        west = eta_ref[k, pl.ds(0, rows), :]
        east = eta_ref[k, pl.ds(2, rows), :]
        ahead = pltpu.roll(middle, 1, 1)
        behind = pltpu.roll(middle, cols - 1, 1)
        south = jnp.where(first_col, 0.0, jnp.where(forward_roll, ahead, behind))
        north = jnp.where(last_col, 0.0, jnp.where(forward_roll, behind, ahead))
        base_w = 0.5 * (middle + west)
        base_e = 0.5 * (east + middle)
        base_s = 0.5 * (middle + south)
        base_n = 0.5 * (north + middle)
        face_w = weight_x * base_w
        face_e = weight_x * base_e
        face_s = weight_y * base_s
        face_n = weight_y * base_n
        react = re_ref[min(k, re_ref.shape[0] - 1), pl.ds(cut_re, rows), :]
        up = faces_z[k] if k < layers - 1 else 0.0
        down = faces_z[k - 1] if k > 0 else 0.0
        diagonal = face_e + face_w + face_n + face_s
        diagonal = diagonal + (up + down + react)
        if k > 0:
            diagonal = diagonal - faces_z[k - 1] * ratio
        inverse = 1.0 / diagonal
        fxl_ref[k] = base_w
        fxr_ref[k] = base_e
        fyl_ref[k] = base_s
        fyr_ref[k] = base_n
        reo_ref[k] = react
        inv_ref[0, k] = inverse
        if k < layers - 1:
            ratio = faces_z[k] * inverse
            fz_ref[k] = faces_z[k]
            rat_ref[0, k] = ratio


def kernel_operator(eta_level, react_level, level_index, cut_re=0):
    layers, rows_eta, cols = eta_level.shape
    rows = rows_eta - 2
    whole = lambda a: pl.BlockSpec(a.shape, lambda c: (0,) * a.ndim)
    per_part = lambda shape: pl.BlockSpec((1,) + shape, lambda c: (c,) + (0,) * len(shape))
    cell = (layers, rows, cols)
    faces = (layers - 1, rows, cols)
    body = functools.partial(build_kernel, rows=rows, cut_re=cut_re, scale=horizontal_scale / 4.0**level_index)
    shapes = [cell] * 4 + [faces, cell, (2,) + cell, (2,) + faces]
    specs = [pl.BlockSpec(cell, lambda c: (0, 0, 0))] * 4 + [
        pl.BlockSpec(faces, lambda c: (0, 0, 0)),
        pl.BlockSpec(cell, lambda c: (0, 0, 0)),
        per_part(cell),
        per_part(faces),
    ]
    return tuple(
        pl.pallas_call(
            body,
            grid=(2,),
            in_specs=[whole(eta_level), whole(react_level)],
            out_specs=specs,
            out_shape=[jax.ShapeDtypeStruct(s, jnp.float32) for s in shapes],
        )(eta_level, react_level)
    ) + (horizontal_scale / 4.0**level_index,)


def kernel_coarse(target, lanes, mask, turns):
    parts, layers, rows, cols = target.shape
    fxl, fxr, fyl, fyr, fz, re, inv, rat, scale = lanes
    per_part = lambda a: pl.BlockSpec((1,) + a.shape[1:], lambda c: (c,) + (0,) * (a.ndim - 1))
    whole = lambda a: pl.BlockSpec(a.shape, lambda c: (0,) * a.ndim)
    operands = [target, fxl, fxr, fyl, fyr, fz, re, inv, rat, mask]
    specs = [per_part(target), whole(fxl), whole(fxr), whole(fyl), whole(fyr),
             whole(fz), whole(re), per_part(inv), per_part(rat), whole(mask)]
    body = functools.partial(coarse_kernel, rows=rows, turns=turns, scale=scale)
    return pl.pallas_call(
        body,
        grid=(parts,),
        in_specs=specs,
        out_specs=pl.BlockSpec((1, layers, rows, cols), lambda c: (c, 0, 0, 0)),
        out_shape=jax.ShapeDtypeStruct((parts, layers, rows, cols), jnp.float32),
        scratch_shapes=[pltpu.VMEM((1, layers, rows + 16, cols), jnp.float32)],
    )(*operands)


def rows_inside(cells, halo, extent, cols):
    return jnp.broadcast_to(inside(cells, halo, extent)[0, 0], (extent, cols)).astype(jnp.float32)


def shrink(operator, cut):
    if cut == 0:
        return operator
    face_x, face_y, face_z, react_level, inverses, ratios = operator
    rows = face_y.shape[2]
    return (
        face_x[:, :, cut : rows + 1 - cut],
        face_y[:, :, cut : rows - cut],
        face_z[:, cut : rows - cut],
        react_level[:, cut : rows - cut],
        inverses[:, :, cut : rows - cut],
        ratios[:, :, cut : rows - cut],
    )


def apply_operator(field_rim, operator):
    face_x, face_y, face_z, react_level, inverses, ratios = operator
    field = field_rim[:, :, 1:-1, :]
    flux_x = face_x * (field_rim[:, :, 1:, :] - field_rim[:, :, :-1, :])
    result = -(flux_x[:, :, 1:] - flux_x[:, :, :-1])
    padded = jnp.pad(field, ((0, 0), (0, 0), (0, 0), (1, 1)))
    flux_y = face_y * (padded[..., 1:] - padded[..., :-1])
    result = result - (flux_y[..., 1:] - flux_y[..., :-1])
    flux_z = face_z[None] * (field[:, 1:] - field[:, :-1])
    flux_z = jnp.pad(flux_z, ((0, 0), (1, 1), (0, 0), (0, 0)))
    result = result - (flux_z[:, 1:] - flux_z[:, :-1])
    return result + react_level[None] * field


def line_solve(residual, operator):
    face_z, inverses, ratios = (operator[2], operator[4], operator[5])
    layers = residual.shape[1]
    forward = [residual[:, 0] * inverses[:, 0]]
    for layer in range(1, layers):
        forward.append((residual[:, layer] + face_z[layer - 1] * forward[-1]) * inverses[:, layer])
    backward = [forward[-1]]
    for layer in range(layers - 2, -1, -1):
        backward.append(forward[layer] + ratios[:, layer] * backward[-1])
    return jnp.stack(backward[::-1], 1)


def sweep(field_rim, target, operator):
    field = field_rim[:, :, 1:-1, :]
    return field + relax_weight * line_solve(target - apply_operator(field_rim, operator), operator)


def restrict(field):
    return block_mean(field, 2)


def prolong(field):
    cols = field.shape[3]
    spread = (jnp.arange(cols)[:, None] == jnp.arange(2 * cols)[None, :] // 2).astype(jnp.float32)
    wide = jnp.einsum("ckxy,yz->ckxz", field, spread, precision=lax.Precision.HIGHEST)
    return jnp.repeat(wide, 2, axis=2)


def pad_rim(field):
    return jnp.pad(field, ((0, 0), (0, 0), (1, 1), (0, 0)))


def inside(cells, halo, extent):
    count = lax.axis_size("gx")
    first = lax.axis_index("gx") * cells - halo
    index = first + jnp.arange(extent)
    return ((index >= 0) & (index < count * cells)).reshape(1, 1, extent, 1)


def keep_inside(field, cells, halo):
    return jnp.where(inside(cells, halo, field.shape[2]), field, 0.0)


def window(full, dim, start, size, pad):
    widths = [(0, 0)] * full.ndim
    widths[dim] = (pad, pad)
    return lax.dynamic_slice_in_dim(jnp.pad(full, widths), start, size, axis=dim)


def nearby(cells, dim, hops):
    count = lax.axis_size("gx")
    lows = []
    highs = []
    for step in range(1, hops + 1):
        lows.insert(0, lax.ppermute(cells, "gx", [(i, i + step) for i in range(count - step)]))
        highs.append(lax.ppermute(cells, "gx", [(i + step, i) for i in range(count - step)]))
    return jnp.concatenate(lows + [cells] + highs, axis=dim)


def shards(misfit, adjoint_guess, viscosity, friction, ice_mask, forward_bed):
    layers, cells, cols = viscosity.shape
    where = lax.axis_index("gx")
    react_fine = reaction_field(friction, ice_mask, layers)
    react_pair = react_fine[:2]

    eta_1 = block_mean(viscosity, 2)
    react_1 = block_mean(react_pair, 2)
    pieces = [eta_1, react_1]
    packed = jnp.concatenate([p.reshape(-1) for p in pieces])
    gathered = lax.all_gather(packed[None], "gx", axis=0, tiled=True)
    count = gathered.shape[0]
    unpacked = []
    offset = 0
    for p in pieces:
        block = gathered[:, offset : offset + p.size].reshape((count,) + p.shape)
        offset += p.size
        unpacked.append(jnp.moveaxis(block, 0, 1).reshape((p.shape[0], count * p.shape[1], p.shape[2])))
    eta_1_all, react_1_all = unpacked
    eta_2_all = block_mean(eta_1_all, 2)
    react_2_all = block_mean(react_1_all, 2)

    halo = 4
    eta_wide, guess_wide, misfit_wide, react_wide = trade(
        [(viscosity, 1), (adjoint_guess, 2), (misfit, 2), (react_pair, 1)], halo
    )
    op_0 = kernel_operator(eta_wide, react_wide, 0, 1)
    fine = kernel_sweep(guess_wide, misfit_wide, op_0, 1, 0, rows_inside(cells, 3, cells + 6, cols))
    fine = kernel_sweep(fine, misfit_wide, op_0, 2, 1, rows_inside(cells, 2, cells + 4, cols))
    residual = kernel_sweep(fine, misfit_wide, op_0, 4, 3, rows_inside(cells, 0, cells, cols), "residual", 1, cells)
    middle_rhs = restrict(residual)

    half = cells // 2
    wide = cols // 2
    rhs_wide = with_halo(middle_rhs, (("gx", 2),), half)
    eta_1_wide = window(eta_1_all, 1, where * half, 3 * half + 2, half + 1)
    react_1_wide = window(react_1_all, 1, where * half, 3 * half, half)
    op_1 = kernel_operator(eta_1_wide, react_1_wide, 1)
    middle = kernel_sweep(rhs_wide, rhs_wide, op_1, 0, 0, rows_inside(half, half, 3 * half, wide), "zero", 0, 3 * half)
    middle = kernel_sweep(middle, rhs_wide, op_1, 1, 1, rows_inside(half, half - 1, 3 * half - 2, wide))
    residual = kernel_sweep(middle, rhs_wide, op_1, half, half, rows_inside(half, 0, half, wide), "residual", half - 2, half)
    coarse_rhs = restrict(residual)

    quarter = cells // 4
    narrow = cols // 4
    reach = 3
    span = reach + COARSE_SWEEPS - 1
    coarse_rhs_near = nearby(coarse_rhs, 2, span // quarter)
    eta_2_near = window(eta_2_all, 1, where * quarter, quarter + 2 * span + 2, span + 1)
    react_2_near = window(react_2_all, 1, where * quarter, quarter + 2 * span, span)
    op_2 = kernel_operator(eta_2_near, react_2_near, 2)
    extent = quarter + 2 * span
    coarse_mask = rows_inside(quarter, span, extent, narrow)
    coarse = kernel_coarse(coarse_rhs_near, op_2, coarse_mask, COARSE_SWEEPS)
    coarse_near = coarse[:, :, span - reach : span + quarter + reach]

    lift = prolong(coarse_near)
    trim = 2 * reach - (half - 1)
    middle = middle + lift[:, :, trim : lift.shape[2] - trim]
    middle = kernel_sweep(middle, rhs_wide, op_1, 2, 2, rows_inside(half, half - 2, 3 * half - 4, wide))
    middle = kernel_sweep(middle, rhs_wide, op_1, 3, 3, rows_inside(half, half - 3, 3 * half - 6, wide))
    fine = fine + prolong(middle)
    fine = kernel_sweep(fine, misfit_wide, op_0, 3, 2, rows_inside(cells, 1, cells + 2, cols))
    fine = kernel_sweep(fine, misfit_wide, op_0, 4, 3, rows_inside(cells, 0, cells, cols))
    grounded = (ice_mask == 2).astype(jnp.float32)
    gradient = -grounded * (forward_bed[0] * fine[0, 0] + forward_bed[1] * fine[1, 0])
    return (fine, gradient)


def solution(mesh):
    placed = (
        P("ens", None, "gx", None),
        P("ens", None, "gx", None),
        P("ens", "gx", None),
        P("gx", "ens"),
        P("gx", "ens"),
        P("ens", "gx", None),
    )
    return jax.shard_map(
        shards,
        mesh=mesh,
        in_specs=placed,
        out_specs=(P("ens", None, "gx", None), P("gx", "ens")),
        check_vma=False,
    )
```

```python
import functools

import jax
import jax.numpy as jnp
from jax import lax
from jax.experimental import pallas as pl
from jax.experimental.pallas import tpu as pltpu
from jax.sharding import PartitionSpec as P

NU = 2
COARSE_SWEEPS = 6


horizontal_scale = 1.0
vertical_scale = 4.0
relax_weight = 0.8


def with_halo(cells, sides, width):
    for axis, dim in sides:
        count = lax.axis_size(axis)
        ends = count - 1
        head = lax.slice_in_dim(cells, 0, width, axis=dim)
        tail = lax.slice_in_dim(cells, cells.shape[dim] - width, cells.shape[dim], axis=dim)
        cells = jnp.concatenate(
            [
                lax.ppermute(tail, axis, [(i, (i + 1) % count) for i in range(ends)]),
                cells,
                lax.ppermute(head, axis, [((i + 1) % count, i) for i in range(ends)]),
            ],
            axis=dim,
        )
    return cells


def trade(parts, width):
    count = lax.axis_size("gx")
    ends = count - 1
    heads = [lax.slice_in_dim(a, 0, width, axis=dim) for a, dim in parts]
    tails = [lax.slice_in_dim(a, a.shape[dim] - width, a.shape[dim], axis=dim) for a, dim in parts]
    pack = lambda pieces: jnp.concatenate([p.reshape(-1) for p in pieces])
    from_left = lax.ppermute(pack(tails), "gx", [(i, i + 1) for i in range(ends)])
    from_right = lax.ppermute(pack(heads), "gx", [(i + 1, i) for i in range(ends)])
    out = []
    offset = 0
    for (a, dim), h in zip(parts, heads):
        size = h.size
        left = from_left[offset : offset + size].reshape(h.shape)
        right = from_right[offset : offset + size].reshape(h.shape)
        offset += size
        out.append(jnp.concatenate([left, a, right], axis=dim))
    return out


def block_mean(field, factor):
    while factor > 1:
        lead = field.shape[:-2]
        rows, cols = (field.shape[-2], field.shape[-1])
        pairs = (jnp.arange(cols)[:, None] // 2 == jnp.arange(cols // 2)[None, :]).astype(jnp.float32)
        field = jnp.einsum("...y,yz->...z", field, pairs, precision=lax.Precision.HIGHEST)
        field = 0.25 * field.reshape(lead + (rows // 2, 2, cols // 2)).sum(axis=-2)
        factor //= 2
    return field


def reaction_field(friction, ice_mask, layers):
    open_water = (ice_mask == 0).astype(jnp.float32)
    grounded = (ice_mask == 2).astype(jnp.float32)
    bottom = (jnp.arange(layers) == 0).astype(jnp.float32).reshape(layers, 1, 1)
    return 0.02 + 2.0 * open_water[None] + bottom * (grounded * friction)[None]


def build_operator(eta_level, react_level, level_index):
    scale = horizontal_scale / 4.0**level_index
    weight_x = jnp.array([4.0, 1.0], jnp.float32).reshape(2, 1, 1, 1) * scale
    weight_y = jnp.array([1.0, 4.0], jnp.float32).reshape(2, 1, 1, 1) * scale
    inner = eta_level[:, 1:-1, :]
    face_x = weight_x * (0.5 * (eta_level[:, 1:, :] + eta_level[:, :-1, :]))[None]
    padded = jnp.pad(inner, ((0, 0), (0, 0), (1, 1)))
    face_y = weight_y * (0.5 * (padded[:, :, 1:] + padded[:, :, :-1]))[None]
    face_z = vertical_scale * 0.5 * (inner[1:] + inner[:-1])
    vertical = jnp.pad(face_z, ((1, 1), (0, 0), (0, 0)))
    diagonal = face_x[:, :, 1:] + face_x[:, :, :-1] + face_y[..., 1:] + face_y[..., :-1]
    diagonal = diagonal + (vertical[1:] + vertical[:-1] + react_level)[None]
    layers = diagonal.shape[1]
    inverses = []
    ratios = []
    for layer in range(layers):
        pivot = diagonal[:, layer]
        if layer > 0:
            pivot = pivot - face_z[layer - 1] * ratios[-1]
        inverse = 1.0 / pivot
        inverses.append(inverse)
        if layer < layers - 1:
            ratios.append(face_z[layer] * inverse)
    return (face_x, face_y, face_z, react_level, jnp.stack(inverses, 1), jnp.stack(ratios, 1))


def lane_ops(operator):
    face_x, face_y, face_z, react_level, inverses, ratios = operator
    return (face_x[:, :, :-1], face_x[:, :, 1:], face_y[..., :-1], face_y[..., 1:], face_z, react_level, inverses, ratios)


def sweep_kernel(w_ref, b_ref, fxl_ref, fxr_ref, fyl_ref, fyr_ref, fz_ref, re_ref, inv_ref, rat_ref, mask_ref, out_ref,
                 *more, rows, cut_w, cut_b, cut_op, mode, scale, then):
    lanes = (fxl_ref, fxr_ref, fyl_ref, fyr_ref, fz_ref, re_ref, inv_ref, rat_ref, scale)
    relax(w_ref, b_ref, lanes, mask_ref, out_ref, rows=rows, cut_w=cut_w, cut_b=cut_b, cut_op=cut_op, mode=mode)
    if then is not None:
        res_cut_w, res_rows, res_cut_b, res_cut_op = then
        relax(out_ref, b_ref, lanes, mask_ref, more[0], rows=res_rows, cut_w=res_cut_w, cut_b=res_cut_b,
              cut_op=res_cut_op, mode="residual")


def coarse_kernel(b_ref, fxl_ref, fxr_ref, fyl_ref, fyr_ref, fz_ref, re_ref, inv_ref, rat_ref, mask_ref, out_ref, w_ref,
                  *, rows, turns, scale):
    lanes = (fxl_ref, fxr_ref, fyl_ref, fyr_ref, fz_ref, re_ref, inv_ref, rat_ref, scale)
    w_ref[...] = jnp.zeros(w_ref.shape, jnp.float32)
    for turn in range(turns):
        relax(w_ref, b_ref, lanes, mask_ref, out_ref, rows=rows, cut_w=7, cut_b=0, cut_op=0, mode="sweep")
        if turn < turns - 1:
            for k in range(out_ref.shape[1]):
                w_ref[0, k, pl.ds(8, rows), :] = out_ref[0, k]


def relax(w_ref, b_ref, lanes, mask_ref, out_ref, *, rows, cut_w, cut_b, cut_op, mode):
    fxl_ref, fxr_ref, fyl_ref, fyr_ref, fz_ref, re_ref, inv_ref, rat_ref, scale = lanes
    layers = out_ref.shape[1]
    cols = out_ref.shape[3]
    lane = lax.broadcasted_iota(jnp.int32, (rows, cols), 1)
    probe = pltpu.roll(lane, 1, 1)
    forward_roll = probe == jnp.where(lane == 0, cols - 1, lane - 1)
    first_col = lane == 0
    last_col = lane == cols - 1

    def cell(ref, k, cut):
        return ref[0, k, pl.ds(cut, rows), :]

    component = pl.program_id(0)
    weight_x = jnp.where(component == 0, 4.0, 1.0) * scale
    weight_y = jnp.where(component == 0, 1.0, 4.0) * scale

    def face(ref, weight, k):
        return weight * ref[k, pl.ds(cut_op, rows), :]

    def field(k):
        return w_ref[0, k, pl.ds(cut_w + 1, rows), :]

    def applied(k):
        w = field(k)
        west = w_ref[0, k, pl.ds(cut_w, rows), :]
        east = w_ref[0, k, pl.ds(cut_w + 2, rows), :]
        result = -(face(fxr_ref, weight_x, k) * (east - w) - face(fxl_ref, weight_x, k) * (w - west))
        ahead = pltpu.roll(w, 1, 1)
        behind = pltpu.roll(w, cols - 1, 1)
        south = jnp.where(forward_roll, ahead, behind)
        north = jnp.where(forward_roll, behind, ahead)
        south = jnp.where(first_col, 0.0, south)
        north = jnp.where(last_col, 0.0, north)
        result = result - (face(fyr_ref, weight_y, k) * (north - w) - face(fyl_ref, weight_y, k) * (w - south))
        up = fz_ref[k, pl.ds(cut_op, rows), :] * (field(k + 1) - w) if k < layers - 1 else 0.0
        down = fz_ref[k - 1, pl.ds(cut_op, rows), :] * (w - field(k - 1)) if k > 0 else 0.0
        result = result - (up - down)
        return result + re_ref[k, pl.ds(cut_op, rows), :] * w

    if mode == "residual":
        for k in range(layers):
            out_ref[0, k] = cell(b_ref, k, cut_b) - applied(k)
        return
    keep = mask_ref[...] > 0.5
    previous = None
    for k in range(layers):
        residual = cell(b_ref, k, cut_b)
        if mode == "sweep":
            residual = residual - applied(k)
        if k == 0:
            forward = residual * cell(inv_ref, 0, cut_op)
        else:
            forward = (residual + fz_ref[k - 1, pl.ds(cut_op, rows), :] * previous) * cell(inv_ref, k, cut_op)
        out_ref[0, k] = forward
        previous = forward
    back = previous
    for k in range(layers - 1, -1, -1):
        if k < layers - 1:
            back = out_ref[0, k] + rat_ref[0, k, pl.ds(cut_op, rows), :] * back
        if mode == "sweep":
            value = field(k) + relax_weight * back
        else:
            value = relax_weight * back
        out_ref[0, k] = jnp.where(keep, value, 0.0)


def kernel_sweep(field_rim, target, lanes, cut_b, cut_op, mask, mode="sweep", cut_w=0, rows=None, then=None):
    parts, layers, rows_rim, cols = field_rim.shape
    rows = rows_rim - 2 if rows is None else rows
    fxl, fxr, fyl, fyr, fz, re, inv, rat, scale = lanes
    per_part = lambda a: pl.BlockSpec((1,) + a.shape[1:], lambda c: (c,) + (0,) * (a.ndim - 1))
    whole = lambda a: pl.BlockSpec(a.shape, lambda c: (0,) * a.ndim)
    operands = [field_rim, target, fxl, fxr, fyl, fyr, fz, re, inv, rat, mask]
    specs = [per_part(field_rim), per_part(target), whole(fxl), whole(fxr), whole(fyl), whole(fyr),
             whole(fz), whole(re), per_part(inv), per_part(rat), whole(mask)]
    body = functools.partial(
        sweep_kernel, rows=rows, cut_w=cut_w, cut_b=cut_b, cut_op=cut_op, mode=mode, scale=scale, then=then
    )
    out_specs = [pl.BlockSpec((1, layers, rows, cols), lambda c: (c, 0, 0, 0))]
    out_shape = [jax.ShapeDtypeStruct((parts, layers, rows, cols), jnp.float32)]
    if then is not None:
        out_specs.append(pl.BlockSpec((1, layers, then[1], cols), lambda c: (c, 0, 0, 0)))
        out_shape.append(jax.ShapeDtypeStruct((parts, layers, then[1], cols), jnp.float32))
    outs = pl.pallas_call(body, grid=(parts,), in_specs=specs, out_specs=out_specs, out_shape=out_shape)(*operands)
    return tuple(outs) if then is not None else outs[0]


def build_kernel(eta_ref, re_ref, fxl_ref, fxr_ref, fyl_ref, fyr_ref, fz_ref, reo_ref, inv_ref, rat_ref,
                 *, rows, cut_re, scale):
    component = pl.program_id(0)
    layers = eta_ref.shape[0]
    cols = eta_ref.shape[2]
    lane = lax.broadcasted_iota(jnp.int32, (rows, cols), 1)
    probe = pltpu.roll(lane, 1, 1)
    forward_roll = probe == jnp.where(lane == 0, cols - 1, lane - 1)
    first_col = lane == 0
    last_col = lane == cols - 1
    weight_x = jnp.where(component == 0, 4.0, 1.0) * scale
    weight_y = jnp.where(component == 0, 1.0, 4.0) * scale

    def inner(k):
        return eta_ref[k, pl.ds(1, rows), :]

    faces_z = [vertical_scale * 0.5 * (inner(k + 1) + inner(k)) for k in range(layers - 1)]
    ratio = None
    for k in range(layers):
        middle = inner(k)
        west = eta_ref[k, pl.ds(0, rows), :]
        east = eta_ref[k, pl.ds(2, rows), :]
        ahead = pltpu.roll(middle, 1, 1)
        behind = pltpu.roll(middle, cols - 1, 1)
        south = jnp.where(first_col, 0.0, jnp.where(forward_roll, ahead, behind))
        north = jnp.where(last_col, 0.0, jnp.where(forward_roll, behind, ahead))
        base_w = 0.5 * (middle + west)
        base_e = 0.5 * (east + middle)
        base_s = 0.5 * (middle + south)
        base_n = 0.5 * (north + middle)
        face_w = weight_x * base_w
        face_e = weight_x * base_e
        face_s = weight_y * base_s
        face_n = weight_y * base_n
        react = re_ref[min(k, re_ref.shape[0] - 1), pl.ds(cut_re, rows), :]
        up = faces_z[k] if k < layers - 1 else 0.0
        down = faces_z[k - 1] if k > 0 else 0.0
        diagonal = face_e + face_w + face_n + face_s
        diagonal = diagonal + (up + down + react)
        if k > 0:
            diagonal = diagonal - faces_z[k - 1] * ratio
        inverse = 1.0 / diagonal
        fxl_ref[k] = base_w
        fxr_ref[k] = base_e
        fyl_ref[k] = base_s
        fyr_ref[k] = base_n
        reo_ref[k] = react
        inv_ref[0, k] = inverse
        if k < layers - 1:
            ratio = faces_z[k] * inverse
            fz_ref[k] = faces_z[k]
            rat_ref[0, k] = ratio


def kernel_operator(eta_level, react_level, level_index, cut_re=0):
    layers, rows_eta, cols = eta_level.shape
    rows = rows_eta - 2
    whole = lambda a: pl.BlockSpec(a.shape, lambda c: (0,) * a.ndim)
    per_part = lambda shape: pl.BlockSpec((1,) + shape, lambda c: (c,) + (0,) * len(shape))
    cell = (layers, rows, cols)
    faces = (layers - 1, rows, cols)
    body = functools.partial(build_kernel, rows=rows, cut_re=cut_re, scale=horizontal_scale / 4.0**level_index)
    shapes = [cell] * 4 + [faces, cell, (2,) + cell, (2,) + faces]
    specs = [pl.BlockSpec(cell, lambda c: (0, 0, 0))] * 4 + [
        pl.BlockSpec(faces, lambda c: (0, 0, 0)),
        pl.BlockSpec(cell, lambda c: (0, 0, 0)),
        per_part(cell),
        per_part(faces),
    ]
    return tuple(
        pl.pallas_call(
            body,
            grid=(2,),
            in_specs=[whole(eta_level), whole(react_level)],
            out_specs=specs,
            out_shape=[jax.ShapeDtypeStruct(s, jnp.float32) for s in shapes],
        )(eta_level, react_level)
    ) + (horizontal_scale / 4.0**level_index,)


def kernel_coarse(target, lanes, mask, turns):
    parts, layers, rows, cols = target.shape
    fxl, fxr, fyl, fyr, fz, re, inv, rat, scale = lanes
    per_part = lambda a: pl.BlockSpec((1,) + a.shape[1:], lambda c: (c,) + (0,) * (a.ndim - 1))
    whole = lambda a: pl.BlockSpec(a.shape, lambda c: (0,) * a.ndim)
    operands = [target, fxl, fxr, fyl, fyr, fz, re, inv, rat, mask]
    specs = [per_part(target), whole(fxl), whole(fxr), whole(fyl), whole(fyr),
             whole(fz), whole(re), per_part(inv), per_part(rat), whole(mask)]
    body = functools.partial(coarse_kernel, rows=rows, turns=turns, scale=scale)
    return pl.pallas_call(
        body,
        grid=(parts,),
        in_specs=specs,
        out_specs=pl.BlockSpec((1, layers, rows, cols), lambda c: (c, 0, 0, 0)),
        out_shape=jax.ShapeDtypeStruct((parts, layers, rows, cols), jnp.float32),
        scratch_shapes=[pltpu.VMEM((1, layers, rows + 16, cols), jnp.float32)],
    )(*operands)


def rows_inside(cells, halo, extent, cols):
    return jnp.broadcast_to(inside(cells, halo, extent)[0, 0], (extent, cols)).astype(jnp.float32)


def shrink(operator, cut):
    if cut == 0:
        return operator
    face_x, face_y, face_z, react_level, inverses, ratios = operator
    rows = face_y.shape[2]
    return (
        face_x[:, :, cut : rows + 1 - cut],
        face_y[:, :, cut : rows - cut],
        face_z[:, cut : rows - cut],
        react_level[:, cut : rows - cut],
        inverses[:, :, cut : rows - cut],
        ratios[:, :, cut : rows - cut],
    )


def apply_operator(field_rim, operator):
    face_x, face_y, face_z, react_level, inverses, ratios = operator
    field = field_rim[:, :, 1:-1, :]
    flux_x = face_x * (field_rim[:, :, 1:, :] - field_rim[:, :, :-1, :])
    result = -(flux_x[:, :, 1:] - flux_x[:, :, :-1])
    padded = jnp.pad(field, ((0, 0), (0, 0), (0, 0), (1, 1)))
    flux_y = face_y * (padded[..., 1:] - padded[..., :-1])
    result = result - (flux_y[..., 1:] - flux_y[..., :-1])
    flux_z = face_z[None] * (field[:, 1:] - field[:, :-1])
    flux_z = jnp.pad(flux_z, ((0, 0), (1, 1), (0, 0), (0, 0)))
    result = result - (flux_z[:, 1:] - flux_z[:, :-1])
    return result + react_level[None] * field


def line_solve(residual, operator):
    face_z, inverses, ratios = (operator[2], operator[4], operator[5])
    layers = residual.shape[1]
    forward = [residual[:, 0] * inverses[:, 0]]
    for layer in range(1, layers):
        forward.append((residual[:, layer] + face_z[layer - 1] * forward[-1]) * inverses[:, layer])
    backward = [forward[-1]]
    for layer in range(layers - 2, -1, -1):
        backward.append(forward[layer] + ratios[:, layer] * backward[-1])
    return jnp.stack(backward[::-1], 1)


def sweep(field_rim, target, operator):
    field = field_rim[:, :, 1:-1, :]
    return field + relax_weight * line_solve(target - apply_operator(field_rim, operator), operator)


def restrict(field):
    return block_mean(field, 2)


def prolong(field):
    cols = field.shape[3]
    spread = (jnp.arange(cols)[:, None] == jnp.arange(2 * cols)[None, :] // 2).astype(jnp.float32)
    wide = jnp.einsum("ckxy,yz->ckxz", field, spread, precision=lax.Precision.HIGHEST)
    return jnp.repeat(wide, 2, axis=2)


def pad_rim(field):
    return jnp.pad(field, ((0, 0), (0, 0), (1, 1), (0, 0)))


def inside(cells, halo, extent):
    count = lax.axis_size("gx")
    first = lax.axis_index("gx") * cells - halo
    index = first + jnp.arange(extent)
    return ((index >= 0) & (index < count * cells)).reshape(1, 1, extent, 1)


def keep_inside(field, cells, halo):
    return jnp.where(inside(cells, halo, field.shape[2]), field, 0.0)


def window(full, dim, start, size, pad):
    widths = [(0, 0)] * full.ndim
    widths[dim] = (pad, pad)
    return lax.dynamic_slice_in_dim(jnp.pad(full, widths), start, size, axis=dim)


def nearby(cells, dim, hops):
    count = lax.axis_size("gx")
    lows = []
    highs = []
    for step in range(1, hops + 1):
        lows.insert(0, lax.ppermute(cells, "gx", [(i, i + step) for i in range(count - step)]))
        highs.append(lax.ppermute(cells, "gx", [(i + step, i) for i in range(count - step)]))
    return jnp.concatenate(lows + [cells] + highs, axis=dim)


def shards(misfit, adjoint_guess, viscosity, friction, ice_mask, forward_bed):
    layers, cells, cols = viscosity.shape
    where = lax.axis_index("gx")
    react_fine = reaction_field(friction, ice_mask, layers)
    react_pair = react_fine[:2]

    eta_1 = block_mean(viscosity, 2)
    react_1 = block_mean(react_pair, 2)
    pieces = [eta_1, react_1]
    packed = jnp.concatenate([p.reshape(-1) for p in pieces])
    gathered = lax.all_gather(packed[None], "gx", axis=0, tiled=True)
    count = gathered.shape[0]
    unpacked = []
    offset = 0
    for p in pieces:
        block = gathered[:, offset : offset + p.size].reshape((count,) + p.shape)
        offset += p.size
        unpacked.append(jnp.moveaxis(block, 0, 1).reshape((p.shape[0], count * p.shape[1], p.shape[2])))
    eta_1_all, react_1_all = unpacked
    eta_2_all = block_mean(eta_1_all, 2)
    react_2_all = block_mean(react_1_all, 2)

    halo = 4
    eta_wide, guess_wide, misfit_wide, react_wide = trade(
        [(viscosity, 1), (adjoint_guess, 2), (misfit, 2), (react_pair, 1)], halo
    )
    op_0 = kernel_operator(eta_wide, react_wide, 0, 1)
    fine = kernel_sweep(guess_wide, misfit_wide, op_0, 1, 0, rows_inside(cells, 3, cells + 6, cols))
    fine, residual = kernel_sweep(
        fine, misfit_wide, op_0, 2, 1, rows_inside(cells, 2, cells + 4, cols), then=(1, cells, 4, 3)
    )
    middle_rhs = restrict(residual)

    half = cells // 2
    wide = cols // 2
    rhs_wide = with_halo(middle_rhs, (("gx", 2),), half)
    eta_1_wide = window(eta_1_all, 1, where * half, 3 * half + 2, half + 1)
    react_1_wide = window(react_1_all, 1, where * half, 3 * half, half)
    op_1 = kernel_operator(eta_1_wide, react_1_wide, 1)
    middle = kernel_sweep(rhs_wide, rhs_wide, op_1, 0, 0, rows_inside(half, half, 3 * half, wide), "zero", 0, 3 * half)
    middle, residual = kernel_sweep(
        middle, rhs_wide, op_1, 1, 1, rows_inside(half, half - 1, 3 * half - 2, wide), then=(half - 2, half, half, half)
    )
    coarse_rhs = restrict(residual)

    quarter = cells // 4
    narrow = cols // 4
    reach = 3
    span = reach + COARSE_SWEEPS - 1
    coarse_rhs_near = nearby(coarse_rhs, 2, span // quarter)
    eta_2_near = window(eta_2_all, 1, where * quarter, quarter + 2 * span + 2, span + 1)
    react_2_near = window(react_2_all, 1, where * quarter, quarter + 2 * span, span)
    op_2 = kernel_operator(eta_2_near, react_2_near, 2)
    extent = quarter + 2 * span
    coarse_mask = rows_inside(quarter, span, extent, narrow)
    coarse = kernel_coarse(coarse_rhs_near, op_2, coarse_mask, COARSE_SWEEPS)
    coarse_near = coarse[:, :, span - reach : span + quarter + reach]

    lift = prolong(coarse_near)
    trim = 2 * reach - (half - 1)
    middle = middle + lift[:, :, trim : lift.shape[2] - trim]
    middle = kernel_sweep(middle, rhs_wide, op_1, 2, 2, rows_inside(half, half - 2, 3 * half - 4, wide))
    middle = kernel_sweep(middle, rhs_wide, op_1, 3, 3, rows_inside(half, half - 3, 3 * half - 6, wide))
    fine = fine + prolong(middle)
    fine = kernel_sweep(fine, misfit_wide, op_0, 3, 2, rows_inside(cells, 1, cells + 2, cols))
    fine = kernel_sweep(fine, misfit_wide, op_0, 4, 3, rows_inside(cells, 0, cells, cols))
    grounded = (ice_mask == 2).astype(jnp.float32)
    gradient = -grounded * (forward_bed[0] * fine[0, 0] + forward_bed[1] * fine[1, 0])
    return (fine, gradient)


def solution(mesh):
    placed = (
        P("ens", None, "gx", None),
        P("ens", None, "gx", None),
        P("ens", "gx", None),
        P("gx", "ens"),
        P("gx", "ens"),
        P("ens", "gx", None),
    )
    return jax.shard_map(
        shards,
        mesh=mesh,
        in_specs=placed,
        out_specs=(P("ens", None, "gx", None), P("gx", "ens")),
        check_vma=False,
    )
```

```python
import functools

import jax
import jax.numpy as jnp
from jax import lax
from jax.experimental import pallas as pl
from jax.experimental.pallas import tpu as pltpu
from jax.sharding import PartitionSpec as P

NU = 2
COARSE_SWEEPS = 6


horizontal_scale = 1.0
vertical_scale = 4.0
relax_weight = 0.8


def with_halo(cells, sides, width):
    for axis, dim in sides:
        count = lax.axis_size(axis)
        ends = count - 1
        head = lax.slice_in_dim(cells, 0, width, axis=dim)
        tail = lax.slice_in_dim(cells, cells.shape[dim] - width, cells.shape[dim], axis=dim)
        cells = jnp.concatenate(
            [
                lax.ppermute(tail, axis, [(i, (i + 1) % count) for i in range(ends)]),
                cells,
                lax.ppermute(head, axis, [((i + 1) % count, i) for i in range(ends)]),
            ],
            axis=dim,
        )
    return cells


def trade(parts, width):
    count = lax.axis_size("gx")
    ends = count - 1
    heads = [lax.slice_in_dim(a, 0, width, axis=dim) for a, dim in parts]
    tails = [lax.slice_in_dim(a, a.shape[dim] - width, a.shape[dim], axis=dim) for a, dim in parts]
    pack = lambda pieces: jnp.concatenate([p.reshape(-1) for p in pieces])
    from_left = lax.ppermute(pack(tails), "gx", [(i, i + 1) for i in range(ends)])
    from_right = lax.ppermute(pack(heads), "gx", [(i + 1, i) for i in range(ends)])
    out = []
    offset = 0
    for (a, dim), h in zip(parts, heads):
        size = h.size
        left = from_left[offset : offset + size].reshape(h.shape)
        right = from_right[offset : offset + size].reshape(h.shape)
        offset += size
        out.append(jnp.concatenate([left, a, right], axis=dim))
    return out


def block_mean(field, factor):
    while factor > 1:
        lead = field.shape[:-2]
        rows, cols = (field.shape[-2], field.shape[-1])
        pairs = (jnp.arange(cols)[:, None] // 2 == jnp.arange(cols // 2)[None, :]).astype(jnp.float32)
        field = jnp.einsum("...y,yz->...z", field, pairs, precision=lax.Precision.HIGHEST)
        field = 0.25 * field.reshape(lead + (rows // 2, 2, cols // 2)).sum(axis=-2)
        factor //= 2
    return field


def reaction_field(friction, ice_mask, layers):
    open_water = (ice_mask == 0).astype(jnp.float32)
    grounded = (ice_mask == 2).astype(jnp.float32)
    bottom = (jnp.arange(layers) == 0).astype(jnp.float32).reshape(layers, 1, 1)
    return 0.02 + 2.0 * open_water[None] + bottom * (grounded * friction)[None]


def build_operator(eta_level, react_level, level_index):
    scale = horizontal_scale / 4.0**level_index
    weight_x = jnp.array([4.0, 1.0], jnp.float32).reshape(2, 1, 1, 1) * scale
    weight_y = jnp.array([1.0, 4.0], jnp.float32).reshape(2, 1, 1, 1) * scale
    inner = eta_level[:, 1:-1, :]
    face_x = weight_x * (0.5 * (eta_level[:, 1:, :] + eta_level[:, :-1, :]))[None]
    padded = jnp.pad(inner, ((0, 0), (0, 0), (1, 1)))
    face_y = weight_y * (0.5 * (padded[:, :, 1:] + padded[:, :, :-1]))[None]
    face_z = vertical_scale * 0.5 * (inner[1:] + inner[:-1])
    vertical = jnp.pad(face_z, ((1, 1), (0, 0), (0, 0)))
    diagonal = face_x[:, :, 1:] + face_x[:, :, :-1] + face_y[..., 1:] + face_y[..., :-1]
    diagonal = diagonal + (vertical[1:] + vertical[:-1] + react_level)[None]
    layers = diagonal.shape[1]
    inverses = []
    ratios = []
    for layer in range(layers):
        pivot = diagonal[:, layer]
        if layer > 0:
            pivot = pivot - face_z[layer - 1] * ratios[-1]
        inverse = 1.0 / pivot
        inverses.append(inverse)
        if layer < layers - 1:
            ratios.append(face_z[layer] * inverse)
    return (face_x, face_y, face_z, react_level, jnp.stack(inverses, 1), jnp.stack(ratios, 1))


def lane_ops(operator):
    face_x, face_y, face_z, react_level, inverses, ratios = operator
    return (face_x[:, :, :-1], face_x[:, :, 1:], face_y[..., :-1], face_y[..., 1:], face_z, react_level, inverses, ratios)


def sweep_kernel(w_ref, b_ref, fxl_ref, fxr_ref, fyl_ref, fyr_ref, fz_ref, re_ref, inv_ref, rat_ref, mask_ref, *more,
                 rows, cut_w, cut_b, cut_op, mode, scale, then):
    lanes = (fxl_ref, fxr_ref, fyl_ref, fyr_ref, fz_ref, re_ref, inv_ref, rat_ref, scale)
    out_ref = more[-2] if then is not None else more[-1]
    relax(w_ref, b_ref, lanes, mask_ref, out_ref, rows=rows, cut_w=cut_w, cut_b=cut_b, cut_op=cut_op, mode=mode)
    if then is not None:
        next_cut_w, next_rows, next_cut_b, next_cut_op, next_mode = then
        relax(out_ref, b_ref, lanes, more[0], more[-1], rows=next_rows, cut_w=next_cut_w, cut_b=next_cut_b,
              cut_op=next_cut_op, mode=next_mode)


def coarse_kernel(b_ref, fxl_ref, fxr_ref, fyl_ref, fyr_ref, fz_ref, re_ref, inv_ref, rat_ref, mask_ref, out_ref, w_ref,
                  *, rows, turns, scale):
    lanes = (fxl_ref, fxr_ref, fyl_ref, fyr_ref, fz_ref, re_ref, inv_ref, rat_ref, scale)
    w_ref[...] = jnp.zeros(w_ref.shape, jnp.float32)
    for turn in range(turns):
        relax(w_ref, b_ref, lanes, mask_ref, out_ref, rows=rows, cut_w=7, cut_b=0, cut_op=0, mode="sweep")
        if turn < turns - 1:
            for k in range(out_ref.shape[1]):
                w_ref[0, k, pl.ds(8, rows), :] = out_ref[0, k]


def relax(w_ref, b_ref, lanes, mask_ref, out_ref, *, rows, cut_w, cut_b, cut_op, mode):
    fxl_ref, fxr_ref, fyl_ref, fyr_ref, fz_ref, re_ref, inv_ref, rat_ref, scale = lanes
    layers = out_ref.shape[1]
    cols = out_ref.shape[3]
    lane = lax.broadcasted_iota(jnp.int32, (rows, cols), 1)
    probe = pltpu.roll(lane, 1, 1)
    forward_roll = probe == jnp.where(lane == 0, cols - 1, lane - 1)
    first_col = lane == 0
    last_col = lane == cols - 1

    def cell(ref, k, cut):
        return ref[0, k, pl.ds(cut, rows), :]

    component = pl.program_id(0)
    weight_x = jnp.where(component == 0, 4.0, 1.0) * scale
    weight_y = jnp.where(component == 0, 1.0, 4.0) * scale

    def face(ref, weight, k):
        return weight * ref[k, pl.ds(cut_op, rows), :]

    def field(k):
        return w_ref[0, k, pl.ds(cut_w + 1, rows), :]

    def applied(k):
        w = field(k)
        west = w_ref[0, k, pl.ds(cut_w, rows), :]
        east = w_ref[0, k, pl.ds(cut_w + 2, rows), :]
        result = -(face(fxr_ref, weight_x, k) * (east - w) - face(fxl_ref, weight_x, k) * (w - west))
        ahead = pltpu.roll(w, 1, 1)
        behind = pltpu.roll(w, cols - 1, 1)
        south = jnp.where(forward_roll, ahead, behind)
        north = jnp.where(forward_roll, behind, ahead)
        south = jnp.where(first_col, 0.0, south)
        north = jnp.where(last_col, 0.0, north)
        result = result - (face(fyr_ref, weight_y, k) * (north - w) - face(fyl_ref, weight_y, k) * (w - south))
        up = fz_ref[k, pl.ds(cut_op, rows), :] * (field(k + 1) - w) if k < layers - 1 else 0.0
        down = fz_ref[k - 1, pl.ds(cut_op, rows), :] * (w - field(k - 1)) if k > 0 else 0.0
        result = result - (up - down)
        return result + re_ref[k, pl.ds(cut_op, rows), :] * w

    if mode == "residual":
        for k in range(layers):
            out_ref[0, k] = cell(b_ref, k, cut_b) - applied(k)
        return
    keep = mask_ref[...] > 0.5
    previous = None
    for k in range(layers):
        residual = cell(b_ref, k, cut_b)
        if mode == "sweep":
            residual = residual - applied(k)
        if k == 0:
            forward = residual * cell(inv_ref, 0, cut_op)
        else:
            forward = (residual + fz_ref[k - 1, pl.ds(cut_op, rows), :] * previous) * cell(inv_ref, k, cut_op)
        out_ref[0, k] = forward
        previous = forward
    back = previous
    for k in range(layers - 1, -1, -1):
        if k < layers - 1:
            back = out_ref[0, k] + rat_ref[0, k, pl.ds(cut_op, rows), :] * back
        if mode == "sweep":
            value = field(k) + relax_weight * back
        else:
            value = relax_weight * back
        out_ref[0, k] = jnp.where(keep, value, 0.0)


def kernel_sweep(field_rim, target, lanes, cut_b, cut_op, mask, mode="sweep", cut_w=0, rows=None, then=None,
                 next_mask=None):
    parts, layers, rows_rim, cols = field_rim.shape
    rows = rows_rim - 2 if rows is None else rows
    fxl, fxr, fyl, fyr, fz, re, inv, rat, scale = lanes
    per_part = lambda a: pl.BlockSpec((1,) + a.shape[1:], lambda c: (c,) + (0,) * (a.ndim - 1))
    whole = lambda a: pl.BlockSpec(a.shape, lambda c: (0,) * a.ndim)
    operands = [field_rim, target, fxl, fxr, fyl, fyr, fz, re, inv, rat, mask]
    specs = [per_part(field_rim), per_part(target), whole(fxl), whole(fxr), whole(fyl), whole(fyr),
             whole(fz), whole(re), per_part(inv), per_part(rat), whole(mask)]
    if then is not None:
        next_mask = mask if next_mask is None else next_mask
        operands.append(next_mask)
        specs.append(whole(next_mask))
    body = functools.partial(
        sweep_kernel, rows=rows, cut_w=cut_w, cut_b=cut_b, cut_op=cut_op, mode=mode, scale=scale, then=then
    )
    out_specs = [pl.BlockSpec((1, layers, rows, cols), lambda c: (c, 0, 0, 0))]
    out_shape = [jax.ShapeDtypeStruct((parts, layers, rows, cols), jnp.float32)]
    if then is not None:
        out_specs.append(pl.BlockSpec((1, layers, then[1], cols), lambda c: (c, 0, 0, 0)))
        out_shape.append(jax.ShapeDtypeStruct((parts, layers, then[1], cols), jnp.float32))
    outs = pl.pallas_call(body, grid=(parts,), in_specs=specs, out_specs=out_specs, out_shape=out_shape)(*operands)
    return tuple(outs) if then is not None else outs[0]


def build_kernel(eta_ref, re_ref, fxl_ref, fxr_ref, fyl_ref, fyr_ref, fz_ref, reo_ref, inv_ref, rat_ref,
                 *, rows, cut_re, scale):
    component = pl.program_id(0)
    layers = eta_ref.shape[0]
    cols = eta_ref.shape[2]
    lane = lax.broadcasted_iota(jnp.int32, (rows, cols), 1)
    probe = pltpu.roll(lane, 1, 1)
    forward_roll = probe == jnp.where(lane == 0, cols - 1, lane - 1)
    first_col = lane == 0
    last_col = lane == cols - 1
    weight_x = jnp.where(component == 0, 4.0, 1.0) * scale
    weight_y = jnp.where(component == 0, 1.0, 4.0) * scale

    def inner(k):
        return eta_ref[k, pl.ds(1, rows), :]

    faces_z = [vertical_scale * 0.5 * (inner(k + 1) + inner(k)) for k in range(layers - 1)]
    ratio = None
    for k in range(layers):
        middle = inner(k)
        west = eta_ref[k, pl.ds(0, rows), :]
        east = eta_ref[k, pl.ds(2, rows), :]
        ahead = pltpu.roll(middle, 1, 1)
        behind = pltpu.roll(middle, cols - 1, 1)
        south = jnp.where(first_col, 0.0, jnp.where(forward_roll, ahead, behind))
        north = jnp.where(last_col, 0.0, jnp.where(forward_roll, behind, ahead))
        base_w = 0.5 * (middle + west)
        base_e = 0.5 * (east + middle)
        base_s = 0.5 * (middle + south)
        base_n = 0.5 * (north + middle)
        face_w = weight_x * base_w
        face_e = weight_x * base_e
        face_s = weight_y * base_s
        face_n = weight_y * base_n
        react = re_ref[min(k, re_ref.shape[0] - 1), pl.ds(cut_re, rows), :]
        up = faces_z[k] if k < layers - 1 else 0.0
        down = faces_z[k - 1] if k > 0 else 0.0
        diagonal = face_e + face_w + face_n + face_s
        diagonal = diagonal + (up + down + react)
        if k > 0:
            diagonal = diagonal - faces_z[k - 1] * ratio
        inverse = 1.0 / diagonal
        fxl_ref[k] = base_w
        fxr_ref[k] = base_e
        fyl_ref[k] = base_s
        fyr_ref[k] = base_n
        reo_ref[k] = react
        inv_ref[0, k] = inverse
        if k < layers - 1:
            ratio = faces_z[k] * inverse
            fz_ref[k] = faces_z[k]
            rat_ref[0, k] = ratio


def kernel_operator(eta_level, react_level, level_index, cut_re=0):
    layers, rows_eta, cols = eta_level.shape
    rows = rows_eta - 2
    whole = lambda a: pl.BlockSpec(a.shape, lambda c: (0,) * a.ndim)
    per_part = lambda shape: pl.BlockSpec((1,) + shape, lambda c: (c,) + (0,) * len(shape))
    cell = (layers, rows, cols)
    faces = (layers - 1, rows, cols)
    body = functools.partial(build_kernel, rows=rows, cut_re=cut_re, scale=horizontal_scale / 4.0**level_index)
    shapes = [cell] * 4 + [faces, cell, (2,) + cell, (2,) + faces]
    specs = [pl.BlockSpec(cell, lambda c: (0, 0, 0))] * 4 + [
        pl.BlockSpec(faces, lambda c: (0, 0, 0)),
        pl.BlockSpec(cell, lambda c: (0, 0, 0)),
        per_part(cell),
        per_part(faces),
    ]
    return tuple(
        pl.pallas_call(
            body,
            grid=(2,),
            in_specs=[whole(eta_level), whole(react_level)],
            out_specs=specs,
            out_shape=[jax.ShapeDtypeStruct(s, jnp.float32) for s in shapes],
        )(eta_level, react_level)
    ) + (horizontal_scale / 4.0**level_index,)


def kernel_coarse(target, lanes, mask, turns):
    parts, layers, rows, cols = target.shape
    fxl, fxr, fyl, fyr, fz, re, inv, rat, scale = lanes
    per_part = lambda a: pl.BlockSpec((1,) + a.shape[1:], lambda c: (c,) + (0,) * (a.ndim - 1))
    whole = lambda a: pl.BlockSpec(a.shape, lambda c: (0,) * a.ndim)
    operands = [target, fxl, fxr, fyl, fyr, fz, re, inv, rat, mask]
    specs = [per_part(target), whole(fxl), whole(fxr), whole(fyl), whole(fyr),
             whole(fz), whole(re), per_part(inv), per_part(rat), whole(mask)]
    body = functools.partial(coarse_kernel, rows=rows, turns=turns, scale=scale)
    return pl.pallas_call(
        body,
        grid=(parts,),
        in_specs=specs,
        out_specs=pl.BlockSpec((1, layers, rows, cols), lambda c: (c, 0, 0, 0)),
        out_shape=jax.ShapeDtypeStruct((parts, layers, rows, cols), jnp.float32),
        scratch_shapes=[pltpu.VMEM((1, layers, rows + 16, cols), jnp.float32)],
    )(*operands)


def rows_inside(cells, halo, extent, cols):
    return jnp.broadcast_to(inside(cells, halo, extent)[0, 0], (extent, cols)).astype(jnp.float32)


def shrink(operator, cut):
    if cut == 0:
        return operator
    face_x, face_y, face_z, react_level, inverses, ratios = operator
    rows = face_y.shape[2]
    return (
        face_x[:, :, cut : rows + 1 - cut],
        face_y[:, :, cut : rows - cut],
        face_z[:, cut : rows - cut],
        react_level[:, cut : rows - cut],
        inverses[:, :, cut : rows - cut],
        ratios[:, :, cut : rows - cut],
    )


def apply_operator(field_rim, operator):
    face_x, face_y, face_z, react_level, inverses, ratios = operator
    field = field_rim[:, :, 1:-1, :]
    flux_x = face_x * (field_rim[:, :, 1:, :] - field_rim[:, :, :-1, :])
    result = -(flux_x[:, :, 1:] - flux_x[:, :, :-1])
    padded = jnp.pad(field, ((0, 0), (0, 0), (0, 0), (1, 1)))
    flux_y = face_y * (padded[..., 1:] - padded[..., :-1])
    result = result - (flux_y[..., 1:] - flux_y[..., :-1])
    flux_z = face_z[None] * (field[:, 1:] - field[:, :-1])
    flux_z = jnp.pad(flux_z, ((0, 0), (1, 1), (0, 0), (0, 0)))
    result = result - (flux_z[:, 1:] - flux_z[:, :-1])
    return result + react_level[None] * field


def line_solve(residual, operator):
    face_z, inverses, ratios = (operator[2], operator[4], operator[5])
    layers = residual.shape[1]
    forward = [residual[:, 0] * inverses[:, 0]]
    for layer in range(1, layers):
        forward.append((residual[:, layer] + face_z[layer - 1] * forward[-1]) * inverses[:, layer])
    backward = [forward[-1]]
    for layer in range(layers - 2, -1, -1):
        backward.append(forward[layer] + ratios[:, layer] * backward[-1])
    return jnp.stack(backward[::-1], 1)


def sweep(field_rim, target, operator):
    field = field_rim[:, :, 1:-1, :]
    return field + relax_weight * line_solve(target - apply_operator(field_rim, operator), operator)


def restrict(field):
    return block_mean(field, 2)


def prolong(field):
    cols = field.shape[3]
    spread = (jnp.arange(cols)[:, None] == jnp.arange(2 * cols)[None, :] // 2).astype(jnp.float32)
    wide = jnp.einsum("ckxy,yz->ckxz", field, spread, precision=lax.Precision.HIGHEST)
    return jnp.repeat(wide, 2, axis=2)


def pad_rim(field):
    return jnp.pad(field, ((0, 0), (0, 0), (1, 1), (0, 0)))


def inside(cells, halo, extent):
    count = lax.axis_size("gx")
    first = lax.axis_index("gx") * cells - halo
    index = first + jnp.arange(extent)
    return ((index >= 0) & (index < count * cells)).reshape(1, 1, extent, 1)


def keep_inside(field, cells, halo):
    return jnp.where(inside(cells, halo, field.shape[2]), field, 0.0)


def window(full, dim, start, size, pad):
    widths = [(0, 0)] * full.ndim
    widths[dim] = (pad, pad)
    return lax.dynamic_slice_in_dim(jnp.pad(full, widths), start, size, axis=dim)


def nearby(cells, dim, hops):
    count = lax.axis_size("gx")
    lows = []
    highs = []
    for step in range(1, hops + 1):
        lows.insert(0, lax.ppermute(cells, "gx", [(i, i + step) for i in range(count - step)]))
        highs.append(lax.ppermute(cells, "gx", [(i + step, i) for i in range(count - step)]))
    return jnp.concatenate(lows + [cells] + highs, axis=dim)


def shards(misfit, adjoint_guess, viscosity, friction, ice_mask, forward_bed):
    layers, cells, cols = viscosity.shape
    where = lax.axis_index("gx")
    react_fine = reaction_field(friction, ice_mask, layers)
    react_pair = react_fine[:2]

    eta_1 = block_mean(viscosity, 2)
    react_1 = block_mean(react_pair, 2)
    pieces = [eta_1, react_1]
    packed = jnp.concatenate([p.reshape(-1) for p in pieces])
    gathered = lax.all_gather(packed[None], "gx", axis=0, tiled=True)
    count = gathered.shape[0]
    unpacked = []
    offset = 0
    for p in pieces:
        block = gathered[:, offset : offset + p.size].reshape((count,) + p.shape)
        offset += p.size
        unpacked.append(jnp.moveaxis(block, 0, 1).reshape((p.shape[0], count * p.shape[1], p.shape[2])))
    eta_1_all, react_1_all = unpacked
    eta_2_all = block_mean(eta_1_all, 2)
    react_2_all = block_mean(react_1_all, 2)

    halo = 4
    eta_wide, guess_wide, misfit_wide, react_wide = trade(
        [(viscosity, 1), (adjoint_guess, 2), (misfit, 2), (react_pair, 1)], halo
    )
    op_0 = kernel_operator(eta_wide, react_wide, 0, 1)
    fine = kernel_sweep(guess_wide, misfit_wide, op_0, 1, 0, rows_inside(cells, 3, cells + 6, cols))
    fine, residual = kernel_sweep(
        fine, misfit_wide, op_0, 2, 1, rows_inside(cells, 2, cells + 4, cols), then=(1, cells, 4, 3, "residual")
    )
    middle_rhs = restrict(residual)

    half = cells // 2
    wide = cols // 2
    rhs_wide = with_halo(middle_rhs, (("gx", 2),), half)
    eta_1_wide = window(eta_1_all, 1, where * half, 3 * half + 2, half + 1)
    react_1_wide = window(react_1_all, 1, where * half, 3 * half, half)
    op_1 = kernel_operator(eta_1_wide, react_1_wide, 1)
    middle = kernel_sweep(rhs_wide, rhs_wide, op_1, 0, 0, rows_inside(half, half, 3 * half, wide), "zero", 0, 3 * half)
    middle, residual = kernel_sweep(
        middle, rhs_wide, op_1, 1, 1, rows_inside(half, half - 1, 3 * half - 2, wide), then=(half - 2, half, half, half, "residual")
    )
    coarse_rhs = restrict(residual)

    quarter = cells // 4
    narrow = cols // 4
    reach = 3
    span = reach + COARSE_SWEEPS - 1
    coarse_rhs_near = nearby(coarse_rhs, 2, span // quarter)
    eta_2_near = window(eta_2_all, 1, where * quarter, quarter + 2 * span + 2, span + 1)
    react_2_near = window(react_2_all, 1, where * quarter, quarter + 2 * span, span)
    op_2 = kernel_operator(eta_2_near, react_2_near, 2)
    extent = quarter + 2 * span
    coarse_mask = rows_inside(quarter, span, extent, narrow)
    coarse = kernel_coarse(coarse_rhs_near, op_2, coarse_mask, COARSE_SWEEPS)
    coarse_near = coarse[:, :, span - reach : span + quarter + reach]

    lift = prolong(coarse_near)
    trim = 2 * reach - (half - 1)
    middle = middle + lift[:, :, trim : lift.shape[2] - trim]
    middle = kernel_sweep(
        middle, rhs_wide, op_1, 2, 2, rows_inside(half, half - 2, 3 * half - 4, wide),
        then=(0, 3 * half - 6, 3, 3, "sweep"), next_mask=rows_inside(half, half - 3, 3 * half - 6, wide),
    )[1]
    fine = fine + prolong(middle)
    fine = kernel_sweep(
        fine, misfit_wide, op_0, 3, 2, rows_inside(cells, 1, cells + 2, cols),
        then=(0, cells, 4, 3, "sweep"), next_mask=rows_inside(cells, 0, cells, cols),
    )[1]
    grounded = (ice_mask == 2).astype(jnp.float32)
    gradient = -grounded * (forward_bed[0] * fine[0, 0] + forward_bed[1] * fine[1, 0])
    return (fine, gradient)


def solution(mesh):
    placed = (
        P("ens", None, "gx", None),
        P("ens", None, "gx", None),
        P("ens", "gx", None),
        P("gx", "ens"),
        P("gx", "ens"),
        P("ens", "gx", None),
    )
    return jax.shard_map(
        shards,
        mesh=mesh,
        in_specs=placed,
        out_specs=(P("ens", None, "gx", None), P("gx", "ens")),
        check_vma=False,
    )
```

```python
import functools

import jax
import jax.numpy as jnp
from jax import lax
from jax.experimental import pallas as pl
from jax.experimental.pallas import tpu as pltpu
from jax.sharding import PartitionSpec as P

NU = 2
COARSE_SWEEPS = 6


horizontal_scale = 1.0
vertical_scale = 4.0
relax_weight = 0.8


def with_halo(cells, sides, width):
    for axis, dim in sides:
        count = lax.axis_size(axis)
        ends = count - 1
        head = lax.slice_in_dim(cells, 0, width, axis=dim)
        tail = lax.slice_in_dim(cells, cells.shape[dim] - width, cells.shape[dim], axis=dim)
        cells = jnp.concatenate(
            [
                lax.ppermute(tail, axis, [(i, (i + 1) % count) for i in range(ends)]),
                cells,
                lax.ppermute(head, axis, [((i + 1) % count, i) for i in range(ends)]),
            ],
            axis=dim,
        )
    return cells


def trade(parts, width):
    count = lax.axis_size("gx")
    ends = count - 1
    heads = [lax.slice_in_dim(a, 0, width, axis=dim) for a, dim in parts]
    tails = [lax.slice_in_dim(a, a.shape[dim] - width, a.shape[dim], axis=dim) for a, dim in parts]
    pack = lambda pieces: jnp.concatenate([p.reshape(-1) for p in pieces])
    from_left = lax.ppermute(pack(tails), "gx", [(i, i + 1) for i in range(ends)])
    from_right = lax.ppermute(pack(heads), "gx", [(i + 1, i) for i in range(ends)])
    out = []
    offset = 0
    for (a, dim), h in zip(parts, heads):
        size = h.size
        left = from_left[offset : offset + size].reshape(h.shape)
        right = from_right[offset : offset + size].reshape(h.shape)
        offset += size
        out.append(jnp.concatenate([left, a, right], axis=dim))
    return out


def block_mean(field, factor):
    while factor > 1:
        lead = field.shape[:-2]
        rows, cols = (field.shape[-2], field.shape[-1])
        pairs = (jnp.arange(cols)[:, None] // 2 == jnp.arange(cols // 2)[None, :]).astype(jnp.float32)
        field = jnp.einsum("...y,yz->...z", field, pairs, precision=lax.Precision.HIGHEST)
        field = 0.25 * field.reshape(lead + (rows // 2, 2, cols // 2)).sum(axis=-2)
        factor //= 2
    return field


def reaction_field(friction, ice_mask, layers):
    open_water = (ice_mask == 0).astype(jnp.float32)
    grounded = (ice_mask == 2).astype(jnp.float32)
    bottom = (jnp.arange(layers) == 0).astype(jnp.float32).reshape(layers, 1, 1)
    return 0.02 + 2.0 * open_water[None] + bottom * (grounded * friction)[None]


def build_operator(eta_level, react_level, level_index):
    scale = horizontal_scale / 4.0**level_index
    weight_x = jnp.array([4.0, 1.0], jnp.float32).reshape(2, 1, 1, 1) * scale
    weight_y = jnp.array([1.0, 4.0], jnp.float32).reshape(2, 1, 1, 1) * scale
    inner = eta_level[:, 1:-1, :]
    face_x = weight_x * (0.5 * (eta_level[:, 1:, :] + eta_level[:, :-1, :]))[None]
    padded = jnp.pad(inner, ((0, 0), (0, 0), (1, 1)))
    face_y = weight_y * (0.5 * (padded[:, :, 1:] + padded[:, :, :-1]))[None]
    face_z = vertical_scale * 0.5 * (inner[1:] + inner[:-1])
    vertical = jnp.pad(face_z, ((1, 1), (0, 0), (0, 0)))
    diagonal = face_x[:, :, 1:] + face_x[:, :, :-1] + face_y[..., 1:] + face_y[..., :-1]
    diagonal = diagonal + (vertical[1:] + vertical[:-1] + react_level)[None]
    layers = diagonal.shape[1]
    inverses = []
    ratios = []
    for layer in range(layers):
        pivot = diagonal[:, layer]
        if layer > 0:
            pivot = pivot - face_z[layer - 1] * ratios[-1]
        inverse = 1.0 / pivot
        inverses.append(inverse)
        if layer < layers - 1:
            ratios.append(face_z[layer] * inverse)
    return (face_x, face_y, face_z, react_level, jnp.stack(inverses, 1), jnp.stack(ratios, 1))


def lane_ops(operator):
    face_x, face_y, face_z, react_level, inverses, ratios = operator
    return (face_x[:, :, :-1], face_x[:, :, 1:], face_y[..., :-1], face_y[..., 1:], face_z, react_level, inverses, ratios)


def sweep_kernel(w_ref, b_ref, fxl_ref, fxr_ref, fyl_ref, fyr_ref, fz_ref, re_ref, inv_ref, rat_ref, mask_ref, *more,
                 rows, cut_w, cut_b, cut_op, mode, scale, then):
    lanes = (fxl_ref, fxr_ref, fyl_ref, fyr_ref, fz_ref, re_ref, inv_ref, rat_ref, scale)
    steps = len(then)
    masks, outs = more[:steps], more[steps:]
    relax(w_ref, b_ref, lanes, mask_ref, outs[0], rows=rows, cut_w=cut_w, cut_b=cut_b, cut_op=cut_op, mode=mode)
    for step, (next_cut_w, next_rows, next_cut_b, next_cut_op, next_mode) in enumerate(then):
        relax(outs[step], b_ref, lanes, masks[step], outs[step + 1], rows=next_rows, cut_w=next_cut_w,
              cut_b=next_cut_b, cut_op=next_cut_op, mode=next_mode)


def coarse_kernel(b_ref, fxl_ref, fxr_ref, fyl_ref, fyr_ref, fz_ref, re_ref, inv_ref, rat_ref, mask_ref, out_ref, w_ref,
                  *, rows, turns, scale):
    lanes = (fxl_ref, fxr_ref, fyl_ref, fyr_ref, fz_ref, re_ref, inv_ref, rat_ref, scale)
    w_ref[...] = jnp.zeros(w_ref.shape, jnp.float32)
    for turn in range(turns):
        relax(w_ref, b_ref, lanes, mask_ref, out_ref, rows=rows, cut_w=7, cut_b=0, cut_op=0, mode="sweep")
        if turn < turns - 1:
            for k in range(out_ref.shape[1]):
                w_ref[0, k, pl.ds(8, rows), :] = out_ref[0, k]


def relax(w_ref, b_ref, lanes, mask_ref, out_ref, *, rows, cut_w, cut_b, cut_op, mode):
    fxl_ref, fxr_ref, fyl_ref, fyr_ref, fz_ref, re_ref, inv_ref, rat_ref, scale = lanes
    layers = out_ref.shape[1]
    cols = out_ref.shape[3]
    lane = lax.broadcasted_iota(jnp.int32, (rows, cols), 1)
    probe = pltpu.roll(lane, 1, 1)
    forward_roll = probe == jnp.where(lane == 0, cols - 1, lane - 1)
    first_col = lane == 0
    last_col = lane == cols - 1

    def cell(ref, k, cut):
        return ref[0, k, pl.ds(cut, rows), :]

    component = pl.program_id(0)
    weight_x = jnp.where(component == 0, 4.0, 1.0) * scale
    weight_y = jnp.where(component == 0, 1.0, 4.0) * scale

    def face(ref, weight, k):
        return weight * ref[k, pl.ds(cut_op, rows), :]

    def field(k):
        return w_ref[0, k, pl.ds(cut_w + 1, rows), :]

    def applied(k):
        w = field(k)
        west = w_ref[0, k, pl.ds(cut_w, rows), :]
        east = w_ref[0, k, pl.ds(cut_w + 2, rows), :]
        result = -(face(fxr_ref, weight_x, k) * (east - w) - face(fxl_ref, weight_x, k) * (w - west))
        ahead = pltpu.roll(w, 1, 1)
        behind = pltpu.roll(w, cols - 1, 1)
        south = jnp.where(forward_roll, ahead, behind)
        north = jnp.where(forward_roll, behind, ahead)
        south = jnp.where(first_col, 0.0, south)
        north = jnp.where(last_col, 0.0, north)
        result = result - (face(fyr_ref, weight_y, k) * (north - w) - face(fyl_ref, weight_y, k) * (w - south))
        up = fz_ref[k, pl.ds(cut_op, rows), :] * (field(k + 1) - w) if k < layers - 1 else 0.0
        down = fz_ref[k - 1, pl.ds(cut_op, rows), :] * (w - field(k - 1)) if k > 0 else 0.0
        result = result - (up - down)
        return result + re_ref[k, pl.ds(cut_op, rows), :] * w

    if mode == "residual":
        for k in range(layers):
            out_ref[0, k] = cell(b_ref, k, cut_b) - applied(k)
        return
    keep = mask_ref[...] > 0.5
    previous = None
    for k in range(layers):
        residual = cell(b_ref, k, cut_b)
        if mode == "sweep":
            residual = residual - applied(k)
        if k == 0:
            forward = residual * cell(inv_ref, 0, cut_op)
        else:
            forward = (residual + fz_ref[k - 1, pl.ds(cut_op, rows), :] * previous) * cell(inv_ref, k, cut_op)
        out_ref[0, k] = forward
        previous = forward
    back = previous
    for k in range(layers - 1, -1, -1):
        if k < layers - 1:
            back = out_ref[0, k] + rat_ref[0, k, pl.ds(cut_op, rows), :] * back
        if mode == "sweep":
            value = field(k) + relax_weight * back
        else:
            value = relax_weight * back
        out_ref[0, k] = jnp.where(keep, value, 0.0)


def kernel_sweep(field_rim, target, lanes, cut_b, cut_op, mask, mode="sweep", cut_w=0, rows=None, then=(),
                 masks=()):
    parts, layers, rows_rim, cols = field_rim.shape
    rows = rows_rim - 2 if rows is None else rows
    fxl, fxr, fyl, fyr, fz, re, inv, rat, scale = lanes
    per_part = lambda a: pl.BlockSpec((1,) + a.shape[1:], lambda c: (c,) + (0,) * (a.ndim - 1))
    whole = lambda a: pl.BlockSpec(a.shape, lambda c: (0,) * a.ndim)
    operands = [field_rim, target, fxl, fxr, fyl, fyr, fz, re, inv, rat, mask]
    specs = [per_part(field_rim), per_part(target), whole(fxl), whole(fxr), whole(fyl), whole(fyr),
             whole(fz), whole(re), per_part(inv), per_part(rat), whole(mask)]
    masks = list(masks) + [mask] * (len(then) - len(masks))
    operands += masks
    specs += [whole(m) for m in masks]
    body = functools.partial(
        sweep_kernel, rows=rows, cut_w=cut_w, cut_b=cut_b, cut_op=cut_op, mode=mode, scale=scale, then=then
    )
    out_specs = [pl.BlockSpec((1, layers, rows, cols), lambda c: (c, 0, 0, 0))]
    out_shape = [jax.ShapeDtypeStruct((parts, layers, rows, cols), jnp.float32)]
    for step in then:
        out_specs.append(pl.BlockSpec((1, layers, step[1], cols), lambda c: (c, 0, 0, 0)))
        out_shape.append(jax.ShapeDtypeStruct((parts, layers, step[1], cols), jnp.float32))
    outs = pl.pallas_call(body, grid=(parts,), in_specs=specs, out_specs=out_specs, out_shape=out_shape)(*operands)
    return tuple(outs) if then else outs[0]


def build_kernel(eta_ref, re_ref, fxl_ref, fxr_ref, fyl_ref, fyr_ref, fz_ref, reo_ref, inv_ref, rat_ref,
                 *, rows, cut_re, scale):
    component = pl.program_id(0)
    layers = eta_ref.shape[0]
    cols = eta_ref.shape[2]
    lane = lax.broadcasted_iota(jnp.int32, (rows, cols), 1)
    probe = pltpu.roll(lane, 1, 1)
    forward_roll = probe == jnp.where(lane == 0, cols - 1, lane - 1)
    first_col = lane == 0
    last_col = lane == cols - 1
    weight_x = jnp.where(component == 0, 4.0, 1.0) * scale
    weight_y = jnp.where(component == 0, 1.0, 4.0) * scale

    def inner(k):
        return eta_ref[k, pl.ds(1, rows), :]

    faces_z = [vertical_scale * 0.5 * (inner(k + 1) + inner(k)) for k in range(layers - 1)]
    ratio = None
    for k in range(layers):
        middle = inner(k)
        west = eta_ref[k, pl.ds(0, rows), :]
        east = eta_ref[k, pl.ds(2, rows), :]
        ahead = pltpu.roll(middle, 1, 1)
        behind = pltpu.roll(middle, cols - 1, 1)
        south = jnp.where(first_col, 0.0, jnp.where(forward_roll, ahead, behind))
        north = jnp.where(last_col, 0.0, jnp.where(forward_roll, behind, ahead))
        base_w = 0.5 * (middle + west)
        base_e = 0.5 * (east + middle)
        base_s = 0.5 * (middle + south)
        base_n = 0.5 * (north + middle)
        face_w = weight_x * base_w
        face_e = weight_x * base_e
        face_s = weight_y * base_s
        face_n = weight_y * base_n
        react = re_ref[min(k, re_ref.shape[0] - 1), pl.ds(cut_re, rows), :]
        up = faces_z[k] if k < layers - 1 else 0.0
        down = faces_z[k - 1] if k > 0 else 0.0
        diagonal = face_e + face_w + face_n + face_s
        diagonal = diagonal + (up + down + react)
        if k > 0:
            diagonal = diagonal - faces_z[k - 1] * ratio
        inverse = 1.0 / diagonal
        fxl_ref[k] = base_w
        fxr_ref[k] = base_e
        fyl_ref[k] = base_s
        fyr_ref[k] = base_n
        reo_ref[k] = react
        inv_ref[0, k] = inverse
        if k < layers - 1:
            ratio = faces_z[k] * inverse
            fz_ref[k] = faces_z[k]
            rat_ref[0, k] = ratio


def kernel_operator(eta_level, react_level, level_index, cut_re=0):
    layers, rows_eta, cols = eta_level.shape
    rows = rows_eta - 2
    whole = lambda a: pl.BlockSpec(a.shape, lambda c: (0,) * a.ndim)
    per_part = lambda shape: pl.BlockSpec((1,) + shape, lambda c: (c,) + (0,) * len(shape))
    cell = (layers, rows, cols)
    faces = (layers - 1, rows, cols)
    body = functools.partial(build_kernel, rows=rows, cut_re=cut_re, scale=horizontal_scale / 4.0**level_index)
    shapes = [cell] * 4 + [faces, cell, (2,) + cell, (2,) + faces]
    specs = [pl.BlockSpec(cell, lambda c: (0, 0, 0))] * 4 + [
        pl.BlockSpec(faces, lambda c: (0, 0, 0)),
        pl.BlockSpec(cell, lambda c: (0, 0, 0)),
        per_part(cell),
        per_part(faces),
    ]
    return tuple(
        pl.pallas_call(
            body,
            grid=(2,),
            in_specs=[whole(eta_level), whole(react_level)],
            out_specs=specs,
            out_shape=[jax.ShapeDtypeStruct(s, jnp.float32) for s in shapes],
        )(eta_level, react_level)
    ) + (horizontal_scale / 4.0**level_index,)


def kernel_coarse(target, lanes, mask, turns):
    parts, layers, rows, cols = target.shape
    fxl, fxr, fyl, fyr, fz, re, inv, rat, scale = lanes
    per_part = lambda a: pl.BlockSpec((1,) + a.shape[1:], lambda c: (c,) + (0,) * (a.ndim - 1))
    whole = lambda a: pl.BlockSpec(a.shape, lambda c: (0,) * a.ndim)
    operands = [target, fxl, fxr, fyl, fyr, fz, re, inv, rat, mask]
    specs = [per_part(target), whole(fxl), whole(fxr), whole(fyl), whole(fyr),
             whole(fz), whole(re), per_part(inv), per_part(rat), whole(mask)]
    body = functools.partial(coarse_kernel, rows=rows, turns=turns, scale=scale)
    return pl.pallas_call(
        body,
        grid=(parts,),
        in_specs=specs,
        out_specs=pl.BlockSpec((1, layers, rows, cols), lambda c: (c, 0, 0, 0)),
        out_shape=jax.ShapeDtypeStruct((parts, layers, rows, cols), jnp.float32),
        scratch_shapes=[pltpu.VMEM((1, layers, rows + 16, cols), jnp.float32)],
    )(*operands)


def rows_inside(cells, halo, extent, cols):
    return jnp.broadcast_to(inside(cells, halo, extent)[0, 0], (extent, cols)).astype(jnp.float32)


def shrink(operator, cut):
    if cut == 0:
        return operator
    face_x, face_y, face_z, react_level, inverses, ratios = operator
    rows = face_y.shape[2]
    return (
        face_x[:, :, cut : rows + 1 - cut],
        face_y[:, :, cut : rows - cut],
        face_z[:, cut : rows - cut],
        react_level[:, cut : rows - cut],
        inverses[:, :, cut : rows - cut],
        ratios[:, :, cut : rows - cut],
    )


def apply_operator(field_rim, operator):
    face_x, face_y, face_z, react_level, inverses, ratios = operator
    field = field_rim[:, :, 1:-1, :]
    flux_x = face_x * (field_rim[:, :, 1:, :] - field_rim[:, :, :-1, :])
    result = -(flux_x[:, :, 1:] - flux_x[:, :, :-1])
    padded = jnp.pad(field, ((0, 0), (0, 0), (0, 0), (1, 1)))
    flux_y = face_y * (padded[..., 1:] - padded[..., :-1])
    result = result - (flux_y[..., 1:] - flux_y[..., :-1])
    flux_z = face_z[None] * (field[:, 1:] - field[:, :-1])
    flux_z = jnp.pad(flux_z, ((0, 0), (1, 1), (0, 0), (0, 0)))
    result = result - (flux_z[:, 1:] - flux_z[:, :-1])
    return result + react_level[None] * field


def line_solve(residual, operator):
    face_z, inverses, ratios = (operator[2], operator[4], operator[5])
    layers = residual.shape[1]
    forward = [residual[:, 0] * inverses[:, 0]]
    for layer in range(1, layers):
        forward.append((residual[:, layer] + face_z[layer - 1] * forward[-1]) * inverses[:, layer])
    backward = [forward[-1]]
    for layer in range(layers - 2, -1, -1):
        backward.append(forward[layer] + ratios[:, layer] * backward[-1])
    return jnp.stack(backward[::-1], 1)


def sweep(field_rim, target, operator):
    field = field_rim[:, :, 1:-1, :]
    return field + relax_weight * line_solve(target - apply_operator(field_rim, operator), operator)


def restrict(field):
    return block_mean(field, 2)


def prolong(field):
    cols = field.shape[3]
    spread = (jnp.arange(cols)[:, None] == jnp.arange(2 * cols)[None, :] // 2).astype(jnp.float32)
    wide = jnp.einsum("ckxy,yz->ckxz", field, spread, precision=lax.Precision.HIGHEST)
    return jnp.repeat(wide, 2, axis=2)


def pad_rim(field):
    return jnp.pad(field, ((0, 0), (0, 0), (1, 1), (0, 0)))


def inside(cells, halo, extent):
    count = lax.axis_size("gx")
    first = lax.axis_index("gx") * cells - halo
    index = first + jnp.arange(extent)
    return ((index >= 0) & (index < count * cells)).reshape(1, 1, extent, 1)


def keep_inside(field, cells, halo):
    return jnp.where(inside(cells, halo, field.shape[2]), field, 0.0)


def window(full, dim, start, size, pad):
    widths = [(0, 0)] * full.ndim
    widths[dim] = (pad, pad)
    return lax.dynamic_slice_in_dim(jnp.pad(full, widths), start, size, axis=dim)


def nearby(cells, dim, hops):
    count = lax.axis_size("gx")
    lows = []
    highs = []
    for step in range(1, hops + 1):
        lows.insert(0, lax.ppermute(cells, "gx", [(i, i + step) for i in range(count - step)]))
        highs.append(lax.ppermute(cells, "gx", [(i + step, i) for i in range(count - step)]))
    return jnp.concatenate(lows + [cells] + highs, axis=dim)


def shards(misfit, adjoint_guess, viscosity, friction, ice_mask, forward_bed):
    layers, cells, cols = viscosity.shape
    where = lax.axis_index("gx")
    react_fine = reaction_field(friction, ice_mask, layers)
    react_pair = react_fine[:2]

    eta_1 = block_mean(viscosity, 2)
    react_1 = block_mean(react_pair, 2)
    pieces = [eta_1, react_1]
    packed = jnp.concatenate([p.reshape(-1) for p in pieces])
    gathered = lax.all_gather(packed[None], "gx", axis=0, tiled=True)
    count = gathered.shape[0]
    unpacked = []
    offset = 0
    for p in pieces:
        block = gathered[:, offset : offset + p.size].reshape((count,) + p.shape)
        offset += p.size
        unpacked.append(jnp.moveaxis(block, 0, 1).reshape((p.shape[0], count * p.shape[1], p.shape[2])))
    eta_1_all, react_1_all = unpacked
    eta_2_all = block_mean(eta_1_all, 2)
    react_2_all = block_mean(react_1_all, 2)

    halo = 4
    eta_wide, guess_wide, misfit_wide, react_wide = trade(
        [(viscosity, 1), (adjoint_guess, 2), (misfit, 2), (react_pair, 1)], halo
    )
    op_0 = kernel_operator(eta_wide, react_wide, 0, 1)
    _, fine, residual = kernel_sweep(
        guess_wide, misfit_wide, op_0, 1, 0, rows_inside(cells, 3, cells + 6, cols),
        then=((0, cells + 4, 2, 1, "sweep"), (1, cells, 4, 3, "residual")),
        masks=(rows_inside(cells, 2, cells + 4, cols),),
    )
    middle_rhs = restrict(residual)

    half = cells // 2
    wide = cols // 2
    rhs_wide = with_halo(middle_rhs, (("gx", 2),), half)
    eta_1_wide = window(eta_1_all, 1, where * half, 3 * half + 2, half + 1)
    react_1_wide = window(react_1_all, 1, where * half, 3 * half, half)
    op_1 = kernel_operator(eta_1_wide, react_1_wide, 1)
    _, middle, residual = kernel_sweep(
        rhs_wide, rhs_wide, op_1, 0, 0, rows_inside(half, half, 3 * half, wide), "zero", 0, 3 * half,
        then=((0, 3 * half - 2, 1, 1, "sweep"), (half - 2, half, half, half, "residual")),
        masks=(rows_inside(half, half - 1, 3 * half - 2, wide),),
    )
    coarse_rhs = restrict(residual)

    quarter = cells // 4
    narrow = cols // 4
    reach = 3
    span = reach + COARSE_SWEEPS - 1
    coarse_rhs_near = nearby(coarse_rhs, 2, span // quarter)
    eta_2_near = window(eta_2_all, 1, where * quarter, quarter + 2 * span + 2, span + 1)
    react_2_near = window(react_2_all, 1, where * quarter, quarter + 2 * span, span)
    op_2 = kernel_operator(eta_2_near, react_2_near, 2)
    extent = quarter + 2 * span
    coarse_mask = rows_inside(quarter, span, extent, narrow)
    coarse = kernel_coarse(coarse_rhs_near, op_2, coarse_mask, COARSE_SWEEPS)
    coarse_near = coarse[:, :, span - reach : span + quarter + reach]

    lift = prolong(coarse_near)
    trim = 2 * reach - (half - 1)
    middle = middle + lift[:, :, trim : lift.shape[2] - trim]
    middle = kernel_sweep(
        middle, rhs_wide, op_1, 2, 2, rows_inside(half, half - 2, 3 * half - 4, wide),
        then=((0, 3 * half - 6, 3, 3, "sweep"),), masks=(rows_inside(half, half - 3, 3 * half - 6, wide),),
    )[1]
    fine = fine + prolong(middle)
    fine = kernel_sweep(
        fine, misfit_wide, op_0, 3, 2, rows_inside(cells, 1, cells + 2, cols),
        then=((0, cells, 4, 3, "sweep"),), masks=(rows_inside(cells, 0, cells, cols),),
    )[1]
    grounded = (ice_mask == 2).astype(jnp.float32)
    gradient = -grounded * (forward_bed[0] * fine[0, 0] + forward_bed[1] * fine[1, 0])
    return (fine, gradient)


def solution(mesh):
    placed = (
        P("ens", None, "gx", None),
        P("ens", None, "gx", None),
        P("ens", "gx", None),
        P("gx", "ens"),
        P("gx", "ens"),
        P("ens", "gx", None),
    )
    return jax.shard_map(
        shards,
        mesh=mesh,
        in_specs=placed,
        out_specs=(P("ens", None, "gx", None), P("gx", "ens")),
        check_vma=False,
    )
```

```python
import functools

import jax
import jax.numpy as jnp
from jax import lax
from jax.experimental import pallas as pl
from jax.experimental.pallas import tpu as pltpu
from jax.sharding import PartitionSpec as P

NU = 2
COARSE_SWEEPS = 6


horizontal_scale = 1.0
vertical_scale = 4.0
relax_weight = 0.8


def with_halo(cells, sides, width):
    for axis, dim in sides:
        count = lax.axis_size(axis)
        ends = count - 1
        head = lax.slice_in_dim(cells, 0, width, axis=dim)
        tail = lax.slice_in_dim(cells, cells.shape[dim] - width, cells.shape[dim], axis=dim)
        cells = jnp.concatenate(
            [
                lax.ppermute(tail, axis, [(i, (i + 1) % count) for i in range(ends)]),
                cells,
                lax.ppermute(head, axis, [((i + 1) % count, i) for i in range(ends)]),
            ],
            axis=dim,
        )
    return cells


def trade(parts, width):
    count = lax.axis_size("gx")
    ends = count - 1
    heads = [lax.slice_in_dim(a, 0, width, axis=dim) for a, dim in parts]
    tails = [lax.slice_in_dim(a, a.shape[dim] - width, a.shape[dim], axis=dim) for a, dim in parts]
    pack = lambda pieces: jnp.concatenate([p.reshape(-1) for p in pieces])
    from_left = lax.ppermute(pack(tails), "gx", [(i, i + 1) for i in range(ends)])
    from_right = lax.ppermute(pack(heads), "gx", [(i + 1, i) for i in range(ends)])
    out = []
    offset = 0
    for (a, dim), h in zip(parts, heads):
        size = h.size
        left = from_left[offset : offset + size].reshape(h.shape)
        right = from_right[offset : offset + size].reshape(h.shape)
        offset += size
        out.append(jnp.concatenate([left, a, right], axis=dim))
    return out


def block_mean(field, factor):
    while factor > 1:
        lead = field.shape[:-2]
        rows, cols = (field.shape[-2], field.shape[-1])
        pairs = (jnp.arange(cols)[:, None] // 2 == jnp.arange(cols // 2)[None, :]).astype(jnp.float32)
        field = jnp.einsum("...y,yz->...z", field, pairs, precision=lax.Precision.HIGHEST)
        field = 0.25 * field.reshape(lead + (rows // 2, 2, cols // 2)).sum(axis=-2)
        factor //= 2
    return field


def reaction_field(friction, ice_mask, layers):
    open_water = (ice_mask == 0).astype(jnp.float32)
    grounded = (ice_mask == 2).astype(jnp.float32)
    bottom = (jnp.arange(layers) == 0).astype(jnp.float32).reshape(layers, 1, 1)
    return 0.02 + 2.0 * open_water[None] + bottom * (grounded * friction)[None]


def build_operator(eta_level, react_level, level_index):
    scale = horizontal_scale / 4.0**level_index
    weight_x = jnp.array([4.0, 1.0], jnp.float32).reshape(2, 1, 1, 1) * scale
    weight_y = jnp.array([1.0, 4.0], jnp.float32).reshape(2, 1, 1, 1) * scale
    inner = eta_level[:, 1:-1, :]
    face_x = weight_x * (0.5 * (eta_level[:, 1:, :] + eta_level[:, :-1, :]))[None]
    padded = jnp.pad(inner, ((0, 0), (0, 0), (1, 1)))
    face_y = weight_y * (0.5 * (padded[:, :, 1:] + padded[:, :, :-1]))[None]
    face_z = vertical_scale * 0.5 * (inner[1:] + inner[:-1])
    vertical = jnp.pad(face_z, ((1, 1), (0, 0), (0, 0)))
    diagonal = face_x[:, :, 1:] + face_x[:, :, :-1] + face_y[..., 1:] + face_y[..., :-1]
    diagonal = diagonal + (vertical[1:] + vertical[:-1] + react_level)[None]
    layers = diagonal.shape[1]
    inverses = []
    ratios = []
    for layer in range(layers):
        pivot = diagonal[:, layer]
        if layer > 0:
            pivot = pivot - face_z[layer - 1] * ratios[-1]
        inverse = 1.0 / pivot
        inverses.append(inverse)
        if layer < layers - 1:
            ratios.append(face_z[layer] * inverse)
    return (face_x, face_y, face_z, react_level, jnp.stack(inverses, 1), jnp.stack(ratios, 1))


def lane_ops(operator):
    face_x, face_y, face_z, react_level, inverses, ratios = operator
    return (face_x[:, :, :-1], face_x[:, :, 1:], face_y[..., :-1], face_y[..., 1:], face_z, react_level, inverses, ratios)


def sweep_kernel(w_ref, b_ref, fxl_ref, fxr_ref, fyl_ref, fyr_ref, fz_ref, re_ref, inv_ref, rat_ref, mask_ref, *more,
                 rows, cut_w, cut_b, cut_op, mode, scale, then, lifted):
    lanes = (fxl_ref, fxr_ref, fyl_ref, fyr_ref, fz_ref, re_ref, inv_ref, rat_ref, scale)
    add_ref = more[0] if lifted else None
    more = more[1:] if lifted else more
    steps = len(then)
    masks, outs = more[:steps], more[steps:]
    relax(w_ref, b_ref, lanes, mask_ref, outs[0], rows=rows, cut_w=cut_w, cut_b=cut_b, cut_op=cut_op, mode=mode,
          add_ref=add_ref)
    for step, (next_cut_w, next_rows, next_cut_b, next_cut_op, next_mode) in enumerate(then):
        relax(outs[step], b_ref, lanes, masks[step], outs[step + 1], rows=next_rows, cut_w=next_cut_w,
              cut_b=next_cut_b, cut_op=next_cut_op, mode=next_mode)


def coarse_kernel(b_ref, fxl_ref, fxr_ref, fyl_ref, fyr_ref, fz_ref, re_ref, inv_ref, rat_ref, mask_ref, out_ref, w_ref,
                  *, rows, turns, scale):
    lanes = (fxl_ref, fxr_ref, fyl_ref, fyr_ref, fz_ref, re_ref, inv_ref, rat_ref, scale)
    w_ref[...] = jnp.zeros(w_ref.shape, jnp.float32)
    for turn in range(turns):
        relax(w_ref, b_ref, lanes, mask_ref, out_ref, rows=rows, cut_w=7, cut_b=0, cut_op=0, mode="sweep")
        if turn < turns - 1:
            for k in range(out_ref.shape[1]):
                w_ref[0, k, pl.ds(8, rows), :] = out_ref[0, k]


def relax(w_ref, b_ref, lanes, mask_ref, out_ref, *, rows, cut_w, cut_b, cut_op, mode, add_ref=None):
    fxl_ref, fxr_ref, fyl_ref, fyr_ref, fz_ref, re_ref, inv_ref, rat_ref, scale = lanes
    layers = out_ref.shape[1]
    cols = out_ref.shape[3]
    lane = lax.broadcasted_iota(jnp.int32, (rows, cols), 1)
    probe = pltpu.roll(lane, 1, 1)
    forward_roll = probe == jnp.where(lane == 0, cols - 1, lane - 1)
    first_col = lane == 0
    last_col = lane == cols - 1

    def cell(ref, k, cut):
        return ref[0, k, pl.ds(cut, rows), :]

    component = pl.program_id(0)
    weight_x = jnp.where(component == 0, 4.0, 1.0) * scale
    weight_y = jnp.where(component == 0, 1.0, 4.0) * scale

    def face(ref, weight, k):
        return weight * ref[k, pl.ds(cut_op, rows), :]

    def rim(k, start):
        value = w_ref[0, k, pl.ds(start, rows), :]
        return value if add_ref is None else value + add_ref[0, k, pl.ds(start, rows), :]

    def field(k):
        return rim(k, cut_w + 1)

    def applied(k):
        w = field(k)
        west = rim(k, cut_w)
        east = rim(k, cut_w + 2)
        result = -(face(fxr_ref, weight_x, k) * (east - w) - face(fxl_ref, weight_x, k) * (w - west))
        ahead = pltpu.roll(w, 1, 1)
        behind = pltpu.roll(w, cols - 1, 1)
        south = jnp.where(forward_roll, ahead, behind)
        north = jnp.where(forward_roll, behind, ahead)
        south = jnp.where(first_col, 0.0, south)
        north = jnp.where(last_col, 0.0, north)
        result = result - (face(fyr_ref, weight_y, k) * (north - w) - face(fyl_ref, weight_y, k) * (w - south))
        up = fz_ref[k, pl.ds(cut_op, rows), :] * (field(k + 1) - w) if k < layers - 1 else 0.0
        down = fz_ref[k - 1, pl.ds(cut_op, rows), :] * (w - field(k - 1)) if k > 0 else 0.0
        result = result - (up - down)
        return result + re_ref[k, pl.ds(cut_op, rows), :] * w

    if mode == "residual":
        for k in range(layers):
            out_ref[0, k] = cell(b_ref, k, cut_b) - applied(k)
        return
    keep = mask_ref[...] > 0.5
    previous = None
    for k in range(layers):
        residual = cell(b_ref, k, cut_b)
        if mode == "sweep":
            residual = residual - applied(k)
        if k == 0:
            forward = residual * cell(inv_ref, 0, cut_op)
        else:
            forward = (residual + fz_ref[k - 1, pl.ds(cut_op, rows), :] * previous) * cell(inv_ref, k, cut_op)
        out_ref[0, k] = forward
        previous = forward
    back = previous
    for k in range(layers - 1, -1, -1):
        if k < layers - 1:
            back = out_ref[0, k] + rat_ref[0, k, pl.ds(cut_op, rows), :] * back
        if mode == "sweep":
            value = field(k) + relax_weight * back
        else:
            value = relax_weight * back
        out_ref[0, k] = jnp.where(keep, value, 0.0)


def kernel_sweep(field_rim, target, lanes, cut_b, cut_op, mask, mode="sweep", cut_w=0, rows=None, then=(),
                 masks=(), lift=None):
    parts, layers, rows_rim, cols = field_rim.shape
    rows = rows_rim - 2 if rows is None else rows
    fxl, fxr, fyl, fyr, fz, re, inv, rat, scale = lanes
    per_part = lambda a: pl.BlockSpec((1,) + a.shape[1:], lambda c: (c,) + (0,) * (a.ndim - 1))
    whole = lambda a: pl.BlockSpec(a.shape, lambda c: (0,) * a.ndim)
    operands = [field_rim, target, fxl, fxr, fyl, fyr, fz, re, inv, rat, mask]
    specs = [per_part(field_rim), per_part(target), whole(fxl), whole(fxr), whole(fyl), whole(fyr),
             whole(fz), whole(re), per_part(inv), per_part(rat), whole(mask)]
    if lift is not None:
        operands.append(lift)
        specs.append(per_part(lift))
    masks = list(masks) + [mask] * (len(then) - len(masks))
    operands += masks
    specs += [whole(m) for m in masks]
    body = functools.partial(
        sweep_kernel, rows=rows, cut_w=cut_w, cut_b=cut_b, cut_op=cut_op, mode=mode, scale=scale, then=then,
        lifted=lift is not None,
    )
    out_specs = [pl.BlockSpec((1, layers, rows, cols), lambda c: (c, 0, 0, 0))]
    out_shape = [jax.ShapeDtypeStruct((parts, layers, rows, cols), jnp.float32)]
    for step in then:
        out_specs.append(pl.BlockSpec((1, layers, step[1], cols), lambda c: (c, 0, 0, 0)))
        out_shape.append(jax.ShapeDtypeStruct((parts, layers, step[1], cols), jnp.float32))
    outs = pl.pallas_call(body, grid=(parts,), in_specs=specs, out_specs=out_specs, out_shape=out_shape)(*operands)
    return tuple(outs) if then else outs[0]


def build_kernel(eta_ref, re_ref, fxl_ref, fxr_ref, fyl_ref, fyr_ref, fz_ref, reo_ref, inv_ref, rat_ref,
                 *, rows, cut_re, scale):
    component = pl.program_id(0)
    layers = eta_ref.shape[0]
    cols = eta_ref.shape[2]
    lane = lax.broadcasted_iota(jnp.int32, (rows, cols), 1)
    probe = pltpu.roll(lane, 1, 1)
    forward_roll = probe == jnp.where(lane == 0, cols - 1, lane - 1)
    first_col = lane == 0
    last_col = lane == cols - 1
    weight_x = jnp.where(component == 0, 4.0, 1.0) * scale
    weight_y = jnp.where(component == 0, 1.0, 4.0) * scale

    def inner(k):
        return eta_ref[k, pl.ds(1, rows), :]

    faces_z = [vertical_scale * 0.5 * (inner(k + 1) + inner(k)) for k in range(layers - 1)]
    ratio = None
    for k in range(layers):
        middle = inner(k)
        west = eta_ref[k, pl.ds(0, rows), :]
        east = eta_ref[k, pl.ds(2, rows), :]
        ahead = pltpu.roll(middle, 1, 1)
        behind = pltpu.roll(middle, cols - 1, 1)
        south = jnp.where(first_col, 0.0, jnp.where(forward_roll, ahead, behind))
        north = jnp.where(last_col, 0.0, jnp.where(forward_roll, behind, ahead))
        base_w = 0.5 * (middle + west)
        base_e = 0.5 * (east + middle)
        base_s = 0.5 * (middle + south)
        base_n = 0.5 * (north + middle)
        face_w = weight_x * base_w
        face_e = weight_x * base_e
        face_s = weight_y * base_s
        face_n = weight_y * base_n
        react = re_ref[min(k, re_ref.shape[0] - 1), pl.ds(cut_re, rows), :]
        up = faces_z[k] if k < layers - 1 else 0.0
        down = faces_z[k - 1] if k > 0 else 0.0
        diagonal = face_e + face_w + face_n + face_s
        diagonal = diagonal + (up + down + react)
        if k > 0:
            diagonal = diagonal - faces_z[k - 1] * ratio
        inverse = 1.0 / diagonal
        fxl_ref[k] = base_w
        fxr_ref[k] = base_e
        fyl_ref[k] = base_s
        fyr_ref[k] = base_n
        reo_ref[k] = react
        inv_ref[0, k] = inverse
        if k < layers - 1:
            ratio = faces_z[k] * inverse
            fz_ref[k] = faces_z[k]
            rat_ref[0, k] = ratio


def kernel_operator(eta_level, react_level, level_index, cut_re=0):
    layers, rows_eta, cols = eta_level.shape
    rows = rows_eta - 2
    whole = lambda a: pl.BlockSpec(a.shape, lambda c: (0,) * a.ndim)
    per_part = lambda shape: pl.BlockSpec((1,) + shape, lambda c: (c,) + (0,) * len(shape))
    cell = (layers, rows, cols)
    faces = (layers - 1, rows, cols)
    body = functools.partial(build_kernel, rows=rows, cut_re=cut_re, scale=horizontal_scale / 4.0**level_index)
    shapes = [cell] * 4 + [faces, cell, (2,) + cell, (2,) + faces]
    specs = [pl.BlockSpec(cell, lambda c: (0, 0, 0))] * 4 + [
        pl.BlockSpec(faces, lambda c: (0, 0, 0)),
        pl.BlockSpec(cell, lambda c: (0, 0, 0)),
        per_part(cell),
        per_part(faces),
    ]
    return tuple(
        pl.pallas_call(
            body,
            grid=(2,),
            in_specs=[whole(eta_level), whole(react_level)],
            out_specs=specs,
            out_shape=[jax.ShapeDtypeStruct(s, jnp.float32) for s in shapes],
        )(eta_level, react_level)
    ) + (horizontal_scale / 4.0**level_index,)


def kernel_coarse(target, lanes, mask, turns):
    parts, layers, rows, cols = target.shape
    fxl, fxr, fyl, fyr, fz, re, inv, rat, scale = lanes
    per_part = lambda a: pl.BlockSpec((1,) + a.shape[1:], lambda c: (c,) + (0,) * (a.ndim - 1))
    whole = lambda a: pl.BlockSpec(a.shape, lambda c: (0,) * a.ndim)
    operands = [target, fxl, fxr, fyl, fyr, fz, re, inv, rat, mask]
    specs = [per_part(target), whole(fxl), whole(fxr), whole(fyl), whole(fyr),
             whole(fz), whole(re), per_part(inv), per_part(rat), whole(mask)]
    body = functools.partial(coarse_kernel, rows=rows, turns=turns, scale=scale)
    return pl.pallas_call(
        body,
        grid=(parts,),
        in_specs=specs,
        out_specs=pl.BlockSpec((1, layers, rows, cols), lambda c: (c, 0, 0, 0)),
        out_shape=jax.ShapeDtypeStruct((parts, layers, rows, cols), jnp.float32),
        scratch_shapes=[pltpu.VMEM((1, layers, rows + 16, cols), jnp.float32)],
    )(*operands)


def rows_inside(cells, halo, extent, cols):
    return jnp.broadcast_to(inside(cells, halo, extent)[0, 0], (extent, cols)).astype(jnp.float32)


def shrink(operator, cut):
    if cut == 0:
        return operator
    face_x, face_y, face_z, react_level, inverses, ratios = operator
    rows = face_y.shape[2]
    return (
        face_x[:, :, cut : rows + 1 - cut],
        face_y[:, :, cut : rows - cut],
        face_z[:, cut : rows - cut],
        react_level[:, cut : rows - cut],
        inverses[:, :, cut : rows - cut],
        ratios[:, :, cut : rows - cut],
    )


def apply_operator(field_rim, operator):
    face_x, face_y, face_z, react_level, inverses, ratios = operator
    field = field_rim[:, :, 1:-1, :]
    flux_x = face_x * (field_rim[:, :, 1:, :] - field_rim[:, :, :-1, :])
    result = -(flux_x[:, :, 1:] - flux_x[:, :, :-1])
    padded = jnp.pad(field, ((0, 0), (0, 0), (0, 0), (1, 1)))
    flux_y = face_y * (padded[..., 1:] - padded[..., :-1])
    result = result - (flux_y[..., 1:] - flux_y[..., :-1])
    flux_z = face_z[None] * (field[:, 1:] - field[:, :-1])
    flux_z = jnp.pad(flux_z, ((0, 0), (1, 1), (0, 0), (0, 0)))
    result = result - (flux_z[:, 1:] - flux_z[:, :-1])
    return result + react_level[None] * field


def line_solve(residual, operator):
    face_z, inverses, ratios = (operator[2], operator[4], operator[5])
    layers = residual.shape[1]
    forward = [residual[:, 0] * inverses[:, 0]]
    for layer in range(1, layers):
        forward.append((residual[:, layer] + face_z[layer - 1] * forward[-1]) * inverses[:, layer])
    backward = [forward[-1]]
    for layer in range(layers - 2, -1, -1):
        backward.append(forward[layer] + ratios[:, layer] * backward[-1])
    return jnp.stack(backward[::-1], 1)


def sweep(field_rim, target, operator):
    field = field_rim[:, :, 1:-1, :]
    return field + relax_weight * line_solve(target - apply_operator(field_rim, operator), operator)


def restrict(field):
    return block_mean(field, 2)


def prolong(field):
    cols = field.shape[3]
    spread = (jnp.arange(cols)[:, None] == jnp.arange(2 * cols)[None, :] // 2).astype(jnp.float32)
    wide = jnp.einsum("ckxy,yz->ckxz", field, spread, precision=lax.Precision.HIGHEST)
    return jnp.repeat(wide, 2, axis=2)


def pad_rim(field):
    return jnp.pad(field, ((0, 0), (0, 0), (1, 1), (0, 0)))


def inside(cells, halo, extent):
    count = lax.axis_size("gx")
    first = lax.axis_index("gx") * cells - halo
    index = first + jnp.arange(extent)
    return ((index >= 0) & (index < count * cells)).reshape(1, 1, extent, 1)


def keep_inside(field, cells, halo):
    return jnp.where(inside(cells, halo, field.shape[2]), field, 0.0)


def window(full, dim, start, size, pad):
    widths = [(0, 0)] * full.ndim
    widths[dim] = (pad, pad)
    return lax.dynamic_slice_in_dim(jnp.pad(full, widths), start, size, axis=dim)


def nearby(cells, dim, hops):
    count = lax.axis_size("gx")
    lows = []
    highs = []
    for step in range(1, hops + 1):
        lows.insert(0, lax.ppermute(cells, "gx", [(i, i + step) for i in range(count - step)]))
        highs.append(lax.ppermute(cells, "gx", [(i + step, i) for i in range(count - step)]))
    return jnp.concatenate(lows + [cells] + highs, axis=dim)


def shards(misfit, adjoint_guess, viscosity, friction, ice_mask, forward_bed):
    layers, cells, cols = viscosity.shape
    where = lax.axis_index("gx")
    react_fine = reaction_field(friction, ice_mask, layers)
    react_pair = react_fine[:2]

    eta_1 = block_mean(viscosity, 2)
    react_1 = block_mean(react_pair, 2)
    pieces = [eta_1, react_1]
    packed = jnp.concatenate([p.reshape(-1) for p in pieces])
    gathered = lax.all_gather(packed[None], "gx", axis=0, tiled=True)
    count = gathered.shape[0]
    unpacked = []
    offset = 0
    for p in pieces:
        block = gathered[:, offset : offset + p.size].reshape((count,) + p.shape)
        offset += p.size
        unpacked.append(jnp.moveaxis(block, 0, 1).reshape((p.shape[0], count * p.shape[1], p.shape[2])))
    eta_1_all, react_1_all = unpacked
    eta_2_all = block_mean(eta_1_all, 2)
    react_2_all = block_mean(react_1_all, 2)

    halo = 4
    eta_wide, guess_wide, misfit_wide, react_wide = trade(
        [(viscosity, 1), (adjoint_guess, 2), (misfit, 2), (react_pair, 1)], halo
    )
    op_0 = kernel_operator(eta_wide, react_wide, 0, 1)
    _, fine, residual = kernel_sweep(
        guess_wide, misfit_wide, op_0, 1, 0, rows_inside(cells, 3, cells + 6, cols),
        then=((0, cells + 4, 2, 1, "sweep"), (1, cells, 4, 3, "residual")),
        masks=(rows_inside(cells, 2, cells + 4, cols),),
    )
    middle_rhs = restrict(residual)

    half = cells // 2
    wide = cols // 2
    rhs_wide = with_halo(middle_rhs, (("gx", 2),), half)
    eta_1_wide = window(eta_1_all, 1, where * half, 3 * half + 2, half + 1)
    react_1_wide = window(react_1_all, 1, where * half, 3 * half, half)
    op_1 = kernel_operator(eta_1_wide, react_1_wide, 1)
    _, middle, residual = kernel_sweep(
        rhs_wide, rhs_wide, op_1, 0, 0, rows_inside(half, half, 3 * half, wide), "zero", 0, 3 * half,
        then=((0, 3 * half - 2, 1, 1, "sweep"), (half - 2, half, half, half, "residual")),
        masks=(rows_inside(half, half - 1, 3 * half - 2, wide),),
    )
    coarse_rhs = restrict(residual)

    quarter = cells // 4
    narrow = cols // 4
    reach = 3
    span = reach + COARSE_SWEEPS - 1
    coarse_rhs_near = nearby(coarse_rhs, 2, span // quarter)
    eta_2_near = window(eta_2_all, 1, where * quarter, quarter + 2 * span + 2, span + 1)
    react_2_near = window(react_2_all, 1, where * quarter, quarter + 2 * span, span)
    op_2 = kernel_operator(eta_2_near, react_2_near, 2)
    extent = quarter + 2 * span
    coarse_mask = rows_inside(quarter, span, extent, narrow)
    coarse = kernel_coarse(coarse_rhs_near, op_2, coarse_mask, COARSE_SWEEPS)
    coarse_near = coarse[:, :, span - reach : span + quarter + reach]

    lift = prolong(coarse_near)
    trim = 2 * reach - (half - 1)
    middle = middle + lift[:, :, trim : lift.shape[2] - trim]
    middle = kernel_sweep(
        middle, rhs_wide, op_1, 2, 2, rows_inside(half, half - 2, 3 * half - 4, wide),
        then=((0, 3 * half - 6, 3, 3, "sweep"),), masks=(rows_inside(half, half - 3, 3 * half - 6, wide),),
    )[1]
    fine = kernel_sweep(
        fine, misfit_wide, op_0, 3, 2, rows_inside(cells, 1, cells + 2, cols), lift=prolong(middle),
        then=((0, cells, 4, 3, "sweep"),), masks=(rows_inside(cells, 0, cells, cols),),
    )[1]
    grounded = (ice_mask == 2).astype(jnp.float32)
    gradient = -grounded * (forward_bed[0] * fine[0, 0] + forward_bed[1] * fine[1, 0])
    return (fine, gradient)


def solution(mesh):
    placed = (
        P("ens", None, "gx", None),
        P("ens", None, "gx", None),
        P("ens", "gx", None),
        P("gx", "ens"),
        P("gx", "ens"),
        P("ens", "gx", None),
    )
    return jax.shard_map(
        shards,
        mesh=mesh,
        in_specs=placed,
        out_specs=(P("ens", None, "gx", None), P("gx", "ens")),
        check_vma=False,
    )
```
